32 devices in a mesh: dp: 4 (over x, core), space: 8 (over z, y).
Axes of the slice: x: 2, y: 2, z: 4, core: 2. Of those that a mesh axis runs over, the one named last changes fastest.
Arguments:
- inputs: bfloat16 [8, 4, 48, 48, 128], P('space', 'dp'), may hold values from -6 to 6
- cotangent: bfloat16 [8, 4, 48, 48, 128], P('space', 'dp'), may hold values from -6 to 6
- weight_first: bfloat16 [3, 3, 128, 128], replicated, may hold values from -0.1875 to 0.1875
- weight_second: bfloat16 [3, 3, 128, 128], replicated, may hold values from -0.1875 to 0.1875
- slot_tile: int32 [8], replicated, may hold values from 0 to 7, as said below
- neighbour_tile: int32 [8, 8], replicated, may hold values from 0 to 7, as said below
- neighbour_turns: int32 [8, 8], replicated, may hold values from 0 to 3, as said below
- corner_live: int32 [8, 4], replicated, may hold values from 0 to 1, as said below
Outputs:
- grad_inputs: bfloat16 [8, 4, 48, 48, 128], P('space', 'dp')
- grad_first: float32 [3, 3, 128, 128], replicated
- grad_second: float32 [3, 3, 128, 128], replicated
The draws below stay inside these ranges and needn't reach their ends.
Inputs may be any that keep to these rules, and one draw needn't show every extreme that they name: `slot_tile`: a permutation of the 8 tiles; slot s is held by device s of space. A tile and each of its 8 neighbours sit at slots at most 7 apart counted around the cycle of 8 slots. `neighbour_tile`: the tables are consistent: if u is beside t in direction k with code r, then t is beside u in the opposite direction (top and bottom, left and right, top-left and bottom-right, top-right and bottom-left) with code (4 - r) % 4. No slot holds more than two of a tile's top, bottom, left and right neighbours. `neighbour_turns`: number of counterclockwise quarter turns that bring the neighbour's pixel frame into the tile's. `corner_live`: 0 where the corner pixel is missing; the tiles that meet at a vertex agree.
All inputs are finite; a program needn't handle non-finite values.
Results may differ from the reference program's by a relative error of at most 0.0049.
Values may be sent and summed in bfloat16 or wider, within the bound.
No kernel may reach another device: no remote copies, remote signals or barrier semaphores. Data moves between devices by JAX's collectives and lax.ppermute only.
A program may use at most 64 MiB of HBM per device.

```python
import math
import jax
import jax.numpy as jnp
import numpy as np
from jax import lax

C = 128
S = 48
BAND = 4
TILES = 8
BATCH = 4


def quarter_maps():
    single = [3, 2, 0, 1, 5, 7, 4, 6]
    table = [list(range(8))]
    for turn in range(3):
        table.append([single[k] for k in table[-1]])
    return np.array(table, dtype=np.int32)


def surface_tables(key):
    count = TILES
    rows_all = count // BAND
    index = jnp.arange(count, dtype=jnp.int32)
    row = index // BAND
    column = index % BAND
    orient = jax.random.randint(jax.random.fold_in(key, 11), (count,), 0, 4)
    missing = (jax.random.randint(jax.random.fold_in(key, 12), (count,), 0, 4) == 0).astype(jnp.int32)
    maps = jnp.asarray(quarter_maps())
    global_dir = maps[orient]
    step_row = jnp.array([-1, 1, 0, 0, -1, -1, 1, 1], jnp.int32)
    step_col = jnp.array([0, 0, -1, 1, -1, 1, -1, 1], jnp.int32)
    near_row = (row[:, None] + step_row[global_dir]) % rows_all
    near_col = (column[:, None] + step_col[global_dir]) % BAND
    neighbour = near_row * BAND + near_col
    turns = (orient[:, None] - orient[neighbour]) % 4
    corner_dir = global_dir[:, 4:] - 4
    vertex_row = jnp.array([0, 0, 1, 1], jnp.int32)
    vertex_col = jnp.array([0, 1, 0, 1], jnp.int32)
    vertex = (row[:, None] + vertex_row[corner_dir]) % rows_all * BAND + (column[:, None] + vertex_col[corner_dir]) % BAND
    live = 1 - missing[vertex]
    return (neighbour.astype(jnp.int32), turns.astype(jnp.int32), live.astype(jnp.int32))


def draw_slot_tile(key, part):
    swaps = jax.random.randint(jax.random.fold_in(key, 13), (TILES // 2,), 0, 2)
    swaps = swaps.at[0].set(1).at[3].set(1)
    base = jnp.arange(TILES // 2, dtype=jnp.int32) * 2
    order = jnp.stack([base + swaps, base + 1 - swaps], axis=1).reshape(TILES)
    offset = jax.random.randint(jax.random.fold_in(key, 14), (), 0, TILES)
    return ((order + offset) % TILES).astype(jnp.int32)


def draw_neighbour_tile(key, part):
    return surface_tables(key)[0]


def draw_neighbour_turns(key, part):
    return surface_tables(key)[1]


def draw_corner_live(key, part):
    return surface_tables(key)[2]


def levels(rng, shape, cuts, least, high):
    level, own = 1.0, jax.random.fold_in(rng, 6)
    for axis_at, shards_of in cuts:
        draws = jnp.exp(jax.random.uniform(jax.random.fold_in(own, axis_at), (shards_of,), jnp.float32, least / len(cuts), high / len(cuts)))
        level = level * jnp.repeat(draws, shape[axis_at] // shards_of).reshape([-1 if axis == axis_at else 1 for axis in range(len(shape))])
    return level


def scatter_about(own_key, shape, scale, limit, split=(), kind=jnp.bfloat16):
    gain = levels(own_key, shape, split, -0.22, 0.18) if split else 1.0
    values = jax.random.normal(own_key, shape, jnp.float32) * scale * gain
    return jnp.minimum(jnp.maximum(values, -limit), limit).astype(kind)


def setup_inputs(seed: int = 0) -> dict:
    streams_of = jax.random.split(jax.random.key(seed), 9)
    return {
        "inputs": scatter_about(streams_of[0], (TILES, BATCH, S, S, C), 1.0, 6.0, ((0, 8), (1, 4))),
        "cotangent": scatter_about(streams_of[1], (TILES, BATCH, S, S, C), 1.0, 6.0, ((0, 8), (1, 4))),
        "weight_first": scatter_about(streams_of[2], (3, 3, C, C), (9 * C) ** -0.5, 0.1875),
        "weight_second": scatter_about(streams_of[3], (3, 3, C, C), (9 * C) ** -0.5, 0.1875),
        "slot_tile": draw_slot_tile(jax.random.fold_in(streams_of[8], 71), 0),
        "neighbour_tile": draw_neighbour_tile(jax.random.fold_in(streams_of[8], 71), 0),
        "neighbour_turns": draw_neighbour_turns(jax.random.fold_in(streams_of[8], 71), 0),
        "corner_live": draw_corner_live(jax.random.fold_in(streams_of[8], 71), 0),
    }


def rotate_tile(tile, turns):
    options = jnp.stack([jnp.rot90(tile, k, axes=(1, 2)) for k in range(4)])
    return options[turns]

def assemble(own, top, bottom, left, right, top_left, top_right, bottom_left, bottom_right):
    top_row = jnp.concatenate([top_left[:, None], top, top_right[:, None]], axis=1)
    bottom_row = jnp.concatenate([bottom_left[:, None], bottom, bottom_right[:, None]], axis=1)
    middle = jnp.concatenate([left[:, :, None], own, right[:, :, None]], axis=2)
    return jnp.concatenate([top_row[:, None], middle, bottom_row[:, None]], axis=1)

def pad_field(field, slot_tile, neighbour_tile, neighbour_turns, corner_live):
    count = field.shape[0]
    slot_of_tile = jnp.zeros((count,), jnp.int32).at[slot_tile].set(jnp.arange(count, dtype=jnp.int32))

    def one_slot(slot):
        tile_id = slot_tile[slot]
        pieces = []
        for k in range(8):
            other = field[slot_of_tile[neighbour_tile[tile_id, k]]]
            pieces.append(rotate_tile(other, neighbour_turns[tile_id, k]))
        flags = corner_live[tile_id].astype(field.dtype)
        return assemble(field[slot], pieces[0][:, -1], pieces[1][:, 0], pieces[2][:, :, -1], pieces[3][:, :, 0], pieces[4][:, -1, -1] * flags[0], pieces[5][:, -1, 0] * flags[1], pieces[6][:, 0, -1] * flags[2], pieces[7][:, 0, 0] * flags[3])
    return lax.map(one_slot, jnp.arange(count, dtype=jnp.int32))

def conv_tile(padded, weight):
    total = jnp.zeros(padded.shape[:1] + (S, S, weight.shape[3]), jnp.float32)
    for di in range(3):
        for dj in range(3):
            window = padded[:, di:di + S, dj:dj + S].astype(jnp.float32)
            total = total + jnp.einsum('bijc,cd->bijd', window, weight[di, dj].astype(jnp.float32), precision=lax.Precision.HIGHEST)
    return total

def weight_grad(padded, cot):

    def one_slot(pair):
        pad_one, cot_one = pair
        cot32 = cot_one.astype(jnp.float32)
        taps = []
        for di in range(3):
            row = []
            for dj in range(3):
                window = pad_one[:, di:di + S, dj:dj + S].astype(jnp.float32)
                row.append(jnp.einsum('bijc,bijd->cd', window, cot32, precision=lax.Precision.HIGHEST))
            taps.append(jnp.stack(row))
        return jnp.stack(taps)
    return lax.optimization_barrier(jnp.sum(lax.map(one_slot, (padded, cot)), axis=0))

def gelu_tanh(value):
    return jax.nn.gelu(value, approximate=True)

def reference(inputs, cotangent, weight_first, weight_second, slot_tile, neighbour_tile, neighbour_turns, corner_live):

    def padder(field):
        return pad_field(field, slot_tile, neighbour_tile, neighbour_turns, corner_live)

    def conv_all(field, weight):
        return lax.map(lambda padded: conv_tile(padded, weight), padder(field))
    padded_in = padder(inputs)
    hidden = lax.map(lambda padded: conv_tile(padded, weight_first), padded_in)
    active = gelu_tanh(hidden).astype(jnp.bfloat16)
    padded_act = padder(active)
    second32 = weight_second.astype(jnp.float32)
    first32 = weight_first.astype(jnp.float32)
    _, pull_second = jax.vjp(lambda v: conv_all(v, second32), active.astype(jnp.float32))
    grad_active = pull_second(cotangent.astype(jnp.float32))[0]
    _, pull_gelu = jax.vjp(gelu_tanh, hidden)
    grad_hidden = pull_gelu(grad_active)[0].astype(jnp.bfloat16)
    _, pull_first = jax.vjp(lambda v: conv_all(v, first32), inputs.astype(jnp.float32))
    grad_inputs = pull_first(grad_hidden.astype(jnp.float32))[0].astype(jnp.bfloat16)
    scale = 1.0 / math.sqrt(BATCH * TILES * S * S)
    grad_first = weight_grad(padded_in, grad_hidden) * scale
    grad_second = weight_grad(padded_act, cotangent) * scale
    return (grad_inputs, grad_first, grad_second)
```

```python
import math

import jax
import jax.numpy as jnp
import numpy as np
from jax import lax
from jax.sharding import PartitionSpec as P

REACH = 7

NEED_SIDE = (1, 0, 3, 2, 1, 1, 0, 0)


def side_tables():
    one = ((3, 0), (2, 0), (0, 1), (1, 1))
    side = np.zeros((4, 4), np.int32)
    flip = np.zeros((4, 4), np.int32)
    side[0] = np.arange(4)
    for r in range(1, 4):
        for s in range(4):
            s1, f1 = one[s]
            side[r, s] = side[r - 1, s1]
            flip[r, s] = flip[r - 1, s1] ^ f1
    return side, flip


def edge_rims(tile):
    return jnp.stack([tile[:, 0], tile[:, -1], tile[:, :, 0], tile[:, :, -1]])


def residues(devices):
    found = []
    for offset in range(-REACH, REACH + 1):
        res = offset % devices
        if res != 0 and res not in found:
            found.append(res)
    return found


def shift(value, by):
    length = lax.axis_size("space")
    return lax.ppermute(value, "space", [(i, (i + by) % length) for i in range(length)])


def exchange(own, offs):
    return jnp.stack([own] + [shift(own, (-o) % lax.axis_size("space")) for o in offs])


def make_plan(me, tables, devices, offs):
    slot_tile, slot_of_tile, neighbour_tile, neighbour_turns, corner_live = tables
    tile_id = slot_tile[me]
    owners = slot_of_tile[neighbour_tile[tile_id]]
    position = np.zeros((devices,), np.int32)
    for i, o in enumerate(offs):
        position[o] = i + 1
    position = jnp.asarray(position)
    from_idx = position[(owners - me) % devices]
    to_res = (owners - me) % devices
    turns = neighbour_turns[tile_id]
    side_tab, flip_tab = side_tables()
    need = jnp.asarray(np.array(NEED_SIDE, np.int32))
    sides = jnp.asarray(side_tab)[turns, need]
    flips = jnp.asarray(flip_tab)[turns, need]
    return from_idx, to_res, sides, flips, corner_live[tile_id]


def assemble(own, top, bottom, left, right, top_left, top_right, bottom_left, bottom_right):
    top_row = jnp.concatenate([top_left[:, None], top, top_right[:, None]], axis=1)
    bottom_row = jnp.concatenate([bottom_left[:, None], bottom, bottom_right[:, None]], axis=1)
    middle = jnp.concatenate([left[:, :, None], own, right[:, :, None]], axis=2)
    return jnp.concatenate([top_row[:, None], middle, bottom_row[:, None]], axis=1)


def pad_tile(tile, received, plan):
    from_idx, to_res, sides, flips, live = plan
    rows = []
    for k in range(8):
        row = received[from_idx[k], sides[k]]
        rows.append(jnp.where(flips[k] == 1, row[:, ::-1], row))
    flags = live.astype(tile.dtype)
    return assemble(
        tile,
        rows[0],
        rows[1],
        rows[2],
        rows[3],
        rows[4][:, -1] * flags[0],
        rows[5][:, 0] * flags[1],
        rows[6][:, -1] * flags[2],
        rows[7][:, 0] * flags[3],
    )


def conv_valid(padded, weight):
    return lax.conv_general_dilated(
        padded,
        weight,
        (1, 1),
        "VALID",
        dimension_numbers=("NHWC", "HWIO", "NHWC"),
        preferred_element_type=jnp.float32,
    )


def conv_full(cot, weight):
    flipped = jnp.flip(weight, (0, 1)).transpose(0, 1, 3, 2)
    return lax.conv_general_dilated(
        cot,
        flipped,
        (1, 1),
        ((2, 2), (2, 2)),
        dimension_numbers=("NHWC", "HWIO", "NHWC"),
        preferred_element_type=jnp.float32,
    )


def weight_grad(padded, cot):
    size = cot.shape[1]
    taps = []
    for di in range(3):
        row = []
        for dj in range(3):
            window = padded[:, di : di + size, dj : dj + size]
            row.append(jnp.einsum("bijc,bijd->cd", window, cot, preferred_element_type=jnp.float32))
        taps.append(jnp.stack(row))
    return jnp.stack(taps)


def send_buffers(full, plan, offs):
    from_idx, to_res, sides, flips, live = plan
    size = full.shape[1] - 2
    flags = live.astype(jnp.float32)
    rows = [full[:, 0, 1:-1], full[:, -1, 1:-1], full[:, 1:-1, 0], full[:, 1:-1, -1]]
    corners = [full[:, 0, 0] * flags[0], full[:, 0, -1] * flags[1],
               full[:, -1, 0] * flags[2], full[:, -1, -1] * flags[3]]
    ends = (size - 1, 0, size - 1, 0)
    cells = jnp.arange(size, dtype=jnp.int32)
    placed = []
    for k in range(8):
        if k < 4:
            vec = jnp.where(flips[k] == 1, rows[k][:, ::-1], rows[k])
        else:
            at = jnp.where(flips[k] == 1, size - 1 - ends[k - 4], ends[k - 4])
            vec = jnp.where((cells == at)[None, :, None], corners[k - 4][:, None, :], 0.0)
        pick = jnp.arange(4, dtype=jnp.int32) == sides[k]
        placed.append(jnp.where(pick[:, None, None, None], vec[None], 0.0))
    buffers = []
    for res in [0] + list(offs):
        total = None
        for k in range(8):
            term = jnp.where(to_res[k] == res, placed[k], 0.0)
            total = term if total is None else total + term
        buffers.append(total)
    return buffers


def return_rims(buffers, offs):
    total = buffers[0]
    for o, buf in zip(offs, buffers[1:]):
        total = total + shift(buf, o)
    return total


def add_rims(inner, total):
    inner = inner.at[:, 0].add(total[0]).at[:, -1].add(total[1])
    return inner.at[:, :, 0].add(total[2]).at[:, :, -1].add(total[3])


def xor_swap(value, axis, bit):
    size = lax.axis_size(axis)
    return lax.ppermute(value, axis, [(i, i ^ bit) for i in range(size)])


def all_reduce(flat, axes):
    stages = []
    for axis in axes:
        size = lax.axis_size(axis)
        if size & (size - 1):
            return lax.psum(flat, axes)
        bit = 1
        while bit < size:
            stages.append((axis, bit))
            bit *= 2
    if flat.shape[0] % (1 << len(stages)):
        return lax.psum(flat, axes)
    buf = flat
    for axis, bit in stages:
        half = buf.shape[0] // 2
        high = (lax.axis_index(axis) & bit) != 0
        low_part, high_part = buf[:half], buf[half:]
        send = jnp.where(high, low_part, high_part)
        keep = jnp.where(high, high_part, low_part)
        buf = keep + xor_swap(send, axis, bit)
    for axis, bit in reversed(stages):
        high = (lax.axis_index(axis) & bit) != 0
        other = xor_swap(buf, axis, bit)
        buf = jnp.where(high, jnp.concatenate([other, buf]), jnp.concatenate([buf, other]))
    return buf


def gelu_tanh(value):
    return jax.nn.gelu(value, approximate=True)


def shards(
    inputs,
    cotangent,
    weight_first,
    weight_second,
    slot_tile,
    neighbour_tile,
    neighbour_turns,
    corner_live,
):
    count = slot_tile.shape[0]
    devices = lax.axis_size("space")
    me = lax.axis_index("space")
    offs = residues(devices)
    slot_of_tile = (
        jnp.zeros((count,), jnp.int32).at[slot_tile].set(jnp.arange(count, dtype=jnp.int32))
    )
    tables = (slot_tile, slot_of_tile, neighbour_tile, neighbour_turns, corner_live)
    plan = make_plan(me, tables, devices, offs)
    tile = inputs[0]
    cot_tile = cotangent[0]
    samples_all = tile.shape[0] * lax.axis_size("dp") * devices
    scale = 1.0 / math.sqrt(samples_all * tile.shape[1] * tile.shape[2])

    got_in = exchange(edge_rims(tile), offs)
    full_second = conv_full(cot_tile, weight_second)
    back_second = return_rims(send_buffers(full_second, plan, offs), offs)

    padded_in = pad_tile(tile, got_in, plan)
    hidden = conv_valid(padded_in, weight_first)
    active = gelu_tanh(hidden).astype(jnp.bfloat16)
    got_act = exchange(edge_rims(active), offs)
    padded_act = pad_tile(active, got_act, plan)
    local_second = weight_grad(padded_act, cot_tile)

    grad_active = add_rims(full_second[:, 1:-1, 1:-1], back_second)
    _, pull_gelu = jax.vjp(gelu_tanh, hidden)
    grad_hidden = pull_gelu(grad_active)[0].astype(jnp.bfloat16)
    local_first = weight_grad(padded_in, grad_hidden)
    full_first = conv_full(grad_hidden, weight_first)
    back_first = return_rims(send_buffers(full_first, plan, offs), offs)
    grad_tile = add_rims(full_first[:, 1:-1, 1:-1], back_first).astype(jnp.bfloat16)

    flat = jnp.concatenate([local_first.reshape(-1), local_second.reshape(-1)])
    summed = all_reduce(flat, ("dp", "space"))
    half = local_first.size
    summed_first = summed[:half].reshape(local_first.shape)
    summed_second = summed[half:].reshape(local_second.shape)
    return (grad_tile[None], summed_first * scale, summed_second * scale)


def solution(mesh):
    in_specs = (
        P("space", "dp", None, None, None),
        P("space", "dp", None, None, None),
        P(),
        P(),
        P(),
        P(),
        P(),
        P(),
    )
    out_specs = (P("space", "dp", None, None, None), P(), P())
    return jax.shard_map(shards, mesh=mesh, in_specs=in_specs, out_specs=out_specs, check_vma=False)
```

```python
import math

import jax
import jax.numpy as jnp
import numpy as np
from jax import lax
from jax.sharding import PartitionSpec as P

REACH = 7

NEED_SIDE = (1, 0, 3, 2, 1, 1, 0, 0)


def side_tables():
    one = ((3, 0), (2, 0), (0, 1), (1, 1))
    side = np.zeros((4, 4), np.int32)
    flip = np.zeros((4, 4), np.int32)
    side[0] = np.arange(4)
    for r in range(1, 4):
        for s in range(4):
            s1, f1 = one[s]
            side[r, s] = side[r - 1, s1]
            flip[r, s] = flip[r - 1, s1] ^ f1
    return side, flip


def edge_rims(tile):
    return jnp.stack([tile[:, 0], tile[:, -1], tile[:, :, 0], tile[:, :, -1]])


def residues(devices):
    found = []
    for offset in range(-REACH, REACH + 1):
        res = offset % devices
        if res != 0 and res not in found:
            found.append(res)
    return found


def shift(value, by):
    length = lax.axis_size("space")
    return lax.ppermute(value, "space", [(i, (i + by) % length) for i in range(length)])


def exchange(own, offs):
    return jnp.stack([own] + [shift(own, (-o) % lax.axis_size("space")) for o in offs])


def make_plan(me, tables, devices, offs):
    slot_tile, slot_of_tile, neighbour_tile, neighbour_turns, corner_live = tables
    tile_id = slot_tile[me]
    owners = slot_of_tile[neighbour_tile[tile_id]]
    position = np.zeros((devices,), np.int32)
    for i, o in enumerate(offs):
        position[o] = i + 1
    res = (owners - me) % devices
    src = jnp.asarray(position)[res]
    turns = neighbour_turns[tile_id]
    side_tab, flip_tab = side_tables()
    need = np.array(NEED_SIDE, np.int32)
    sides = jnp.asarray(side_tab)[turns, need]
    flips = jnp.asarray(flip_tab)[turns, need]
    return src, res, sides, flips, corner_live[tile_id]


def flip_index(flips, size):
    cells = jnp.arange(size, dtype=jnp.int32)[None, :]
    return jnp.where(flips[:, None] == 1, size - 1 - cells, cells)


def assemble(own, top, bottom, left, right, top_left, top_right, bottom_left, bottom_right):
    top_row = jnp.concatenate([top_left[:, None], top, top_right[:, None]], axis=1)
    bottom_row = jnp.concatenate([bottom_left[:, None], bottom, bottom_right[:, None]], axis=1)
    middle = jnp.concatenate([left[:, :, None], own, right[:, :, None]], axis=2)
    return jnp.concatenate([top_row[:, None], middle, bottom_row[:, None]], axis=1)


def pad_tile(tile, received, plan):
    src, res, sides, flips, live = plan
    size = tile.shape[1]
    cells = flip_index(flips, size)
    picked = received[src[:, None], sides[:, None], :, cells]
    rows = picked.transpose(0, 2, 1, 3)
    corners = jnp.stack([rows[4][:, -1], rows[5][:, 0], rows[6][:, -1], rows[7][:, 0]])
    corners = corners * live.astype(tile.dtype)[:, None, None]
    return assemble(tile, rows[0], rows[1], rows[2], rows[3], corners[0], corners[1], corners[2], corners[3])


def conv_valid(padded, weight):
    return lax.conv_general_dilated(
        padded,
        weight,
        (1, 1),
        "VALID",
        dimension_numbers=("NHWC", "HWIO", "NHWC"),
        preferred_element_type=jnp.float32,
    )


def conv_full(cot, weight):
    flipped = jnp.flip(weight, (0, 1)).transpose(0, 1, 3, 2)
    return lax.conv_general_dilated(
        cot,
        flipped,
        (1, 1),
        ((2, 2), (2, 2)),
        dimension_numbers=("NHWC", "HWIO", "NHWC"),
        preferred_element_type=jnp.float32,
    )


def weight_grad(padded, cot):
    return lax.conv_general_dilated(
        padded,
        cot,
        (1, 1),
        "VALID",
        dimension_numbers=("CHWN", "IHWO", "HWNC"),
        preferred_element_type=jnp.float32,
    )


def send_buffers(full, plan, offs):
    src, res, sides, flips, live = plan
    size = full.shape[1] - 2
    rows = jnp.stack([full[:, 0, 1:-1], full[:, -1, 1:-1], full[:, 1:-1, 0], full[:, 1:-1, -1]])
    values = jnp.stack([full[:, 0, 0], full[:, 0, -1], full[:, -1, 0], full[:, -1, -1]])
    values = values * live.astype(jnp.float32)[:, None, None]
    ends = np.zeros((4, size), np.float32)
    ends[[0, 1, 2, 3], [size - 1, 0, size - 1, 0]] = 1.0
    corner_rows = jnp.asarray(ends)[:, None, :, None] * values[:, :, None, :]
    vecs = jnp.concatenate([rows, corner_rows]).transpose(0, 2, 1, 3)
    vecs = vecs[jnp.arange(8)[:, None], flip_index(flips, size)]
    targets = np.array([0] + list(offs), np.int32)
    mask = (res[None, None, :] == targets[:, None, None]) & (
        sides[None, None, :] == jnp.arange(4, dtype=jnp.int32)[None, :, None]
    )
    flat = vecs.reshape(8, -1)
    buffers = jnp.sum(jnp.where(mask[..., None], flat[None, None], 0.0), axis=2)
    shape = (len(targets), 4, size) + full.shape[:1] + full.shape[3:]
    return buffers.reshape(shape).transpose(0, 1, 3, 2, 4)


def return_rims(buffers, offs):
    total = buffers[0]
    for i, o in enumerate(offs):
        total = total + shift(buffers[i + 1], o)
    return total


def add_rims(inner, total):
    inner = inner.at[:, 0].add(total[0]).at[:, -1].add(total[1])
    return inner.at[:, :, 0].add(total[2]).at[:, :, -1].add(total[3])


def xor_swap(value, axis, bit):
    size = lax.axis_size(axis)
    return lax.ppermute(value, axis, [(i, i ^ bit) for i in range(size)])


def all_reduce(flat, axes):
    stages = []
    for axis in axes:
        size = lax.axis_size(axis)
        if size & (size - 1):
            return lax.psum(flat, axes)
        bit = 1
        while bit < size:
            stages.append((axis, bit))
            bit *= 2
    if flat.shape[0] % (1 << len(stages)):
        return lax.psum(flat, axes)
    buf = flat
    for axis, bit in stages:
        half = buf.shape[0] // 2
        high = (lax.axis_index(axis) & bit) != 0
        low_part, high_part = buf[:half], buf[half:]
        send = jnp.where(high, low_part, high_part)
        keep = jnp.where(high, high_part, low_part)
        buf = keep + xor_swap(send, axis, bit)
    for axis, bit in reversed(stages):
        high = (lax.axis_index(axis) & bit) != 0
        other = xor_swap(buf, axis, bit)
        buf = jnp.where(high, jnp.concatenate([other, buf]), jnp.concatenate([buf, other]))
    return buf


def gelu_tanh(value):
    return jax.nn.gelu(value, approximate=True)


def shards(
    inputs,
    cotangent,
    weight_first,
    weight_second,
    slot_tile,
    neighbour_tile,
    neighbour_turns,
    corner_live,
):
    count = slot_tile.shape[0]
    devices = lax.axis_size("space")
    me = lax.axis_index("space")
    offs = residues(devices)
    slot_of_tile = (
        jnp.zeros((count,), jnp.int32).at[slot_tile].set(jnp.arange(count, dtype=jnp.int32))
    )
    tables = (slot_tile, slot_of_tile, neighbour_tile, neighbour_turns, corner_live)
    plan = make_plan(me, tables, devices, offs)
    tile = inputs[0]
    cot_tile = cotangent[0]
    samples_all = tile.shape[0] * lax.axis_size("dp") * devices
    scale = 1.0 / math.sqrt(samples_all * tile.shape[1] * tile.shape[2])

    got_in = exchange(edge_rims(tile), offs)
    full_second = conv_full(cot_tile, weight_second)
    back_second = return_rims(send_buffers(full_second, plan, offs), offs)

    padded_in = pad_tile(tile, got_in, plan)
    hidden = conv_valid(padded_in, weight_first)
    active = gelu_tanh(hidden).astype(jnp.bfloat16)
    got_act = exchange(edge_rims(active), offs)
    padded_act = pad_tile(active, got_act, plan)
    local_second = weight_grad(padded_act, cot_tile)

    grad_active = add_rims(full_second[:, 1:-1, 1:-1], back_second)
    _, pull_gelu = jax.vjp(gelu_tanh, hidden)
    grad_hidden = pull_gelu(grad_active)[0].astype(jnp.bfloat16)
    local_first = weight_grad(padded_in, grad_hidden)
    full_first = conv_full(grad_hidden, weight_first)
    back_first = return_rims(send_buffers(full_first, plan, offs), offs)
    grad_tile = add_rims(full_first[:, 1:-1, 1:-1], back_first).astype(jnp.bfloat16)

    flat = jnp.concatenate([local_first.reshape(-1), local_second.reshape(-1)])
    summed = all_reduce(flat, ("dp", "space"))
    half = local_first.size
    summed_first = summed[:half].reshape(local_first.shape)
    summed_second = summed[half:].reshape(local_second.shape)
    return (grad_tile[None], summed_first * scale, summed_second * scale)


def solution(mesh):
    in_specs = (
        P("space", "dp", None, None, None),
        P("space", "dp", None, None, None),
        P(),
        P(),
        P(),
        P(),
        P(),
        P(),
    )
    out_specs = (P("space", "dp", None, None, None), P(), P())
    return jax.shard_map(shards, mesh=mesh, in_specs=in_specs, out_specs=out_specs, check_vma=False)
```

```python
import math

import jax
import jax.numpy as jnp
import numpy as np
from jax import lax
from jax.sharding import PartitionSpec as P

REACH = 7

NEED_SIDE = (1, 0, 3, 2, 1, 1, 0, 0)


def side_tables():
    one = ((3, 0), (2, 0), (0, 1), (1, 1))
    side = np.zeros((4, 4), np.int32)
    flip = np.zeros((4, 4), np.int32)
    side[0] = np.arange(4)
    for r in range(1, 4):
        for s in range(4):
            s1, f1 = one[s]
            side[r, s] = side[r - 1, s1]
            flip[r, s] = flip[r - 1, s1] ^ f1
    return side, flip


def edge_rims(tile):
    return jnp.stack([tile[:, 0], tile[:, -1], tile[:, :, 0], tile[:, :, -1]])


def residues(devices):
    found = []
    for offset in range(-REACH, REACH + 1):
        res = offset % devices
        if res != 0 and res not in found:
            found.append(res)
    return found


def shift(value, by):
    length = lax.axis_size("space")
    return lax.ppermute(value, "space", [(i, (i + by) % length) for i in range(length)])


def round_trip(pull, push, offs):
    devices = lax.axis_size("space")
    index = {o: i + 1 for i, o in enumerate(offs)}
    size = pull.shape[2]
    flat_pull = pull.transpose(0, 2, 1, 3).reshape(4 * size, -1)
    got = [flat_pull]
    total = push[0]
    for o in offs:
        back = (devices - o) % devices
        payload = jnp.concatenate([flat_pull.astype(jnp.float32), push[index[back]]])
        arrived = lax.ppermute(payload, "space", [(i, (i - o) % devices) for i in range(devices)])
        got.append(arrived[: 4 * size].astype(pull.dtype))
        total = total + arrived[4 * size :]
    back_rims = total.reshape((4, size) + pull.shape[1:2] + pull.shape[3:]).transpose(0, 2, 1, 3)
    return jnp.stack(got), back_rims


def make_plan(me, tables, devices, offs):
    slot_tile, slot_of_tile, neighbour_tile, neighbour_turns, corner_live = tables
    tile_id = slot_tile[me]
    owners = slot_of_tile[neighbour_tile[tile_id]]
    position = np.zeros((devices,), np.int32)
    for i, o in enumerate(offs):
        position[o] = i + 1
    res = (owners - me) % devices
    src = jnp.asarray(position)[res]
    turns = neighbour_turns[tile_id]
    side_tab, flip_tab = side_tables()
    need = np.array(NEED_SIDE, np.int32)
    sides = jnp.asarray(side_tab)[turns, need]
    flips = jnp.asarray(flip_tab)[turns, need]
    return src, res, sides, flips, corner_live[tile_id]


def flip_index(flips, size):
    cells = jnp.arange(size, dtype=jnp.int32)[None, :]
    return jnp.where(flips[:, None] == 1, size - 1 - cells, cells)


def assemble(own, top, bottom, left, right, top_left, top_right, bottom_left, bottom_right):
    top_row = jnp.concatenate([top_left[:, None], top, top_right[:, None]], axis=1)
    bottom_row = jnp.concatenate([bottom_left[:, None], bottom, bottom_right[:, None]], axis=1)
    middle = jnp.concatenate([left[:, :, None], own, right[:, :, None]], axis=2)
    return jnp.concatenate([top_row[:, None], middle, bottom_row[:, None]], axis=1)


def pad_tile(tile, received, plan):
    src, res, sides, flips, live = plan
    size = tile.shape[1]
    n_src = received.shape[0]
    cells = flip_index(flips, size)
    pick = (
        (jnp.arange(n_src)[None, None, :, None, None] == src[:, None, None, None, None])
        & (jnp.arange(4)[None, None, None, :, None] == sides[:, None, None, None, None])
        & (jnp.arange(size)[None, None, None, None, :] == cells[:, :, None, None, None])
    )
    pick = pick.reshape(8 * size, n_src * 4 * size).astype(tile.dtype)
    rows = jnp.dot(pick, received.reshape(n_src * 4 * size, -1), preferred_element_type=jnp.float32)
    rows = rows.astype(tile.dtype).reshape((8, size) + tile.shape[:1] + tile.shape[3:])
    rows = rows.transpose(0, 2, 1, 3)
    corners = jnp.stack([rows[4][:, -1], rows[5][:, 0], rows[6][:, -1], rows[7][:, 0]])
    corners = corners * live.astype(tile.dtype)[:, None, None]
    return assemble(tile, rows[0], rows[1], rows[2], rows[3], corners[0], corners[1], corners[2], corners[3])


def conv_valid(padded, weight):
    return lax.conv_general_dilated(
        padded,
        weight,
        (1, 1),
        "VALID",
        dimension_numbers=("NHWC", "HWIO", "NHWC"),
        preferred_element_type=jnp.float32,
    )


def conv_full(cot, weight):
    flipped = jnp.flip(weight, (0, 1)).transpose(0, 1, 3, 2)
    return lax.conv_general_dilated(
        cot,
        flipped,
        (1, 1),
        ((2, 2), (2, 2)),
        dimension_numbers=("NHWC", "HWIO", "NHWC"),
        preferred_element_type=jnp.float32,
    )


def weight_grad(padded, cot):
    return lax.conv_general_dilated(
        padded,
        cot,
        (1, 1),
        "VALID",
        dimension_numbers=("CHWN", "IHWO", "HWNC"),
        preferred_element_type=jnp.float32,
    )


def send_buffers(full, plan, offs):
    src, res, sides, flips, live = plan
    size = full.shape[1] - 2
    rows = jnp.stack([full[:, 0, 1:-1], full[:, -1, 1:-1], full[:, 1:-1, 0], full[:, 1:-1, -1]])
    values = jnp.stack([full[:, 0, 0], full[:, 0, -1], full[:, -1, 0], full[:, -1, -1]])
    values = values * live.astype(jnp.float32)[:, None, None]
    ends = np.zeros((4, size), np.float32)
    ends[[0, 1, 2, 3], [size - 1, 0, size - 1, 0]] = 1.0
    corner_rows = jnp.asarray(ends)[:, None, :, None] * values[:, :, None, :]
    vecs = jnp.concatenate([rows, corner_rows]).transpose(0, 2, 1, 3).reshape(8 * size, -1)
    targets = jnp.asarray(np.array([0] + list(offs), np.int32))
    count = len(offs) + 1
    cells = flip_index(flips, size)
    route = (
        (res[None, None, None, :, None] == targets[:, None, None, None, None])
        & (sides[None, None, None, :, None] == jnp.arange(4)[None, :, None, None, None])
        & (jnp.arange(size)[None, None, None, None, :] == cells.T[None, None, :, :, None])
    )
    route = route.reshape(count * 4 * size, 8 * size).astype(jnp.float32)
    buffers = jnp.dot(route, vecs, precision=lax.Precision.HIGHEST, preferred_element_type=jnp.float32)
    return buffers.reshape(count, 4 * size, -1)


def add_rims(inner, total):
    inner = inner.at[:, 0].add(total[0]).at[:, -1].add(total[1])
    return inner.at[:, :, 0].add(total[2]).at[:, :, -1].add(total[3])


def xor_swap(value, axis, bit):
    size = lax.axis_size(axis)
    return lax.ppermute(value, axis, [(i, i ^ bit) for i in range(size)])


def all_reduce(flat, axes):
    stages = []
    for axis in axes:
        size = lax.axis_size(axis)
        if size & (size - 1):
            return lax.psum(flat, axes)
        bit = 1
        while bit < size:
            stages.append((axis, bit))
            bit *= 2
    if flat.shape[0] % (1 << len(stages)):
        return lax.psum(flat, axes)
    buf = flat
    for axis, bit in stages:
        half = buf.shape[0] // 2
        high = (lax.axis_index(axis) & bit) != 0
        low_part, high_part = buf[:half], buf[half:]
        send = jnp.where(high, low_part, high_part)
        keep = jnp.where(high, high_part, low_part)
        buf = keep + xor_swap(send, axis, bit)
    for axis, bit in reversed(stages):
        high = (lax.axis_index(axis) & bit) != 0
        other = xor_swap(buf, axis, bit)
        buf = jnp.where(high, jnp.concatenate([other, buf]), jnp.concatenate([buf, other]))
    return buf


def gelu_tanh(value):
    return jax.nn.gelu(value, approximate=True)


def shards(
    inputs,
    cotangent,
    weight_first,
    weight_second,
    slot_tile,
    neighbour_tile,
    neighbour_turns,
    corner_live,
):
    count = slot_tile.shape[0]
    devices = lax.axis_size("space")
    me = lax.axis_index("space")
    offs = residues(devices)
    slot_of_tile = (
        jnp.zeros((count,), jnp.int32).at[slot_tile].set(jnp.arange(count, dtype=jnp.int32))
    )
    tables = (slot_tile, slot_of_tile, neighbour_tile, neighbour_turns, corner_live)
    plan = make_plan(me, tables, devices, offs)
    tile = inputs[0]
    cot_tile = cotangent[0]
    samples_all = tile.shape[0] * lax.axis_size("dp") * devices
    scale = 1.0 / math.sqrt(samples_all * tile.shape[1] * tile.shape[2])

    full_second = conv_full(cot_tile, weight_second)
    push_second = send_buffers(full_second, plan, offs)
    got_in, back_second = round_trip(edge_rims(tile), push_second, offs)

    padded_in = pad_tile(tile, got_in, plan)
    hidden = conv_valid(padded_in, weight_first)
    active = gelu_tanh(hidden).astype(jnp.bfloat16)

    grad_active = add_rims(full_second[:, 1:-1, 1:-1], back_second)
    _, pull_gelu = jax.vjp(gelu_tanh, hidden)
    grad_hidden = pull_gelu(grad_active)[0].astype(jnp.bfloat16)
    local_first = weight_grad(padded_in, grad_hidden)
    full_first = conv_full(grad_hidden, weight_first)
    push_first = send_buffers(full_first, plan, offs)
    got_act, back_first = round_trip(edge_rims(active), push_first, offs)

    padded_act = pad_tile(active, got_act, plan)
    local_second = weight_grad(padded_act, cot_tile)
    grad_tile = add_rims(full_first[:, 1:-1, 1:-1], back_first).astype(jnp.bfloat16)

    flat = jnp.concatenate([local_first.reshape(-1), local_second.reshape(-1)])
    summed = all_reduce(flat, ("dp", "space"))
    half = local_first.size
    summed_first = summed[:half].reshape(local_first.shape)
    summed_second = summed[half:].reshape(local_second.shape)
    return (grad_tile[None], summed_first * scale, summed_second * scale)


def solution(mesh):
    in_specs = (
        P("space", "dp", None, None, None),
        P("space", "dp", None, None, None),
        P(),
        P(),
        P(),
        P(),
        P(),
        P(),
    )
    out_specs = (P("space", "dp", None, None, None), P(), P())
    return jax.shard_map(shards, mesh=mesh, in_specs=in_specs, out_specs=out_specs, check_vma=False)
```

```python
import math

import jax
import jax.numpy as jnp
import numpy as np
from jax import lax
from jax.sharding import PartitionSpec as P

REACH = 7

NEED_SIDE = (1, 0, 3, 2, 1, 1, 0, 0)


def side_tables():
    one = ((3, 0), (2, 0), (0, 1), (1, 1))
    side = np.zeros((4, 4), np.int32)
    flip = np.zeros((4, 4), np.int32)
    side[0] = np.arange(4)
    for r in range(1, 4):
        for s in range(4):
            s1, f1 = one[s]
            side[r, s] = side[r - 1, s1]
            flip[r, s] = flip[r - 1, s1] ^ f1
    return side, flip


def edge_rims(tile):
    return jnp.stack([tile[:, 0], tile[:, -1], tile[:, :, 0], tile[:, :, -1]])


def residues(devices):
    found = []
    for offset in range(-REACH, REACH + 1):
        res = offset % devices
        if res != 0 and res not in found:
            found.append(res)
    return found


def shift(value, by):
    length = lax.axis_size("space")
    return lax.ppermute(value, "space", [(i, (i + by) % length) for i in range(length)])


def round_trip(pull, push, offs):
    devices = lax.axis_size("space")
    index = {o: i + 1 for i, o in enumerate(offs)}
    size = pull.shape[2]
    flat_pull = pull.transpose(0, 2, 1, 3).reshape(4 * size, -1)
    got = [flat_pull]
    total = push[0]
    for o in offs:
        back = (devices - o) % devices
        payload = jnp.concatenate([flat_pull.astype(jnp.float32), push[index[back]]])
        arrived = lax.ppermute(payload, "space", [(i, (i - o) % devices) for i in range(devices)])
        got.append(arrived[: 4 * size].astype(pull.dtype))
        total = total + arrived[4 * size :]
    back_rims = total.reshape((4, size) + pull.shape[1:2] + pull.shape[3:]).transpose(0, 2, 1, 3)
    return jnp.stack(got), back_rims


def make_plan(me, tables, devices, offs):
    slot_tile, slot_of_tile, neighbour_tile, neighbour_turns, corner_live = tables
    tile_id = slot_tile[me]
    owners = slot_of_tile[neighbour_tile[tile_id]]
    position = np.zeros((devices,), np.int32)
    for i, o in enumerate(offs):
        position[o] = i + 1
    res = (owners - me) % devices
    src = jnp.asarray(position)[res]
    turns = neighbour_turns[tile_id]
    side_tab, flip_tab = side_tables()
    need = np.array(NEED_SIDE, np.int32)
    sides = jnp.asarray(side_tab)[turns, need]
    flips = jnp.asarray(flip_tab)[turns, need]
    return src, res, sides, flips, corner_live[tile_id]


def flip_index(flips, size):
    cells = jnp.arange(size, dtype=jnp.int32)[None, :]
    return jnp.where(flips[:, None] == 1, size - 1 - cells, cells)


def assemble(own, top, bottom, left, right, top_left, top_right, bottom_left, bottom_right):
    top_row = jnp.concatenate([top_left[:, None], top, top_right[:, None]], axis=1)
    bottom_row = jnp.concatenate([bottom_left[:, None], bottom, bottom_right[:, None]], axis=1)
    middle = jnp.concatenate([left[:, :, None], own, right[:, :, None]], axis=2)
    return jnp.concatenate([top_row[:, None], middle, bottom_row[:, None]], axis=1)


def pad_tile(tile, received, plan):
    src, res, sides, flips, live = plan
    size = tile.shape[1]
    n_src = received.shape[0]
    cells = flip_index(flips, size)
    pick = (
        (jnp.arange(n_src)[None, None, :, None, None] == src[:, None, None, None, None])
        & (jnp.arange(4)[None, None, None, :, None] == sides[:, None, None, None, None])
        & (jnp.arange(size)[None, None, None, None, :] == cells[:, :, None, None, None])
    )
    pick = pick.reshape(8 * size, n_src * 4 * size).astype(tile.dtype)
    rows = jnp.dot(pick, received.reshape(n_src * 4 * size, -1), preferred_element_type=jnp.float32)
    rows = rows.astype(tile.dtype).reshape((8, size) + tile.shape[:1] + tile.shape[3:])
    rows = rows.transpose(0, 2, 1, 3)
    corners = jnp.stack([rows[4][:, -1], rows[5][:, 0], rows[6][:, -1], rows[7][:, 0]])
    corners = corners * live.astype(tile.dtype)[:, None, None]
    return assemble(tile, rows[0], rows[1], rows[2], rows[3], corners[0], corners[1], corners[2], corners[3])


def conv_valid(padded, weight):
    return lax.conv_general_dilated(
        padded,
        weight,
        (1, 1),
        "VALID",
        dimension_numbers=("NHWC", "HWIO", "NHWC"),
        preferred_element_type=jnp.float32,
    )


def conv_full(cot, weight):
    flipped = jnp.flip(weight, (0, 1)).transpose(0, 1, 3, 2)
    return lax.conv_general_dilated(
        cot,
        flipped,
        (1, 1),
        ((2, 2), (2, 2)),
        dimension_numbers=("NHWC", "HWIO", "NHWC"),
        preferred_element_type=jnp.float32,
    )


def weight_grad(padded, cot):
    return lax.conv_general_dilated(
        padded,
        cot,
        (1, 1),
        "VALID",
        dimension_numbers=("CHWN", "IHWO", "HWNC"),
        preferred_element_type=jnp.float32,
    )


def send_buffers(full, plan, offs):
    src, res, sides, flips, live = plan
    size = full.shape[1] - 2
    rows = jnp.stack([full[:, 0, 1:-1], full[:, -1, 1:-1], full[:, 1:-1, 0], full[:, 1:-1, -1]])
    values = jnp.stack([full[:, 0, 0], full[:, 0, -1], full[:, -1, 0], full[:, -1, -1]])
    values = values * live.astype(jnp.float32)[:, None, None]
    ends = np.zeros((4, size), np.float32)
    ends[[0, 1, 2, 3], [size - 1, 0, size - 1, 0]] = 1.0
    corner_rows = jnp.asarray(ends)[:, None, :, None] * values[:, :, None, :]
    vecs = jnp.concatenate([rows, corner_rows]).transpose(0, 2, 1, 3).reshape(8 * size, -1)
    targets = jnp.asarray(np.array([0] + list(offs), np.int32))
    count = len(offs) + 1
    cells = flip_index(flips, size)
    route = (
        (res[None, None, None, :, None] == targets[:, None, None, None, None])
        & (sides[None, None, None, :, None] == jnp.arange(4)[None, :, None, None, None])
        & (jnp.arange(size)[None, None, None, None, :] == cells.T[None, None, :, :, None])
    )
    route = route.reshape(count * 4 * size, 8 * size).astype(jnp.float32)
    buffers = jnp.dot(route, vecs, precision=lax.Precision.HIGHEST, preferred_element_type=jnp.float32)
    return buffers.reshape(count, 4 * size, -1)


def add_rims(inner, total):
    inner = inner.at[:, 0].add(total[0]).at[:, -1].add(total[1])
    return inner.at[:, :, 0].add(total[2]).at[:, :, -1].add(total[3])


def xor_swap(value, axis, bit):
    size = lax.axis_size(axis)
    return lax.ppermute(value, axis, [(i, i ^ bit) for i in range(size)])


def all_reduce(flat, axes):
    stages = []
    for axis in axes:
        size = lax.axis_size(axis)
        if size & (size - 1):
            return lax.psum(flat, axes)
        bit = 1
        while bit < size:
            stages.append((axis, bit))
            bit *= 2
    if flat.shape[0] % (1 << len(stages)):
        return lax.psum(flat, axes)
    buf = flat
    for axis, bit in stages:
        half = buf.shape[0] // 2
        high = (lax.axis_index(axis) & bit) != 0
        low_part, high_part = buf[:half], buf[half:]
        send = jnp.where(high, low_part, high_part)
        keep = jnp.where(high, high_part, low_part)
        buf = keep + xor_swap(send, axis, bit)
    for axis, bit in reversed(stages):
        high = (lax.axis_index(axis) & bit) != 0
        other = xor_swap(buf, axis, bit)
        buf = jnp.where(high, jnp.concatenate([other, buf]), jnp.concatenate([buf, other]))
    return buf


def gelu_tanh(value):
    return jax.nn.gelu(value, approximate=True)


def shards(
    inputs,
    cotangent,
    weight_first,
    weight_second,
    slot_tile,
    neighbour_tile,
    neighbour_turns,
    corner_live,
):
    count = slot_tile.shape[0]
    devices = lax.axis_size("space")
    me = lax.axis_index("space")
    offs = residues(devices)
    slot_of_tile = (
        jnp.zeros((count,), jnp.int32).at[slot_tile].set(jnp.arange(count, dtype=jnp.int32))
    )
    tables = (slot_tile, slot_of_tile, neighbour_tile, neighbour_turns, corner_live)
    plan = make_plan(me, tables, devices, offs)
    tile = inputs[0]
    cot_tile = cotangent[0]
    samples_all = tile.shape[0] * lax.axis_size("dp") * devices
    scale = 1.0 / math.sqrt(samples_all * tile.shape[1] * tile.shape[2])

    full_second = conv_full(cot_tile, weight_second)
    push_second = send_buffers(full_second, plan, offs)
    got_in, back_second = round_trip(edge_rims(tile), push_second, offs)

    padded_in = pad_tile(tile, got_in, plan)
    hidden = conv_valid(padded_in, weight_first)
    active = gelu_tanh(hidden).astype(jnp.bfloat16)

    grad_active = add_rims(full_second[:, 1:-1, 1:-1], back_second)
    _, pull_gelu = jax.vjp(gelu_tanh, hidden)
    grad_hidden = pull_gelu(grad_active)[0].astype(jnp.bfloat16)
    local_first = weight_grad(padded_in, grad_hidden)
    summed_first = all_reduce(local_first.reshape(-1), ("dp", "space")).reshape(local_first.shape)
    full_first = conv_full(grad_hidden, weight_first)
    push_first = send_buffers(full_first, plan, offs)
    got_act, back_first = round_trip(edge_rims(active), push_first, offs)

    padded_act = pad_tile(active, got_act, plan)
    local_second = weight_grad(padded_act, cot_tile)
    grad_tile = add_rims(full_first[:, 1:-1, 1:-1], back_first).astype(jnp.bfloat16)

    summed_second = all_reduce(local_second.reshape(-1), ("dp", "space")).reshape(local_second.shape)
    return (grad_tile[None], summed_first * scale, summed_second * scale)


def solution(mesh):
    in_specs = (
        P("space", "dp", None, None, None),
        P("space", "dp", None, None, None),
        P(),
        P(),
        P(),
        P(),
        P(),
        P(),
    )
    out_specs = (P("space", "dp", None, None, None), P(), P())
    return jax.shard_map(shards, mesh=mesh, in_specs=in_specs, out_specs=out_specs, check_vma=False)
```

```python
import math

import jax
import jax.numpy as jnp
import numpy as np
from jax import lax
from jax.sharding import PartitionSpec as P

REACH = 7

NEED_SIDE = (1, 0, 3, 2, 1, 1, 0, 0)


def side_tables():
    one = ((3, 0), (2, 0), (0, 1), (1, 1))
    side = np.zeros((4, 4), np.int32)
    flip = np.zeros((4, 4), np.int32)
    side[0] = np.arange(4)
    for r in range(1, 4):
        for s in range(4):
            s1, f1 = one[s]
            side[r, s] = side[r - 1, s1]
            flip[r, s] = flip[r - 1, s1] ^ f1
    return side, flip


def edge_rims(tile):
    return jnp.stack([tile[:, 0], tile[:, -1], tile[:, :, 0], tile[:, :, -1]])


def residues(devices):
    found = []
    for offset in range(-REACH, REACH + 1):
        res = offset % devices
        if res != 0 and res not in found:
            found.append(res)
    return found


def shift(value, by):
    length = lax.axis_size("space")
    return lax.ppermute(value, "space", [(i, (i + by) % length) for i in range(length)])


def round_trip(pull, push, offs):
    devices = lax.axis_size("space")
    index = {o: i + 1 for i, o in enumerate(offs)}
    rows = pull.shape[1]
    got_pull = [pull[0]]
    got_push = [push[0]]
    for o in offs:
        back = index[(devices - o) % devices]
        payload = jnp.concatenate([pull[back].astype(jnp.float32), push[back]])
        arrived = lax.ppermute(payload, "space", [(i, (i - o) % devices) for i in range(devices)])
        got_pull.append(arrived[:rows].astype(pull.dtype))
        got_push.append(arrived[rows:])
    return jnp.stack(got_pull), jnp.stack(got_push)


def make_plans(tables, devices):
    slot_tile, slot_of_tile, neighbour_tile, neighbour_turns, corner_live = tables
    slots = jnp.arange(devices, dtype=jnp.int32)
    owners = slot_of_tile[neighbour_tile[slot_tile]]
    res = (owners - slots[:, None]) % devices
    turns = neighbour_turns[slot_tile]
    side_tab, flip_tab = side_tables()
    need = np.array(NEED_SIDE, np.int32)[None, :]
    sides = jnp.asarray(side_tab)[turns, need]
    flips = jnp.asarray(flip_tab)[turns, need]
    edge = res[:, :4]
    earlier = np.tril(np.ones((4, 4), bool), -1)
    rank = jnp.sum((edge[:, :, None] == edge[:, None, :]) & earlier, axis=2)
    return res, rank, sides, flips, corner_live[slot_tile]


def flip_index(flips, size):
    cells = jnp.arange(size, dtype=jnp.int32)[None, :]
    return jnp.where(flips[:, None] == 1, size - 1 - cells, cells)


def assemble(own, top, bottom, left, right, top_left, top_right, bottom_left, bottom_right):
    top_row = jnp.concatenate([top_left[:, None], top, top_right[:, None]], axis=1)
    bottom_row = jnp.concatenate([bottom_left[:, None], bottom, bottom_right[:, None]], axis=1)
    middle = jnp.concatenate([left[:, :, None], own, right[:, :, None]], axis=2)
    return jnp.concatenate([top_row[:, None], middle, bottom_row[:, None]], axis=1)


def corner_at(flips, size):
    ends = np.array([size - 1, 0, size - 1, 0], np.int32)
    return jnp.where(flips == 1, size - 1 - ends, ends)


def to_rows(flat, like):
    size = like.shape[1]
    return flat.reshape((-1, size) + like.shape[:1] + like.shape[3:]).transpose(0, 2, 1, 3)


def from_rows(rims):
    return rims.transpose(0, 2, 1, 3).reshape(rims.shape[0] * rims.shape[2], -1)


def pull_payloads(tile, theirs, back):
    res, rank, sides, flips, live = theirs
    size = tile.shape[1]
    hit = res == back[:, None]
    q = jnp.arange(2)[None, :, None, None]
    s = jnp.arange(4)[None, None, :, None]
    edge = jnp.sum(
        hit[:, None, None, :4] & (rank[:, None, None, :] == q) & (sides[:, None, None, :4] == s), axis=3
    )
    eye = jnp.eye(size, dtype=jnp.bool_)
    edge = (edge[:, :, None, :, None] > 0) & eye[None, None, :, None, :]
    at = corner_at(flips[:, 4:], size)
    corner = (
        hit[:, 4:, None, None]
        & (sides[:, 4:, None, None] == jnp.arange(4)[None, None, :, None])
        & (jnp.arange(size)[None, None, None, :] == at[:, :, None, None])
    )
    count = res.shape[0]
    pick = jnp.concatenate([edge.reshape(count, 2 * size, 4 * size), corner.reshape(count, 4, 4 * size)], axis=1)
    rims = from_rows(edge_rims(tile))
    out = jnp.einsum("twx,xc->twc", pick.astype(tile.dtype), rims, preferred_element_type=jnp.float32)
    return out.astype(tile.dtype)


def pad_tile(tile, received, mine, position):
    res, rank, sides, flips, live = mine
    size = tile.shape[1]
    n_src, width = received.shape[0], received.shape[1]
    src = jnp.asarray(position)[res]
    cells = flip_index(flips[:4], size)
    column = rank[:, None] * size + cells
    edge = (jnp.arange(n_src)[None, None, :, None] == src[:4, None, None, None]) & (
        jnp.arange(width)[None, None, None, :] == column[:, :, None, None]
    )
    corner = (jnp.arange(n_src)[None, :, None] == src[4:, None, None]) & (
        jnp.arange(width)[None, None, :] == (2 * size + jnp.arange(4))[:, None, None]
    )
    pick = jnp.concatenate([edge.reshape(4 * size, n_src * width), corner.reshape(4, n_src * width)])
    flat = jnp.dot(pick.astype(tile.dtype), received.reshape(n_src * width, -1), preferred_element_type=jnp.float32)
    flat = flat.astype(tile.dtype)
    rows = to_rows(flat[: 4 * size], tile)
    corners = flat[4 * size :].reshape((4,) + tile.shape[:1] + tile.shape[3:])
    corners = corners * live.astype(tile.dtype)[:, None, None]
    return assemble(tile, rows[0], rows[1], rows[2], rows[3], corners[0], corners[1], corners[2], corners[3])


def conv_valid(padded, weight):
    return lax.conv_general_dilated(
        padded,
        weight,
        (1, 1),
        "VALID",
        dimension_numbers=("NHWC", "HWIO", "NHWC"),
        preferred_element_type=jnp.float32,
    )


def conv_full(cot, weight):
    flipped = jnp.flip(weight, (0, 1)).transpose(0, 1, 3, 2)
    return lax.conv_general_dilated(
        cot,
        flipped,
        (1, 1),
        ((2, 2), (2, 2)),
        dimension_numbers=("NHWC", "HWIO", "NHWC"),
        preferred_element_type=jnp.float32,
    )


def weight_grad(padded, cot):
    return lax.conv_general_dilated(
        padded,
        cot,
        (1, 1),
        "VALID",
        dimension_numbers=("CHWN", "IHWO", "HWNC"),
        preferred_element_type=jnp.float32,
    )


def push_payloads(full, mine, resid):
    res, rank, sides, flips, live = mine
    size = full.shape[1] - 2
    rows = jnp.stack([full[:, 0, 1:-1], full[:, -1, 1:-1], full[:, 1:-1, 0], full[:, 1:-1, -1]])
    values = jnp.stack([full[:, 0, 0], full[:, 0, -1], full[:, -1, 0], full[:, -1, -1]])
    values = values * live.astype(jnp.float32)[:, None, None]
    source = jnp.concatenate([from_rows(rows), values.reshape(4, -1)])
    hit = res[None, :] == jnp.asarray(resid)[:, None]
    count = len(resid)
    edge = hit[:, None, :4] & (rank[None, None, :] == jnp.arange(2)[None, :, None])
    eye = jnp.eye(size, dtype=jnp.bool_)
    edge = edge[:, :, None, :, None] & eye[None, None, :, None, :]
    edge = jnp.concatenate(
        [edge.reshape(count, 2 * size, 4 * size), jnp.zeros((count, 2 * size, 4), jnp.bool_)], axis=2
    )
    corner = hit[:, 4:, None] & jnp.eye(4, dtype=jnp.bool_)[None]
    corner = jnp.concatenate([jnp.zeros((count, 4, 4 * size), jnp.bool_), corner], axis=2)
    route = jnp.concatenate([edge, corner], axis=1).astype(jnp.float32)
    return jnp.einsum(
        "twx,xc->twc", route, source, precision=lax.Precision.HIGHEST, preferred_element_type=jnp.float32
    )


def back_rims(received, theirs, back, like):
    res, rank, sides, flips, live = theirs
    size = like.shape[1]
    n_src, width = received.shape[0], received.shape[1]
    hit = res == back[:, None]
    s = jnp.arange(4)[:, None, None, None, None]
    j = jnp.arange(size)[None, :, None, None, None]
    q = (jnp.arange(width) // size)[None, None, None, :, None]
    jj = (jnp.arange(width) % size)[None, None, None, :, None]
    in_edge = (jnp.arange(width) < 2 * size)[None, None, None, :, None]
    e_hit = hit[None, None, :, None, :4]
    e_side = sides[None, None, :, None, :4] == s
    e_rank = rank[None, None, :, None, :] == q
    e_cell = jnp.where(flips[None, None, :, None, :4] == 1, size - 1 - j, j) == jj
    edge = jnp.any(e_hit & e_side & e_rank & e_cell & in_edge, axis=4)
    at = corner_at(flips[:, 4:], size)
    c_slot = (jnp.arange(width) - 2 * size)[None, None, None, :, None] == jnp.arange(4)[None, None, None, None, :]
    c_hit = hit[None, None, :, None, 4:] & (sides[None, None, :, None, 4:] == s)
    c_cell = j == at[None, None, :, None, :]
    corner = jnp.any(c_hit & c_cell & c_slot, axis=4)
    route = (edge | corner).reshape(4 * size, n_src * width).astype(jnp.float32)
    flat = jnp.dot(
        route, received.reshape(n_src * width, -1), precision=lax.Precision.HIGHEST,
        preferred_element_type=jnp.float32,
    )
    return to_rows(flat, like)


def add_rims(inner, total):
    inner = inner.at[:, 0].add(total[0]).at[:, -1].add(total[1])
    return inner.at[:, :, 0].add(total[2]).at[:, :, -1].add(total[3])


def xor_swap(value, axis, bit):
    size = lax.axis_size(axis)
    return lax.ppermute(value, axis, [(i, i ^ bit) for i in range(size)])


def all_reduce(flat, axes):
    stages = []
    for axis in axes:
        size = lax.axis_size(axis)
        if size & (size - 1):
            return lax.psum(flat, axes)
        bit = 1
        while bit < size:
            stages.append((axis, bit))
            bit *= 2
    if flat.shape[0] % (1 << len(stages)):
        return lax.psum(flat, axes)
    buf = flat
    for axis, bit in stages:
        half = buf.shape[0] // 2
        high = (lax.axis_index(axis) & bit) != 0
        low_part, high_part = buf[:half], buf[half:]
        send = jnp.where(high, low_part, high_part)
        keep = jnp.where(high, high_part, low_part)
        buf = keep + xor_swap(send, axis, bit)
    for axis, bit in reversed(stages):
        high = (lax.axis_index(axis) & bit) != 0
        other = xor_swap(buf, axis, bit)
        buf = jnp.where(high, jnp.concatenate([other, buf]), jnp.concatenate([buf, other]))
    return buf


def gelu_tanh(value):
    return jax.nn.gelu(value, approximate=True)


def shards(
    inputs,
    cotangent,
    weight_first,
    weight_second,
    slot_tile,
    neighbour_tile,
    neighbour_turns,
    corner_live,
):
    count = slot_tile.shape[0]
    devices = lax.axis_size("space")
    me = lax.axis_index("space")
    offs = residues(devices)
    slot_of_tile = (
        jnp.zeros((count,), jnp.int32).at[slot_tile].set(jnp.arange(count, dtype=jnp.int32))
    )
    tables = (slot_tile, slot_of_tile, neighbour_tile, neighbour_turns, corner_live)
    plans = make_plans(tables, devices)
    resid = np.array([0] + offs, np.int32)
    position = np.zeros((devices,), np.int32)
    position[resid] = np.arange(len(resid))
    back = jnp.asarray((-resid) % devices)
    mine = tuple(p[me] for p in plans)
    theirs = tuple(p[(me + resid) % devices] for p in plans)
    tile = inputs[0]
    cot_tile = cotangent[0]
    samples_all = tile.shape[0] * lax.axis_size("dp") * devices
    scale = 1.0 / math.sqrt(samples_all * tile.shape[1] * tile.shape[2])

    full_second = conv_full(cot_tile, weight_second)
    push_second = push_payloads(full_second, mine, resid)
    got_in, got_second = round_trip(pull_payloads(tile, theirs, back), push_second, offs)

    padded_in = pad_tile(tile, got_in, mine, position)
    hidden = conv_valid(padded_in, weight_first)
    active = gelu_tanh(hidden).astype(jnp.bfloat16)

    inner_second = full_second[:, 1:-1, 1:-1]
    grad_active = add_rims(inner_second, back_rims(got_second, theirs, back, inner_second))
    _, pull_gelu = jax.vjp(gelu_tanh, hidden)
    grad_hidden = pull_gelu(grad_active)[0].astype(jnp.bfloat16)
    local_first = weight_grad(padded_in, grad_hidden)
    full_first = conv_full(grad_hidden, weight_first)
    push_first = push_payloads(full_first, mine, resid)
    got_act, got_first = round_trip(pull_payloads(active, theirs, back), push_first, offs)

    padded_act = pad_tile(active, got_act, mine, position)
    local_second = weight_grad(padded_act, cot_tile)
    inner_first = full_first[:, 1:-1, 1:-1]
    grad_tile = add_rims(inner_first, back_rims(got_first, theirs, back, inner_first))
    grad_tile = grad_tile.astype(jnp.bfloat16)

    flat = jnp.concatenate([local_first.reshape(-1), local_second.reshape(-1)])
    summed = all_reduce(flat, ("dp", "space"))
    half = local_first.size
    summed_first = summed[:half].reshape(local_first.shape)
    summed_second = summed[half:].reshape(local_second.shape)
    return (grad_tile[None], summed_first * scale, summed_second * scale)


def solution(mesh):
    in_specs = (
        P("space", "dp", None, None, None),
        P("space", "dp", None, None, None),
        P(),
        P(),
        P(),
        P(),
        P(),
        P(),
    )
    out_specs = (P("space", "dp", None, None, None), P(), P())
    return jax.shard_map(shards, mesh=mesh, in_specs=in_specs, out_specs=out_specs, check_vma=False)
```

```python
import math

import jax
import jax.numpy as jnp
import numpy as np
from jax import lax
from jax.sharding import PartitionSpec as P

REACH = 7

NEED_SIDE = (1, 0, 3, 2, 1, 1, 0, 0)


def side_tables():
    one = ((3, 0), (2, 0), (0, 1), (1, 1))
    side = np.zeros((4, 4), np.int32)
    flip = np.zeros((4, 4), np.int32)
    side[0] = np.arange(4)
    for r in range(1, 4):
        for s in range(4):
            s1, f1 = one[s]
            side[r, s] = side[r - 1, s1]
            flip[r, s] = flip[r - 1, s1] ^ f1
    return side, flip


def edge_rims(tile):
    return jnp.stack([tile[:, 0], tile[:, -1], tile[:, :, 0], tile[:, :, -1]])


def residues(devices):
    found = []
    for offset in range(-REACH, REACH + 1):
        res = offset % devices
        if res != 0 and res not in found:
            found.append(res)
    return found


def shift(value, by):
    length = lax.axis_size("space")
    return lax.ppermute(value, "space", [(i, (i + by) % length) for i in range(length)])


def swap_all(pull, push):
    rows = pull.shape[1]
    payload = jnp.concatenate([pull.astype(jnp.float32), push], axis=1)
    arrived = lax.all_to_all(payload, "space", 0, 0)
    return arrived[:, :rows].astype(pull.dtype), arrived[:, rows:]


def round_trip(pull, push, offs):
    devices = lax.axis_size("space")
    index = {o: i + 1 for i, o in enumerate(offs)}
    rows = pull.shape[1]
    got_pull = [pull[0]]
    got_push = [push[0]]
    for o in offs:
        back = index[(devices - o) % devices]
        payload = jnp.concatenate([pull[back].astype(jnp.float32), push[back]])
        arrived = lax.ppermute(payload, "space", [(i, (i - o) % devices) for i in range(devices)])
        got_pull.append(arrived[:rows].astype(pull.dtype))
        got_push.append(arrived[rows:])
    return jnp.stack(got_pull), jnp.stack(got_push)


def make_plans(tables, devices):
    slot_tile, slot_of_tile, neighbour_tile, neighbour_turns, corner_live = tables
    slots = jnp.arange(devices, dtype=jnp.int32)
    owners = slot_of_tile[neighbour_tile[slot_tile]]
    res = (owners - slots[:, None]) % devices
    turns = neighbour_turns[slot_tile]
    side_tab, flip_tab = side_tables()
    need = np.array(NEED_SIDE, np.int32)[None, :]
    sides = jnp.asarray(side_tab)[turns, need]
    flips = jnp.asarray(flip_tab)[turns, need]
    edge = res[:, :4]
    earlier = np.tril(np.ones((4, 4), bool), -1)
    rank = jnp.sum((edge[:, :, None] == edge[:, None, :]) & earlier, axis=2)
    return res, rank, sides, flips, corner_live[slot_tile]


def flip_index(flips, size):
    cells = jnp.arange(size, dtype=jnp.int32)[None, :]
    return jnp.where(flips[:, None] == 1, size - 1 - cells, cells)


def assemble(own, top, bottom, left, right, top_left, top_right, bottom_left, bottom_right):
    top_row = jnp.concatenate([top_left[:, None], top, top_right[:, None]], axis=1)
    bottom_row = jnp.concatenate([bottom_left[:, None], bottom, bottom_right[:, None]], axis=1)
    middle = jnp.concatenate([left[:, :, None], own, right[:, :, None]], axis=2)
    return jnp.concatenate([top_row[:, None], middle, bottom_row[:, None]], axis=1)


def corner_at(flips, size):
    ends = np.array([size - 1, 0, size - 1, 0], np.int32)
    return jnp.where(flips == 1, size - 1 - ends, ends)


def to_rows(flat, like):
    size = like.shape[1]
    return flat.reshape((-1, size) + like.shape[:1] + like.shape[3:]).transpose(0, 2, 1, 3)


def from_rows(rims):
    return rims.transpose(0, 2, 1, 3).reshape(rims.shape[0] * rims.shape[2], -1)


def pull_payloads(tile, theirs, back):
    res, rank, sides, flips, live = theirs
    size = tile.shape[1]
    hit = res == back[:, None]
    q = jnp.arange(2)[None, :, None, None]
    s = jnp.arange(4)[None, None, :, None]
    edge = jnp.sum(
        hit[:, None, None, :4] & (rank[:, None, None, :] == q) & (sides[:, None, None, :4] == s), axis=3
    )
    eye = jnp.eye(size, dtype=jnp.bool_)
    edge = (edge[:, :, None, :, None] > 0) & eye[None, None, :, None, :]
    at = corner_at(flips[:, 4:], size)
    corner = (
        hit[:, 4:, None, None]
        & (sides[:, 4:, None, None] == jnp.arange(4)[None, None, :, None])
        & (jnp.arange(size)[None, None, None, :] == at[:, :, None, None])
    )
    count = res.shape[0]
    pick = jnp.concatenate([edge.reshape(count, 2 * size, 4 * size), corner.reshape(count, 4, 4 * size)], axis=1)
    rims = from_rows(edge_rims(tile))
    out = jnp.einsum("twx,xc->twc", pick.astype(tile.dtype), rims, preferred_element_type=jnp.float32)
    return out.astype(tile.dtype)


def pad_tile(tile, received, mine, position):
    res, rank, sides, flips, live = mine
    size = tile.shape[1]
    n_src, width = received.shape[0], received.shape[1]
    src = jnp.asarray(position)[res]
    cells = flip_index(flips[:4], size)
    column = rank[:, None] * size + cells
    edge = (jnp.arange(n_src)[None, None, :, None] == src[:4, None, None, None]) & (
        jnp.arange(width)[None, None, None, :] == column[:, :, None, None]
    )
    corner = (jnp.arange(n_src)[None, :, None] == src[4:, None, None]) & (
        jnp.arange(width)[None, None, :] == (2 * size + jnp.arange(4))[:, None, None]
    )
    pick = jnp.concatenate([edge.reshape(4 * size, n_src * width), corner.reshape(4, n_src * width)])
    flat = jnp.dot(pick.astype(tile.dtype), received.reshape(n_src * width, -1), preferred_element_type=jnp.float32)
    flat = flat.astype(tile.dtype)
    rows = to_rows(flat[: 4 * size], tile)
    corners = flat[4 * size :].reshape((4,) + tile.shape[:1] + tile.shape[3:])
    corners = corners * live.astype(tile.dtype)[:, None, None]
    return assemble(tile, rows[0], rows[1], rows[2], rows[3], corners[0], corners[1], corners[2], corners[3])


def conv_valid(padded, weight):
    return lax.conv_general_dilated(
        padded,
        weight,
        (1, 1),
        "VALID",
        dimension_numbers=("NHWC", "HWIO", "NHWC"),
        preferred_element_type=jnp.float32,
    )


def conv_full(cot, weight):
    flipped = jnp.flip(weight, (0, 1)).transpose(0, 1, 3, 2)
    return lax.conv_general_dilated(
        cot,
        flipped,
        (1, 1),
        ((2, 2), (2, 2)),
        dimension_numbers=("NHWC", "HWIO", "NHWC"),
        preferred_element_type=jnp.float32,
    )


def weight_grad(padded, cot):
    return lax.conv_general_dilated(
        padded,
        cot,
        (1, 1),
        "VALID",
        dimension_numbers=("CHWN", "IHWO", "HWNC"),
        preferred_element_type=jnp.float32,
    )


def push_payloads(full, mine, resid):
    res, rank, sides, flips, live = mine
    size = full.shape[1] - 2
    rows = jnp.stack([full[:, 0, 1:-1], full[:, -1, 1:-1], full[:, 1:-1, 0], full[:, 1:-1, -1]])
    values = jnp.stack([full[:, 0, 0], full[:, 0, -1], full[:, -1, 0], full[:, -1, -1]])
    values = values * live.astype(jnp.float32)[:, None, None]
    source = jnp.concatenate([from_rows(rows), values.reshape(4, -1)])
    hit = res[None, :] == jnp.asarray(resid)[:, None]
    count = resid.shape[0]
    edge = hit[:, None, :4] & (rank[None, None, :] == jnp.arange(2)[None, :, None])
    eye = jnp.eye(size, dtype=jnp.bool_)
    edge = edge[:, :, None, :, None] & eye[None, None, :, None, :]
    edge = jnp.concatenate(
        [edge.reshape(count, 2 * size, 4 * size), jnp.zeros((count, 2 * size, 4), jnp.bool_)], axis=2
    )
    corner = hit[:, 4:, None] & jnp.eye(4, dtype=jnp.bool_)[None]
    corner = jnp.concatenate([jnp.zeros((count, 4, 4 * size), jnp.bool_), corner], axis=2)
    route = jnp.concatenate([edge, corner], axis=1).astype(jnp.float32)
    return jnp.einsum(
        "twx,xc->twc", route, source, precision=lax.Precision.HIGHEST, preferred_element_type=jnp.float32
    )


def back_rims(received, theirs, back, like):
    res, rank, sides, flips, live = theirs
    size = like.shape[1]
    n_src, width = received.shape[0], received.shape[1]
    hit = res == back[:, None]
    s = jnp.arange(4)[:, None, None, None, None]
    j = jnp.arange(size)[None, :, None, None, None]
    q = (jnp.arange(width) // size)[None, None, None, :, None]
    jj = (jnp.arange(width) % size)[None, None, None, :, None]
    in_edge = (jnp.arange(width) < 2 * size)[None, None, None, :, None]
    e_hit = hit[None, None, :, None, :4]
    e_side = sides[None, None, :, None, :4] == s
    e_rank = rank[None, None, :, None, :] == q
    e_cell = jnp.where(flips[None, None, :, None, :4] == 1, size - 1 - j, j) == jj
    edge = jnp.any(e_hit & e_side & e_rank & e_cell & in_edge, axis=4)
    at = corner_at(flips[:, 4:], size)
    c_slot = (jnp.arange(width) - 2 * size)[None, None, None, :, None] == jnp.arange(4)[None, None, None, None, :]
    c_hit = hit[None, None, :, None, 4:] & (sides[None, None, :, None, 4:] == s)
    c_cell = j == at[None, None, :, None, :]
    corner = jnp.any(c_hit & c_cell & c_slot, axis=4)
    route = (edge | corner).reshape(4 * size, n_src * width).astype(jnp.float32)
    flat = jnp.dot(
        route, received.reshape(n_src * width, -1), precision=lax.Precision.HIGHEST,
        preferred_element_type=jnp.float32,
    )
    return to_rows(flat, like)


def add_rims(inner, total):
    inner = inner.at[:, 0].add(total[0]).at[:, -1].add(total[1])
    return inner.at[:, :, 0].add(total[2]).at[:, :, -1].add(total[3])


def xor_swap(value, axis, bit):
    size = lax.axis_size(axis)
    return lax.ppermute(value, axis, [(i, i ^ bit) for i in range(size)])


def all_reduce(flat, axes):
    stages = []
    for axis in axes:
        size = lax.axis_size(axis)
        if size & (size - 1):
            return lax.psum(flat, axes)
        bit = 1
        while bit < size:
            stages.append((axis, bit))
            bit *= 2
    if flat.shape[0] % (1 << len(stages)):
        return lax.psum(flat, axes)
    buf = flat
    for axis, bit in stages:
        half = buf.shape[0] // 2
        high = (lax.axis_index(axis) & bit) != 0
        low_part, high_part = buf[:half], buf[half:]
        send = jnp.where(high, low_part, high_part)
        keep = jnp.where(high, high_part, low_part)
        buf = keep + xor_swap(send, axis, bit)
    for axis, bit in reversed(stages):
        high = (lax.axis_index(axis) & bit) != 0
        other = xor_swap(buf, axis, bit)
        buf = jnp.where(high, jnp.concatenate([other, buf]), jnp.concatenate([buf, other]))
    return buf


def gelu_tanh(value):
    return jax.nn.gelu(value, approximate=True)


def shards(
    inputs,
    cotangent,
    weight_first,
    weight_second,
    slot_tile,
    neighbour_tile,
    neighbour_turns,
    corner_live,
):
    count = slot_tile.shape[0]
    devices = lax.axis_size("space")
    me = lax.axis_index("space")
    offs = residues(devices)
    slot_of_tile = (
        jnp.zeros((count,), jnp.int32).at[slot_tile].set(jnp.arange(count, dtype=jnp.int32))
    )
    tables = (slot_tile, slot_of_tile, neighbour_tile, neighbour_turns, corner_live)
    plans = make_plans(tables, devices)
    if devices <= 2 * REACH + 1:
        offs = None
        every = jnp.arange(devices, dtype=jnp.int32)
        resid = (every - me) % devices
        position = (every + me) % devices
        back = (me - every) % devices
        theirs = plans
    else:
        resid = np.array([0] + offs, np.int32)
        position = np.zeros((devices,), np.int32)
        position[resid] = np.arange(len(resid))
        back = jnp.asarray((-resid) % devices)
        theirs = tuple(p[(me + resid) % devices] for p in plans)
    mine = tuple(p[me] for p in plans)

    def trip(pull, push):
        if offs is None:
            return swap_all(pull, push)
        return round_trip(pull, push, offs)

    tile = inputs[0]
    cot_tile = cotangent[0]
    samples_all = tile.shape[0] * lax.axis_size("dp") * devices
    scale = 1.0 / math.sqrt(samples_all * tile.shape[1] * tile.shape[2])

    full_second = conv_full(cot_tile, weight_second)
    push_second = push_payloads(full_second, mine, resid)
    got_in, got_second = trip(pull_payloads(tile, theirs, back), push_second)

    padded_in = pad_tile(tile, got_in, mine, position)
    hidden = conv_valid(padded_in, weight_first)
    active = gelu_tanh(hidden).astype(jnp.bfloat16)

    inner_second = full_second[:, 1:-1, 1:-1]
    grad_active = add_rims(inner_second, back_rims(got_second, theirs, back, inner_second))
    _, pull_gelu = jax.vjp(gelu_tanh, hidden)
    grad_hidden = pull_gelu(grad_active)[0].astype(jnp.bfloat16)
    local_first = weight_grad(padded_in, grad_hidden)
    full_first = conv_full(grad_hidden, weight_first)
    push_first = push_payloads(full_first, mine, resid)
    got_act, got_first = trip(pull_payloads(active, theirs, back), push_first)

    padded_act = pad_tile(active, got_act, mine, position)
    local_second = weight_grad(padded_act, cot_tile)
    inner_first = full_first[:, 1:-1, 1:-1]
    grad_tile = add_rims(inner_first, back_rims(got_first, theirs, back, inner_first))
    grad_tile = grad_tile.astype(jnp.bfloat16)

    flat = jnp.concatenate([local_first.reshape(-1), local_second.reshape(-1)])
    summed = all_reduce(flat, ("dp", "space"))
    half = local_first.size
    summed_first = summed[:half].reshape(local_first.shape)
    summed_second = summed[half:].reshape(local_second.shape)
    return (grad_tile[None], summed_first * scale, summed_second * scale)


def solution(mesh):
    in_specs = (
        P("space", "dp", None, None, None),
        P("space", "dp", None, None, None),
        P(),
        P(),
        P(),
        P(),
        P(),
        P(),
    )
    out_specs = (P("space", "dp", None, None, None), P(), P())
    return jax.shard_map(shards, mesh=mesh, in_specs=in_specs, out_specs=out_specs, check_vma=False)
```

```python
import math

import jax
import jax.numpy as jnp
import numpy as np
from jax import lax
from jax.sharding import PartitionSpec as P

REACH = 7

NEED_SIDE = (1, 0, 3, 2, 1, 1, 0, 0)


def side_tables():
    one = ((3, 0), (2, 0), (0, 1), (1, 1))
    side = np.zeros((4, 4), np.int32)
    flip = np.zeros((4, 4), np.int32)
    side[0] = np.arange(4)
    for r in range(1, 4):
        for s in range(4):
            s1, f1 = one[s]
            side[r, s] = side[r - 1, s1]
            flip[r, s] = flip[r - 1, s1] ^ f1
    return side, flip


def edge_rims(tile):
    return jnp.stack([tile[:, 0], tile[:, -1], tile[:, :, 0], tile[:, :, -1]])


def residues(devices):
    found = []
    for offset in range(-REACH, REACH + 1):
        res = offset % devices
        if res != 0 and res not in found:
            found.append(res)
    return found


def shift(value, by):
    length = lax.axis_size("space")
    return lax.ppermute(value, "space", [(i, (i + by) % length) for i in range(length)])


def swap_all(payload):
    return lax.all_to_all(payload, "space", 0, 0)


def round_trip(pull, push, offs):
    devices = lax.axis_size("space")
    index = {o: i + 1 for i, o in enumerate(offs)}
    rows = pull.shape[1]
    got_pull = [pull[0]]
    got_push = [push[0]]
    for o in offs:
        back = index[(devices - o) % devices]
        payload = jnp.concatenate([pull[back].astype(jnp.float32), push[back]])
        arrived = lax.ppermute(payload, "space", [(i, (i - o) % devices) for i in range(devices)])
        got_pull.append(arrived[:rows].astype(pull.dtype))
        got_push.append(arrived[rows:])
    return jnp.stack(got_pull), jnp.stack(got_push)


def make_plans(tables, devices):
    slot_tile, slot_of_tile, neighbour_tile, neighbour_turns, corner_live = tables
    slots = jnp.arange(devices, dtype=jnp.int32)
    owners = slot_of_tile[neighbour_tile[slot_tile]]
    res = (owners - slots[:, None]) % devices
    turns = neighbour_turns[slot_tile]
    side_tab, flip_tab = side_tables()
    need = np.array(NEED_SIDE, np.int32)[None, :]
    sides = jnp.asarray(side_tab)[turns, need]
    flips = jnp.asarray(flip_tab)[turns, need]
    edge = res[:, :4]
    earlier = np.tril(np.ones((4, 4), bool), -1)
    rank = jnp.sum((edge[:, :, None] == edge[:, None, :]) & earlier, axis=2)
    return res, rank, sides, flips, corner_live[slot_tile]


def flip_index(flips, size):
    cells = jnp.arange(size, dtype=jnp.int32)[None, :]
    return jnp.where(flips[:, None] == 1, size - 1 - cells, cells)


def assemble(own, top, bottom, left, right, top_left, top_right, bottom_left, bottom_right):
    top_row = jnp.concatenate([top_left[:, None], top, top_right[:, None]], axis=1)
    bottom_row = jnp.concatenate([bottom_left[:, None], bottom, bottom_right[:, None]], axis=1)
    middle = jnp.concatenate([left[:, :, None], own, right[:, :, None]], axis=2)
    return jnp.concatenate([top_row[:, None], middle, bottom_row[:, None]], axis=1)


def corner_at(flips, size):
    ends = np.array([size - 1, 0, size - 1, 0], np.int32)
    return jnp.where(flips == 1, size - 1 - ends, ends)


def to_rows(flat, like):
    size = like.shape[1]
    return flat.reshape((-1, size) + like.shape[:1] + like.shape[3:]).transpose(0, 2, 1, 3)


def from_rows(rims):
    return rims.transpose(0, 2, 1, 3).reshape(rims.shape[0] * rims.shape[2], -1)


def pull_payloads(tile, theirs, back):
    res, rank, sides, flips, live = theirs
    size = tile.shape[1]
    hit = res == back[:, None]
    q = jnp.arange(2)[None, :, None, None]
    s = jnp.arange(4)[None, None, :, None]
    edge = jnp.sum(
        hit[:, None, None, :4] & (rank[:, None, None, :] == q) & (sides[:, None, None, :4] == s), axis=3
    )
    eye = jnp.eye(size, dtype=jnp.bool_)
    edge = (edge[:, :, None, :, None] > 0) & eye[None, None, :, None, :]
    at = corner_at(flips[:, 4:], size)
    corner = (
        hit[:, 4:, None, None]
        & (sides[:, 4:, None, None] == jnp.arange(4)[None, None, :, None])
        & (jnp.arange(size)[None, None, None, :] == at[:, :, None, None])
    )
    count = res.shape[0]
    pick = jnp.concatenate([edge.reshape(count, 2 * size, 4 * size), corner.reshape(count, 4, 4 * size)], axis=1)
    rims = from_rows(edge_rims(tile))
    out = jnp.einsum("twx,xc->twc", pick.astype(tile.dtype), rims, preferred_element_type=jnp.float32)
    return out.astype(tile.dtype)


def pad_tile(tile, received, mine, position):
    res, rank, sides, flips, live = mine
    size = tile.shape[1]
    n_src, width = received.shape[0], received.shape[1]
    src = jnp.asarray(position)[res]
    cells = flip_index(flips[:4], size)
    column = rank[:, None] * size + cells
    edge = (jnp.arange(n_src)[None, None, :, None] == src[:4, None, None, None]) & (
        jnp.arange(width)[None, None, None, :] == column[:, :, None, None]
    )
    corner = (jnp.arange(n_src)[None, :, None] == src[4:, None, None]) & (
        jnp.arange(width)[None, None, :] == (2 * size + jnp.arange(4))[:, None, None]
    )
    pick = jnp.concatenate([edge.reshape(4 * size, n_src * width), corner.reshape(4, n_src * width)])
    flat = jnp.dot(pick.astype(tile.dtype), received.reshape(n_src * width, -1), preferred_element_type=jnp.float32)
    flat = flat.astype(tile.dtype)
    rows = to_rows(flat[: 4 * size], tile)
    corners = flat[4 * size :].reshape((4,) + tile.shape[:1] + tile.shape[3:])
    corners = corners * live.astype(tile.dtype)[:, None, None]
    return assemble(tile, rows[0], rows[1], rows[2], rows[3], corners[0], corners[1], corners[2], corners[3])


def conv_valid(padded, weight):
    return lax.conv_general_dilated(
        padded,
        weight,
        (1, 1),
        "VALID",
        dimension_numbers=("NHWC", "HWIO", "NHWC"),
        preferred_element_type=jnp.float32,
    )


def conv_full(cot, weight):
    flipped = jnp.flip(weight, (0, 1)).transpose(0, 1, 3, 2)
    return lax.conv_general_dilated(
        cot,
        flipped,
        (1, 1),
        ((2, 2), (2, 2)),
        dimension_numbers=("NHWC", "HWIO", "NHWC"),
        preferred_element_type=jnp.float32,
    )


def weight_grad(padded, cot):
    return lax.conv_general_dilated(
        padded,
        cot,
        (1, 1),
        "VALID",
        dimension_numbers=("CHWN", "IHWO", "HWNC"),
        preferred_element_type=jnp.float32,
    )


def push_payloads(full, mine, resid):
    res, rank, sides, flips, live = mine
    size = full.shape[1] - 2
    rows = jnp.stack([full[:, 0, 1:-1], full[:, -1, 1:-1], full[:, 1:-1, 0], full[:, 1:-1, -1]])
    values = jnp.stack([full[:, 0, 0], full[:, 0, -1], full[:, -1, 0], full[:, -1, -1]])
    values = values * live.astype(jnp.float32)[:, None, None]
    source = jnp.concatenate([from_rows(rows), values.reshape(4, -1)])
    hit = res[None, :] == jnp.asarray(resid)[:, None]
    count = resid.shape[0]
    edge = hit[:, None, :4] & (rank[None, None, :] == jnp.arange(2)[None, :, None])
    eye = jnp.eye(size, dtype=jnp.bool_)
    edge = edge[:, :, None, :, None] & eye[None, None, :, None, :]
    edge = jnp.concatenate(
        [edge.reshape(count, 2 * size, 4 * size), jnp.zeros((count, 2 * size, 4), jnp.bool_)], axis=2
    )
    corner = hit[:, 4:, None] & jnp.eye(4, dtype=jnp.bool_)[None]
    corner = jnp.concatenate([jnp.zeros((count, 4, 4 * size), jnp.bool_), corner], axis=2)
    route = jnp.concatenate([edge, corner], axis=1).astype(jnp.float32)
    return jnp.einsum(
        "twx,xc->twc", route, source, precision=lax.Precision.HIGHEST, preferred_element_type=jnp.float32
    )


def back_rims(received, theirs, back, like):
    res, rank, sides, flips, live = theirs
    size = like.shape[1]
    n_src, width = received.shape[0], received.shape[1]
    hit = res == back[:, None]
    s = jnp.arange(4)[:, None, None, None, None]
    j = jnp.arange(size)[None, :, None, None, None]
    q = (jnp.arange(width) // size)[None, None, None, :, None]
    jj = (jnp.arange(width) % size)[None, None, None, :, None]
    in_edge = (jnp.arange(width) < 2 * size)[None, None, None, :, None]
    e_hit = hit[None, None, :, None, :4]
    e_side = sides[None, None, :, None, :4] == s
    e_rank = rank[None, None, :, None, :] == q
    e_cell = jnp.where(flips[None, None, :, None, :4] == 1, size - 1 - j, j) == jj
    edge = jnp.any(e_hit & e_side & e_rank & e_cell & in_edge, axis=4)
    at = corner_at(flips[:, 4:], size)
    c_slot = (jnp.arange(width) - 2 * size)[None, None, None, :, None] == jnp.arange(4)[None, None, None, None, :]
    c_hit = hit[None, None, :, None, 4:] & (sides[None, None, :, None, 4:] == s)
    c_cell = j == at[None, None, :, None, :]
    corner = jnp.any(c_hit & c_cell & c_slot, axis=4)
    route = (edge | corner).reshape(4 * size, n_src * width).astype(jnp.float32)
    flat = jnp.dot(
        route, received.reshape(n_src * width, -1), precision=lax.Precision.HIGHEST,
        preferred_element_type=jnp.float32,
    )
    return to_rows(flat, like)


def add_rims(inner, total):
    inner = inner.at[:, 0].add(total[0]).at[:, -1].add(total[1])
    return inner.at[:, :, 0].add(total[2]).at[:, :, -1].add(total[3])


def xor_swap(value, axis, bit):
    size = lax.axis_size(axis)
    return lax.ppermute(value, axis, [(i, i ^ bit) for i in range(size)])


def all_reduce(flat, axes):
    stages = []
    for axis in axes:
        size = lax.axis_size(axis)
        if size & (size - 1):
            return lax.psum(flat, axes)
        bit = 1
        while bit < size:
            stages.append((axis, bit))
            bit *= 2
    if flat.shape[0] % (1 << len(stages)):
        return lax.psum(flat, axes)
    buf = flat
    for axis, bit in stages:
        half = buf.shape[0] // 2
        high = (lax.axis_index(axis) & bit) != 0
        low_part, high_part = buf[:half], buf[half:]
        send = jnp.where(high, low_part, high_part)
        keep = jnp.where(high, high_part, low_part)
        buf = keep + xor_swap(send, axis, bit)
    for axis, bit in reversed(stages):
        high = (lax.axis_index(axis) & bit) != 0
        other = xor_swap(buf, axis, bit)
        buf = jnp.where(high, jnp.concatenate([other, buf]), jnp.concatenate([buf, other]))
    return buf


def gelu_tanh(value):
    return jax.nn.gelu(value, approximate=True)


def shards(
    inputs,
    cotangent,
    weight_first,
    weight_second,
    slot_tile,
    neighbour_tile,
    neighbour_turns,
    corner_live,
):
    count = slot_tile.shape[0]
    devices = lax.axis_size("space")
    me = lax.axis_index("space")
    offs = residues(devices)
    slot_of_tile = (
        jnp.zeros((count,), jnp.int32).at[slot_tile].set(jnp.arange(count, dtype=jnp.int32))
    )
    tables = (slot_tile, slot_of_tile, neighbour_tile, neighbour_turns, corner_live)
    plans = make_plans(tables, devices)
    if devices <= 2 * REACH + 1:
        offs = None
        every = jnp.arange(devices, dtype=jnp.int32)
        resid = (every - me) % devices
        position = (every + me) % devices
        back = (me - every) % devices
        theirs = plans
    else:
        resid = np.array([0] + offs, np.int32)
        position = np.zeros((devices,), np.int32)
        position[resid] = np.arange(len(resid))
        back = jnp.asarray((-resid) % devices)
        theirs = tuple(p[(me + resid) % devices] for p in plans)
    mine = tuple(p[me] for p in plans)
    tile = inputs[0]
    cot_tile = cotangent[0]
    samples_all = tile.shape[0] * lax.axis_size("dp") * devices
    scale = 1.0 / math.sqrt(samples_all * tile.shape[1] * tile.shape[2])

    full_second = conv_full(cot_tile, weight_second)
    pull_in = pull_payloads(tile, theirs, back)
    if offs is None:
        got_in = swap_all(pull_in)
        push_second = push_payloads(full_second, mine, resid)
        got_second = swap_all(push_second)
    else:
        push_second = push_payloads(full_second, mine, resid)
        got_in, got_second = round_trip(pull_in, push_second, offs)

    padded_in = pad_tile(tile, got_in, mine, position)
    hidden = conv_valid(padded_in, weight_first)
    active = gelu_tanh(hidden).astype(jnp.bfloat16)
    pull_act = pull_payloads(active, theirs, back)
    if offs is None:
        got_act = swap_all(pull_act)

    inner_second = full_second[:, 1:-1, 1:-1]
    grad_active = add_rims(inner_second, back_rims(got_second, theirs, back, inner_second))
    _, pull_gelu = jax.vjp(gelu_tanh, hidden)
    grad_hidden = pull_gelu(grad_active)[0].astype(jnp.bfloat16)
    local_first = weight_grad(padded_in, grad_hidden)
    full_first = conv_full(grad_hidden, weight_first)
    push_first = push_payloads(full_first, mine, resid)
    if offs is None:
        got_first = swap_all(push_first)
    else:
        got_act, got_first = round_trip(pull_act, push_first, offs)

    padded_act = pad_tile(active, got_act, mine, position)
    local_second = weight_grad(padded_act, cot_tile)
    inner_first = full_first[:, 1:-1, 1:-1]
    grad_tile = add_rims(inner_first, back_rims(got_first, theirs, back, inner_first))
    grad_tile = grad_tile.astype(jnp.bfloat16)

    flat = jnp.concatenate([local_first.reshape(-1), local_second.reshape(-1)])
    summed = all_reduce(flat, ("dp", "space"))
    half = local_first.size
    summed_first = summed[:half].reshape(local_first.shape)
    summed_second = summed[half:].reshape(local_second.shape)
    return (grad_tile[None], summed_first * scale, summed_second * scale)


def solution(mesh):
    in_specs = (
        P("space", "dp", None, None, None),
        P("space", "dp", None, None, None),
        P(),
        P(),
        P(),
        P(),
        P(),
        P(),
    )
    out_specs = (P("space", "dp", None, None, None), P(), P())
    return jax.shard_map(shards, mesh=mesh, in_specs=in_specs, out_specs=out_specs, check_vma=False)
```

```python
import math

import jax
import jax.numpy as jnp
import numpy as np
from jax import lax
from jax.sharding import PartitionSpec as P

REACH = 7

NEED_SIDE = (1, 0, 3, 2, 1, 1, 0, 0)


def side_tables():
    one = ((3, 0), (2, 0), (0, 1), (1, 1))
    side = np.zeros((4, 4), np.int32)
    flip = np.zeros((4, 4), np.int32)
    side[0] = np.arange(4)
    for r in range(1, 4):
        for s in range(4):
            s1, f1 = one[s]
            side[r, s] = side[r - 1, s1]
            flip[r, s] = flip[r - 1, s1] ^ f1
    return side, flip


def edge_rims(tile):
    return jnp.stack([tile[:, 0], tile[:, -1], tile[:, :, 0], tile[:, :, -1]])


def residues(devices):
    found = []
    for offset in range(-REACH, REACH + 1):
        res = offset % devices
        if res != 0 and res not in found:
            found.append(res)
    return found


def shift(value, by):
    length = lax.axis_size("space")
    return lax.ppermute(value, "space", [(i, (i + by) % length) for i in range(length)])


def swap_all(pull, push):
    payload = jnp.concatenate([pull.astype(jnp.float32), push], axis=1)
    return lax.all_to_all(payload, "space", 0, 0)


def round_trip(pull, push, offs):
    devices = lax.axis_size("space")
    index = {o: i + 1 for i, o in enumerate(offs)}
    rows = pull.shape[1]
    got_pull = [pull[0]]
    got_push = [push[0]]
    for o in offs:
        back = index[(devices - o) % devices]
        payload = jnp.concatenate([pull[back].astype(jnp.float32), push[back]])
        arrived = lax.ppermute(payload, "space", [(i, (i - o) % devices) for i in range(devices)])
        got_pull.append(arrived[:rows].astype(pull.dtype))
        got_push.append(arrived[rows:])
    return jnp.stack(got_pull), jnp.stack(got_push)


def make_plans(tables, devices):
    slot_tile, slot_of_tile, neighbour_tile, neighbour_turns, corner_live = tables
    slots = jnp.arange(devices, dtype=jnp.int32)
    owners = slot_of_tile[neighbour_tile[slot_tile]]
    res = (owners - slots[:, None]) % devices
    turns = neighbour_turns[slot_tile]
    side_tab, flip_tab = side_tables()
    need = np.array(NEED_SIDE, np.int32)[None, :]
    sides = jnp.asarray(side_tab)[turns, need]
    flips = jnp.asarray(flip_tab)[turns, need]
    edge = res[:, :4]
    earlier = np.tril(np.ones((4, 4), bool), -1)
    rank = jnp.sum((edge[:, :, None] == edge[:, None, :]) & earlier, axis=2)
    return res, rank, sides, flips, corner_live[slot_tile]


def flip_index(flips, size):
    cells = jnp.arange(size, dtype=jnp.int32)[None, :]
    return jnp.where(flips[:, None] == 1, size - 1 - cells, cells)


def assemble(own, top, bottom, left, right, top_left, top_right, bottom_left, bottom_right):
    top_row = jnp.concatenate([top_left[:, None], top, top_right[:, None]], axis=1)
    bottom_row = jnp.concatenate([bottom_left[:, None], bottom, bottom_right[:, None]], axis=1)
    middle = jnp.concatenate([left[:, :, None], own, right[:, :, None]], axis=2)
    return jnp.concatenate([top_row[:, None], middle, bottom_row[:, None]], axis=1)


def corner_at(flips, size):
    ends = np.array([size - 1, 0, size - 1, 0], np.int32)
    return jnp.where(flips == 1, size - 1 - ends, ends)


def to_rows(flat, like):
    size = like.shape[1]
    return flat.reshape((-1, size) + like.shape[:1] + like.shape[3:]).transpose(0, 2, 1, 3)


def from_rows(rims):
    return rims.transpose(0, 2, 1, 3).reshape(rims.shape[0] * rims.shape[2], -1)


def pull_payloads(tile, theirs, back):
    res, rank, sides, flips, live = theirs
    size = tile.shape[1]
    hit = res == back[:, None]
    q = jnp.arange(2)[None, :, None, None]
    s = jnp.arange(4)[None, None, :, None]
    edge = jnp.sum(
        hit[:, None, None, :4] & (rank[:, None, None, :] == q) & (sides[:, None, None, :4] == s), axis=3
    )
    eye = jnp.eye(size, dtype=jnp.bool_)
    edge = (edge[:, :, None, :, None] > 0) & eye[None, None, :, None, :]
    at = corner_at(flips[:, 4:], size)
    corner = (
        hit[:, 4:, None, None]
        & (sides[:, 4:, None, None] == jnp.arange(4)[None, None, :, None])
        & (jnp.arange(size)[None, None, None, :] == at[:, :, None, None])
    )
    count = res.shape[0]
    pick = jnp.concatenate([edge.reshape(count, 2 * size, 4 * size), corner.reshape(count, 4, 4 * size)], axis=1)
    rims = from_rows(edge_rims(tile))
    out = jnp.einsum("twx,xc->twc", pick.astype(tile.dtype), rims, preferred_element_type=jnp.float32)
    return out.astype(tile.dtype)


def pad_tile(tile, received, mine, position):
    res, rank, sides, flips, live = mine
    size = tile.shape[1]
    n_src, width = received.shape[0], received.shape[1]
    src = jnp.asarray(position)[res]
    cells = flip_index(flips[:4], size)
    column = rank[:, None] * size + cells
    edge = (jnp.arange(n_src)[None, None, :, None] == src[:4, None, None, None]) & (
        jnp.arange(width)[None, None, None, :] == column[:, :, None, None]
    )
    corner = (jnp.arange(n_src)[None, :, None] == src[4:, None, None]) & (
        jnp.arange(width)[None, None, :] == (2 * size + jnp.arange(4))[:, None, None]
    )
    pick = jnp.concatenate([edge.reshape(4 * size, n_src * width), corner.reshape(4, n_src * width)])
    flat = jnp.dot(
        pick.astype(received.dtype), received.reshape(n_src * width, -1), precision=lax.Precision.HIGHEST,
        preferred_element_type=jnp.float32,
    )
    flat = flat.astype(tile.dtype)
    rows = to_rows(flat[: 4 * size], tile)
    corners = flat[4 * size :].reshape((4,) + tile.shape[:1] + tile.shape[3:])
    corners = corners * live.astype(tile.dtype)[:, None, None]
    return assemble(tile, rows[0], rows[1], rows[2], rows[3], corners[0], corners[1], corners[2], corners[3])


def conv_valid(padded, weight):
    return lax.conv_general_dilated(
        padded,
        weight,
        (1, 1),
        "VALID",
        dimension_numbers=("NHWC", "HWIO", "NHWC"),
        preferred_element_type=jnp.float32,
    )


def conv_full(cot, weight):
    flipped = jnp.flip(weight, (0, 1)).transpose(0, 1, 3, 2)
    return lax.conv_general_dilated(
        cot,
        flipped,
        (1, 1),
        ((2, 2), (2, 2)),
        dimension_numbers=("NHWC", "HWIO", "NHWC"),
        preferred_element_type=jnp.float32,
    )


def weight_grad(padded, cot):
    return lax.conv_general_dilated(
        padded,
        cot,
        (1, 1),
        "VALID",
        dimension_numbers=("CHWN", "IHWO", "HWNC"),
        preferred_element_type=jnp.float32,
    )


def push_payloads(full, mine, resid):
    res, rank, sides, flips, live = mine
    size = full.shape[1] - 2
    rows = jnp.stack([full[:, 0, 1:-1], full[:, -1, 1:-1], full[:, 1:-1, 0], full[:, 1:-1, -1]])
    values = jnp.stack([full[:, 0, 0], full[:, 0, -1], full[:, -1, 0], full[:, -1, -1]])
    values = values * live.astype(jnp.float32)[:, None, None]
    source = jnp.concatenate([from_rows(rows), values.reshape(4, -1)])
    hit = res[None, :] == jnp.asarray(resid)[:, None]
    count = resid.shape[0]
    edge = hit[:, None, :4] & (rank[None, None, :] == jnp.arange(2)[None, :, None])
    eye = jnp.eye(size, dtype=jnp.bool_)
    edge = edge[:, :, None, :, None] & eye[None, None, :, None, :]
    edge = jnp.concatenate(
        [edge.reshape(count, 2 * size, 4 * size), jnp.zeros((count, 2 * size, 4), jnp.bool_)], axis=2
    )
    corner = hit[:, 4:, None] & jnp.eye(4, dtype=jnp.bool_)[None]
    corner = jnp.concatenate([jnp.zeros((count, 4, 4 * size), jnp.bool_), corner], axis=2)
    route = jnp.concatenate([edge, corner], axis=1).astype(jnp.float32)
    return jnp.einsum(
        "twx,xc->twc", route, source, precision=lax.Precision.HIGHEST, preferred_element_type=jnp.float32
    )


def back_rims(received, theirs, back, like, offset):
    res, rank, sides, flips, live = theirs
    size = like.shape[1]
    n_src, width = received.shape[0], received.shape[1]
    hit = res == back[:, None]
    s = jnp.arange(4)[:, None, None, None, None]
    j = jnp.arange(size)[None, :, None, None, None]
    cols = jnp.arange(width) - offset
    q = (cols // size)[None, None, None, :, None]
    jj = (cols % size)[None, None, None, :, None]
    in_edge = ((cols >= 0) & (cols < 2 * size))[None, None, None, :, None]
    e_hit = hit[None, None, :, None, :4]
    e_side = sides[None, None, :, None, :4] == s
    e_rank = rank[None, None, :, None, :] == q
    e_cell = jnp.where(flips[None, None, :, None, :4] == 1, size - 1 - j, j) == jj
    edge = jnp.any(e_hit & e_side & e_rank & e_cell & in_edge, axis=4)
    at = corner_at(flips[:, 4:], size)
    c_slot = (cols - 2 * size)[None, None, None, :, None] == jnp.arange(4)[None, None, None, None, :]
    c_hit = hit[None, None, :, None, 4:] & (sides[None, None, :, None, 4:] == s)
    c_cell = j == at[None, None, :, None, :]
    corner = jnp.any(c_hit & c_cell & c_slot, axis=4)
    route = (edge | corner).reshape(4 * size, n_src * width).astype(jnp.float32)
    flat = jnp.dot(
        route, received.reshape(n_src * width, -1), precision=lax.Precision.HIGHEST,
        preferred_element_type=jnp.float32,
    )
    return to_rows(flat, like)


def add_rims(inner, total):
    inner = inner.at[:, 0].add(total[0]).at[:, -1].add(total[1])
    return inner.at[:, :, 0].add(total[2]).at[:, :, -1].add(total[3])


def xor_swap(value, axis, bit):
    size = lax.axis_size(axis)
    return lax.ppermute(value, axis, [(i, i ^ bit) for i in range(size)])


def all_reduce(flat, axes):
    stages = []
    for axis in axes:
        size = lax.axis_size(axis)
        if size & (size - 1):
            return lax.psum(flat, axes)
        bit = 1
        while bit < size:
            stages.append((axis, bit))
            bit *= 2
    if flat.shape[0] % (1 << len(stages)):
        return lax.psum(flat, axes)
    buf = flat
    for axis, bit in stages:
        half = buf.shape[0] // 2
        high = (lax.axis_index(axis) & bit) != 0
        low_part, high_part = buf[:half], buf[half:]
        send = jnp.where(high, low_part, high_part)
        keep = jnp.where(high, high_part, low_part)
        buf = keep + xor_swap(send, axis, bit)
    for axis, bit in reversed(stages):
        high = (lax.axis_index(axis) & bit) != 0
        other = xor_swap(buf, axis, bit)
        buf = jnp.where(high, jnp.concatenate([other, buf]), jnp.concatenate([buf, other]))
    return buf


def gelu_tanh(value):
    return jax.nn.gelu(value, approximate=True)


def shards(
    inputs,
    cotangent,
    weight_first,
    weight_second,
    slot_tile,
    neighbour_tile,
    neighbour_turns,
    corner_live,
):
    count = slot_tile.shape[0]
    devices = lax.axis_size("space")
    me = lax.axis_index("space")
    offs = residues(devices)
    slot_of_tile = (
        jnp.zeros((count,), jnp.int32).at[slot_tile].set(jnp.arange(count, dtype=jnp.int32))
    )
    tables = (slot_tile, slot_of_tile, neighbour_tile, neighbour_turns, corner_live)
    plans = make_plans(tables, devices)
    if devices <= 2 * REACH + 1:
        offs = None
        every = jnp.arange(devices, dtype=jnp.int32)
        resid = (every - me) % devices
        position = (every + me) % devices
        back = (me - every) % devices
        theirs = plans
    else:
        resid = np.array([0] + offs, np.int32)
        position = np.zeros((devices,), np.int32)
        position[resid] = np.arange(len(resid))
        back = jnp.asarray((-resid) % devices)
        theirs = tuple(p[(me + resid) % devices] for p in plans)
    mine = tuple(p[me] for p in plans)

    def trip(pull, push):
        if offs is None:
            arrived = swap_all(pull, push)
            return arrived, arrived, pull.shape[1]
        got_pull, got_push = round_trip(pull, push, offs)
        return got_pull, got_push, 0

    tile = inputs[0]
    cot_tile = cotangent[0]
    samples_all = tile.shape[0] * lax.axis_size("dp") * devices
    scale = 1.0 / math.sqrt(samples_all * tile.shape[1] * tile.shape[2])

    full_second = conv_full(cot_tile, weight_second)
    push_second = push_payloads(full_second, mine, resid)
    got_in, got_second, skip = trip(pull_payloads(tile, theirs, back), push_second)

    padded_in = pad_tile(tile, got_in, mine, position)
    hidden = conv_valid(padded_in, weight_first)
    active = gelu_tanh(hidden).astype(jnp.bfloat16)

    inner_second = full_second[:, 1:-1, 1:-1]
    grad_active = add_rims(inner_second, back_rims(got_second, theirs, back, inner_second, skip))
    _, pull_gelu = jax.vjp(gelu_tanh, hidden)
    grad_hidden = pull_gelu(grad_active)[0].astype(jnp.bfloat16)
    local_first = weight_grad(padded_in, grad_hidden)
    full_first = conv_full(grad_hidden, weight_first)
    push_first = push_payloads(full_first, mine, resid)
    got_act, got_first, skip = trip(pull_payloads(active, theirs, back), push_first)

    padded_act = pad_tile(active, got_act, mine, position)
    local_second = weight_grad(padded_act, cot_tile)
    inner_first = full_first[:, 1:-1, 1:-1]
    grad_tile = add_rims(inner_first, back_rims(got_first, theirs, back, inner_first, skip))
    grad_tile = grad_tile.astype(jnp.bfloat16)

    flat = jnp.concatenate([local_first.reshape(-1), local_second.reshape(-1)])
    summed = all_reduce(flat, ("dp", "space"))
    half = local_first.size
    summed_first = summed[:half].reshape(local_first.shape)
    summed_second = summed[half:].reshape(local_second.shape)
    return (grad_tile[None], summed_first * scale, summed_second * scale)


def solution(mesh):
    in_specs = (
        P("space", "dp", None, None, None),
        P("space", "dp", None, None, None),
        P(),
        P(),
        P(),
        P(),
        P(),
        P(),
    )
    out_specs = (P("space", "dp", None, None, None), P(), P())
    return jax.shard_map(shards, mesh=mesh, in_specs=in_specs, out_specs=out_specs, check_vma=False)
```

```python
import math

import jax
import jax.numpy as jnp
import numpy as np
from jax import lax
from jax.sharding import PartitionSpec as P

REACH = 7

NEED_SIDE = (1, 0, 3, 2, 1, 1, 0, 0)


def side_tables():
    one = ((3, 0), (2, 0), (0, 1), (1, 1))
    side = np.zeros((4, 4), np.int32)
    flip = np.zeros((4, 4), np.int32)
    side[0] = np.arange(4)
    for r in range(1, 4):
        for s in range(4):
            s1, f1 = one[s]
            side[r, s] = side[r - 1, s1]
            flip[r, s] = flip[r - 1, s1] ^ f1
    return side, flip


def edge_rims(tile):
    return jnp.stack([tile[:, 0], tile[:, -1], tile[:, :, 0], tile[:, :, -1]])


def residues(devices):
    found = []
    for offset in range(-REACH, REACH + 1):
        res = offset % devices
        if res != 0 and res not in found:
            found.append(res)
    return found


def shift(value, by):
    length = lax.axis_size("space")
    return lax.ppermute(value, "space", [(i, (i + by) % length) for i in range(length)])


def swap_all(pull, push):
    payload = jnp.concatenate([pull.astype(jnp.float32), push], axis=1)
    return lax.all_to_all(payload, "space", 0, 0)


def round_trip(pull, push, offs):
    devices = lax.axis_size("space")
    index = {o: i + 1 for i, o in enumerate(offs)}
    rows = pull.shape[1]
    got_pull = [pull[0]]
    got_push = [push[0]]
    for o in offs:
        back = index[(devices - o) % devices]
        payload = jnp.concatenate([pull[back].astype(jnp.float32), push[back]])
        arrived = lax.ppermute(payload, "space", [(i, (i - o) % devices) for i in range(devices)])
        got_pull.append(arrived[:rows].astype(pull.dtype))
        got_push.append(arrived[rows:])
    return jnp.stack(got_pull), jnp.stack(got_push)


def make_plans(tables, devices):
    slot_tile, slot_of_tile, neighbour_tile, neighbour_turns, corner_live = tables
    slots = jnp.arange(devices, dtype=jnp.int32)
    owners = slot_of_tile[neighbour_tile[slot_tile]]
    res = (owners - slots[:, None]) % devices
    turns = neighbour_turns[slot_tile]
    side_tab, flip_tab = side_tables()
    need = np.array(NEED_SIDE, np.int32)[None, :]
    sides = jnp.asarray(side_tab)[turns, need]
    flips = jnp.asarray(flip_tab)[turns, need]
    edge = res[:, :4]
    earlier = np.tril(np.ones((4, 4), bool), -1)
    rank = jnp.sum((edge[:, :, None] == edge[:, None, :]) & earlier, axis=2)
    return res, rank, sides, flips, corner_live[slot_tile]


def flip_index(flips, size):
    cells = jnp.arange(size, dtype=jnp.int32)[None, :]
    return jnp.where(flips[:, None] == 1, size - 1 - cells, cells)


def assemble(own, top, bottom, left, right, top_left, top_right, bottom_left, bottom_right):
    top_row = jnp.concatenate([top_left[:, None], top, top_right[:, None]], axis=1)
    bottom_row = jnp.concatenate([bottom_left[:, None], bottom, bottom_right[:, None]], axis=1)
    middle = jnp.concatenate([left[:, :, None], own, right[:, :, None]], axis=2)
    return jnp.concatenate([top_row[:, None], middle, bottom_row[:, None]], axis=1)


def corner_at(flips, size):
    ends = np.array([size - 1, 0, size - 1, 0], np.int32)
    return jnp.where(flips == 1, size - 1 - ends, ends)


def to_rows(flat, like):
    size = like.shape[1]
    return flat.reshape((-1, size) + like.shape[:1] + like.shape[3:]).transpose(0, 2, 1, 3)


def from_rows(rims):
    return rims.transpose(0, 2, 1, 3).reshape(rims.shape[0] * rims.shape[2], -1)


def pull_payloads(tile, theirs, back):
    res, rank, sides, flips, live = theirs
    size = tile.shape[1]
    hit = res == back[:, None]
    q = jnp.arange(2)[None, :, None, None]
    s = jnp.arange(4)[None, None, :, None]
    edge = jnp.sum(
        hit[:, None, None, :4] & (rank[:, None, None, :] == q) & (sides[:, None, None, :4] == s), axis=3
    )
    eye = jnp.eye(size, dtype=jnp.bool_)
    edge = (edge[:, :, None, :, None] > 0) & eye[None, None, :, None, :]
    at = corner_at(flips[:, 4:], size)
    corner = (
        hit[:, 4:, None, None]
        & (sides[:, 4:, None, None] == jnp.arange(4)[None, None, :, None])
        & (jnp.arange(size)[None, None, None, :] == at[:, :, None, None])
    )
    count = res.shape[0]
    pick = jnp.concatenate([edge.reshape(count, 2 * size, 4 * size), corner.reshape(count, 4, 4 * size)], axis=1)
    rims = from_rows(edge_rims(tile))
    out = jnp.einsum("twx,xc->twc", pick.astype(tile.dtype), rims, preferred_element_type=jnp.float32)
    return out.astype(tile.dtype)


def pad_tile(tile, received, mine, position):
    res, rank, sides, flips, live = mine
    size = tile.shape[1]
    n_src, width = received.shape[0], received.shape[1]
    src = jnp.asarray(position)[res]
    cells = flip_index(flips[:4], size)
    column = rank[:, None] * size + cells
    edge = (jnp.arange(n_src)[None, None, :, None] == src[:4, None, None, None]) & (
        jnp.arange(width)[None, None, None, :] == column[:, :, None, None]
    )
    corner = (jnp.arange(n_src)[None, :, None] == src[4:, None, None]) & (
        jnp.arange(width)[None, None, :] == (2 * size + jnp.arange(4))[:, None, None]
    )
    pick = jnp.concatenate([edge.reshape(4 * size, n_src * width), corner.reshape(4, n_src * width)])
    flat = jnp.dot(
        pick.astype(received.dtype), received.reshape(n_src * width, -1), precision=lax.Precision.HIGHEST,
        preferred_element_type=jnp.float32,
    )
    flat = flat.astype(tile.dtype)
    rows = to_rows(flat[: 4 * size], tile)
    corners = flat[4 * size :].reshape((4,) + tile.shape[:1] + tile.shape[3:])
    corners = corners * live.astype(tile.dtype)[:, None, None]
    return assemble(tile, rows[0], rows[1], rows[2], rows[3], corners[0], corners[1], corners[2], corners[3])


def conv_valid(padded, weight):
    return lax.conv_general_dilated(
        padded,
        weight,
        (1, 1),
        "VALID",
        dimension_numbers=("NHWC", "HWIO", "NHWC"),
        preferred_element_type=jnp.float32,
    )


def conv_full(cot, weight):
    flipped = jnp.flip(weight, (0, 1)).transpose(0, 1, 3, 2)
    return lax.conv_general_dilated(
        cot,
        flipped,
        (1, 1),
        ((2, 2), (2, 2)),
        dimension_numbers=("NHWC", "HWIO", "NHWC"),
        preferred_element_type=jnp.float32,
    )


def weight_grad(padded, cot):
    return lax.conv_general_dilated(
        padded,
        cot,
        (1, 1),
        "VALID",
        dimension_numbers=("CHWN", "IHWO", "HWNC"),
        preferred_element_type=jnp.float32,
    )


def push_payloads(full, mine, resid):
    res, rank, sides, flips, live = mine
    size = full.shape[1] - 2
    rows = jnp.stack([full[:, 0, 1:-1], full[:, -1, 1:-1], full[:, 1:-1, 0], full[:, 1:-1, -1]])
    values = jnp.stack([full[:, 0, 0], full[:, 0, -1], full[:, -1, 0], full[:, -1, -1]])
    values = values * live.astype(jnp.float32)[:, None, None]
    source = jnp.concatenate([from_rows(rows), values.reshape(4, -1)])
    hit = res[None, :] == jnp.asarray(resid)[:, None]
    count = resid.shape[0]
    edge = hit[:, None, :4] & (rank[None, None, :] == jnp.arange(2)[None, :, None])
    eye = jnp.eye(size, dtype=jnp.bool_)
    edge = edge[:, :, None, :, None] & eye[None, None, :, None, :]
    edge = jnp.concatenate(
        [edge.reshape(count, 2 * size, 4 * size), jnp.zeros((count, 2 * size, 4), jnp.bool_)], axis=2
    )
    corner = hit[:, 4:, None] & jnp.eye(4, dtype=jnp.bool_)[None]
    corner = jnp.concatenate([jnp.zeros((count, 4, 4 * size), jnp.bool_), corner], axis=2)
    route = jnp.concatenate([edge, corner], axis=1).astype(jnp.float32)
    return jnp.einsum(
        "twx,xc->twc", route, source, precision=lax.Precision.HIGHEST, preferred_element_type=jnp.float32
    )


def back_rims(received, theirs, back, like, offset):
    res, rank, sides, flips, live = theirs
    size = like.shape[1]
    n_src, width = received.shape[0], received.shape[1]
    hit = res == back[:, None]
    s = jnp.arange(4)[:, None, None, None, None]
    j = jnp.arange(size)[None, :, None, None, None]
    cols = jnp.arange(width) - offset
    q = (cols // size)[None, None, None, :, None]
    jj = (cols % size)[None, None, None, :, None]
    in_edge = ((cols >= 0) & (cols < 2 * size))[None, None, None, :, None]
    e_hit = hit[None, None, :, None, :4]
    e_side = sides[None, None, :, None, :4] == s
    e_rank = rank[None, None, :, None, :] == q
    e_cell = jnp.where(flips[None, None, :, None, :4] == 1, size - 1 - j, j) == jj
    edge = jnp.any(e_hit & e_side & e_rank & e_cell & in_edge, axis=4)
    at = corner_at(flips[:, 4:], size)
    c_slot = (cols - 2 * size)[None, None, None, :, None] == jnp.arange(4)[None, None, None, None, :]
    c_hit = hit[None, None, :, None, 4:] & (sides[None, None, :, None, 4:] == s)
    c_cell = j == at[None, None, :, None, :]
    corner = jnp.any(c_hit & c_cell & c_slot, axis=4)
    route = (edge | corner).reshape(4 * size, n_src * width).astype(jnp.float32)
    flat = jnp.dot(
        route, received.reshape(n_src * width, -1), precision=lax.Precision.HIGHEST,
        preferred_element_type=jnp.float32,
    )
    return to_rows(flat, like)


def add_rims(inner, total):
    inner = inner.at[:, 0].add(total[0]).at[:, -1].add(total[1])
    return inner.at[:, :, 0].add(total[2]).at[:, :, -1].add(total[3])


def xor_swap(value, axis, bit):
    size = lax.axis_size(axis)
    return lax.ppermute(value, axis, [(i, i ^ bit) for i in range(size)])


def all_reduce(flat, axes):
    stages = []
    for axis in axes:
        size = lax.axis_size(axis)
        if size & (size - 1):
            return lax.psum(flat, axes)
        bit = 1
        while bit < size:
            stages.append((axis, bit))
            bit *= 2
    if flat.shape[0] % (1 << len(stages)):
        return lax.psum(flat, axes)
    buf = flat
    for axis, bit in stages:
        half = buf.shape[0] // 2
        high = (lax.axis_index(axis) & bit) != 0
        low_part, high_part = buf[:half], buf[half:]
        send = jnp.where(high, low_part, high_part)
        keep = jnp.where(high, high_part, low_part)
        buf = keep + xor_swap(send, axis, bit)
    for axis, bit in reversed(stages):
        high = (lax.axis_index(axis) & bit) != 0
        other = xor_swap(buf, axis, bit)
        buf = jnp.where(high, jnp.concatenate([other, buf]), jnp.concatenate([buf, other]))
    return buf


def gelu_tanh(value):
    return jax.nn.gelu(value, approximate=True)


def shards(
    inputs,
    cotangent,
    weight_first,
    weight_second,
    slot_tile,
    neighbour_tile,
    neighbour_turns,
    corner_live,
):
    count = slot_tile.shape[0]
    devices = lax.axis_size("space")
    me = lax.axis_index("space")
    offs = residues(devices)
    slot_of_tile = (
        jnp.zeros((count,), jnp.int32).at[slot_tile].set(jnp.arange(count, dtype=jnp.int32))
    )
    tables = (slot_tile, slot_of_tile, neighbour_tile, neighbour_turns, corner_live)
    plans = make_plans(tables, devices)
    if devices <= 2 * REACH + 1:
        offs = None
        every = jnp.arange(devices, dtype=jnp.int32)
        resid = (every - me) % devices
        position = (every + me) % devices
        back = (me - every) % devices
        theirs = plans
    else:
        resid = np.array([0] + offs, np.int32)
        position = np.zeros((devices,), np.int32)
        position[resid] = np.arange(len(resid))
        back = jnp.asarray((-resid) % devices)
        theirs = tuple(p[(me + resid) % devices] for p in plans)
    mine = tuple(p[me] for p in plans)

    def trip(pull, push):
        if offs is None:
            arrived = swap_all(pull, push)
            return arrived, arrived, pull.shape[1]
        got_pull, got_push = round_trip(pull, push, offs)
        return got_pull, got_push, 0

    tile = inputs[0]
    cot_tile = cotangent[0]
    samples_all = tile.shape[0] * lax.axis_size("dp") * devices
    scale = 1.0 / math.sqrt(samples_all * tile.shape[1] * tile.shape[2])

    full_second = conv_full(cot_tile, weight_second)
    push_second = push_payloads(full_second, mine, resid)
    got_in, got_second, skip = trip(pull_payloads(tile, theirs, back), push_second)

    padded_in = pad_tile(tile, got_in, mine, position)
    hidden = conv_valid(padded_in, weight_first)
    active = gelu_tanh(hidden).astype(jnp.bfloat16)

    inner_second = full_second[:, 1:-1, 1:-1]
    grad_active = add_rims(inner_second, back_rims(got_second, theirs, back, inner_second, skip))
    _, pull_gelu = jax.vjp(gelu_tanh, hidden)
    grad_hidden = pull_gelu(grad_active)[0].astype(jnp.bfloat16)
    full_first = conv_full(grad_hidden, weight_first)
    push_first = push_payloads(full_first, mine, resid)
    pull_act = pull_payloads(active, theirs, back)
    pull_act, push_first, padded_in, grad_hidden = lax.optimization_barrier(
        (pull_act, push_first, padded_in, grad_hidden)
    )
    got_act, got_first, skip = trip(pull_act, push_first)
    local_first = weight_grad(padded_in, grad_hidden)
    got_act, got_first, local_first = lax.optimization_barrier((got_act, got_first, local_first))

    padded_act = pad_tile(active, got_act, mine, position)
    local_second = weight_grad(padded_act, cot_tile)
    inner_first = full_first[:, 1:-1, 1:-1]
    grad_tile = add_rims(inner_first, back_rims(got_first, theirs, back, inner_first, skip))
    grad_tile = grad_tile.astype(jnp.bfloat16)

    flat = jnp.concatenate([local_first.reshape(-1), local_second.reshape(-1)])
    summed = all_reduce(flat, ("dp", "space"))
    half = local_first.size
    summed_first = summed[:half].reshape(local_first.shape)
    summed_second = summed[half:].reshape(local_second.shape)
    return (grad_tile[None], summed_first * scale, summed_second * scale)


def solution(mesh):
    in_specs = (
        P("space", "dp", None, None, None),
        P("space", "dp", None, None, None),
        P(),
        P(),
        P(),
        P(),
        P(),
        P(),
    )
    out_specs = (P("space", "dp", None, None, None), P(), P())
    return jax.shard_map(shards, mesh=mesh, in_specs=in_specs, out_specs=out_specs, check_vma=False)
```

```python
import math

import jax
import jax.numpy as jnp
import numpy as np
from jax import lax
from jax.sharding import PartitionSpec as P

REACH = 7

NEED_SIDE = (1, 0, 3, 2, 1, 1, 0, 0)


def side_tables():
    one = ((3, 0), (2, 0), (0, 1), (1, 1))
    side = np.zeros((4, 4), np.int32)
    flip = np.zeros((4, 4), np.int32)
    side[0] = np.arange(4)
    for r in range(1, 4):
        for s in range(4):
            s1, f1 = one[s]
            side[r, s] = side[r - 1, s1]
            flip[r, s] = flip[r - 1, s1] ^ f1
    return side, flip


def edge_rims(tile):
    return jnp.stack([tile[:, 0], tile[:, -1], tile[:, :, 0], tile[:, :, -1]])


def residues(devices):
    found = []
    for offset in range(-REACH, REACH + 1):
        res = offset % devices
        if res != 0 and res not in found:
            found.append(res)
    return found


def shift(value, by):
    length = lax.axis_size("space")
    return lax.ppermute(value, "space", [(i, (i + by) % length) for i in range(length)])


def swap_all(pull, push):
    payload = jnp.concatenate([pull.astype(jnp.float32), push], axis=1)
    return lax.all_to_all(payload, "space", 0, 0)


def round_trip(pull, push, offs):
    devices = lax.axis_size("space")
    index = {o: i + 1 for i, o in enumerate(offs)}
    rows = pull.shape[1]
    got_pull = [pull[0]]
    got_push = [push[0]]
    for o in offs:
        back = index[(devices - o) % devices]
        payload = jnp.concatenate([pull[back].astype(jnp.float32), push[back]])
        arrived = lax.ppermute(payload, "space", [(i, (i - o) % devices) for i in range(devices)])
        got_pull.append(arrived[:rows].astype(pull.dtype))
        got_push.append(arrived[rows:])
    return jnp.stack(got_pull), jnp.stack(got_push)


def make_plans(tables, devices):
    slot_tile, slot_of_tile, neighbour_tile, neighbour_turns, corner_live = tables
    slots = jnp.arange(devices, dtype=jnp.int32)
    owners = slot_of_tile[neighbour_tile[slot_tile]]
    res = (owners - slots[:, None]) % devices
    turns = neighbour_turns[slot_tile]
    side_tab, flip_tab = side_tables()
    need = np.array(NEED_SIDE, np.int32)[None, :]
    sides = jnp.asarray(side_tab)[turns, need]
    flips = jnp.asarray(flip_tab)[turns, need]
    edge = res[:, :4]
    earlier = np.tril(np.ones((4, 4), bool), -1)
    rank = jnp.sum((edge[:, :, None] == edge[:, None, :]) & earlier, axis=2)
    return res, rank, sides, flips, corner_live[slot_tile]


def flip_index(flips, size):
    cells = jnp.arange(size, dtype=jnp.int32)[None, :]
    return jnp.where(flips[:, None] == 1, size - 1 - cells, cells)


def assemble(own, top, bottom, left, right, top_left, top_right, bottom_left, bottom_right):
    top_row = jnp.concatenate([top_left[:, None], top, top_right[:, None]], axis=1)
    bottom_row = jnp.concatenate([bottom_left[:, None], bottom, bottom_right[:, None]], axis=1)
    middle = jnp.concatenate([left[:, :, None], own, right[:, :, None]], axis=2)
    return jnp.concatenate([top_row[:, None], middle, bottom_row[:, None]], axis=1)


def corner_at(flips, size):
    ends = np.array([size - 1, 0, size - 1, 0], np.int32)
    return jnp.where(flips == 1, size - 1 - ends, ends)


def to_rows(flat, like):
    size = like.shape[1]
    return flat.reshape((-1, size) + like.shape[:1] + like.shape[3:]).transpose(0, 2, 1, 3)


def from_rows(rims):
    return rims.transpose(0, 2, 1, 3).reshape(rims.shape[0] * rims.shape[2], -1)


def pull_payloads(tile, theirs, back):
    res, rank, sides, flips, live = theirs
    size = tile.shape[1]
    hit = res == back[:, None]
    q = jnp.arange(2)[None, :, None, None]
    s = jnp.arange(4)[None, None, :, None]
    edge = jnp.sum(
        hit[:, None, None, :4] & (rank[:, None, None, :] == q) & (sides[:, None, None, :4] == s), axis=3
    )
    eye = jnp.eye(size, dtype=jnp.bool_)
    edge = (edge[:, :, None, :, None] > 0) & eye[None, None, :, None, :]
    at = corner_at(flips[:, 4:], size)
    corner = (
        hit[:, 4:, None, None]
        & (sides[:, 4:, None, None] == jnp.arange(4)[None, None, :, None])
        & (jnp.arange(size)[None, None, None, :] == at[:, :, None, None])
    )
    count = res.shape[0]
    pick = jnp.concatenate([edge.reshape(count, 2 * size, 4 * size), corner.reshape(count, 4, 4 * size)], axis=1)
    rims = from_rows(edge_rims(tile))
    out = jnp.einsum("twx,xc->twc", pick.astype(tile.dtype), rims, preferred_element_type=jnp.float32)
    return out.astype(tile.dtype)


def pad_tile(tile, received, mine, position):
    res, rank, sides, flips, live = mine
    size = tile.shape[1]
    n_src, width = received.shape[0], received.shape[1]
    src = jnp.asarray(position)[res]
    cells = flip_index(flips[:4], size)
    column = rank[:, None] * size + cells
    edge = (jnp.arange(n_src)[None, None, :, None] == src[:4, None, None, None]) & (
        jnp.arange(width)[None, None, None, :] == column[:, :, None, None]
    )
    corner = (jnp.arange(n_src)[None, :, None] == src[4:, None, None]) & (
        jnp.arange(width)[None, None, :] == (2 * size + jnp.arange(4))[:, None, None]
    )
    pick = jnp.concatenate([edge.reshape(4 * size, n_src * width), corner.reshape(4, n_src * width)])
    flat = jnp.dot(
        pick.astype(received.dtype), received.reshape(n_src * width, -1), precision=lax.Precision.HIGHEST,
        preferred_element_type=jnp.float32,
    )
    flat = flat.astype(tile.dtype)
    rows = to_rows(flat[: 4 * size], tile)
    corners = flat[4 * size :].reshape((4,) + tile.shape[:1] + tile.shape[3:])
    corners = corners * live.astype(tile.dtype)[:, None, None]
    return assemble(tile, rows[0], rows[1], rows[2], rows[3], corners[0], corners[1], corners[2], corners[3])


def conv_valid(padded, weight):
    return lax.conv_general_dilated(
        padded,
        weight,
        (1, 1),
        "VALID",
        dimension_numbers=("NHWC", "HWIO", "NHWC"),
        preferred_element_type=jnp.float32,
    )


def conv_full(cot, weight):
    flipped = jnp.flip(weight, (0, 1)).transpose(0, 1, 3, 2)
    return lax.conv_general_dilated(
        cot,
        flipped,
        (1, 1),
        ((2, 2), (2, 2)),
        dimension_numbers=("NHWC", "HWIO", "NHWC"),
        preferred_element_type=jnp.float32,
    )


def weight_grad(padded, cot):
    return lax.conv_general_dilated(
        padded,
        cot,
        (1, 1),
        "VALID",
        dimension_numbers=("CHWN", "IHWO", "HWNC"),
        preferred_element_type=jnp.float32,
    )


def push_payloads(full, mine, resid):
    res, rank, sides, flips, live = mine
    size = full.shape[1] - 2
    rows = jnp.stack([full[:, 0, 1:-1], full[:, -1, 1:-1], full[:, 1:-1, 0], full[:, 1:-1, -1]])
    values = jnp.stack([full[:, 0, 0], full[:, 0, -1], full[:, -1, 0], full[:, -1, -1]])
    values = values * live.astype(jnp.float32)[:, None, None]
    source = jnp.concatenate([from_rows(rows), values.reshape(4, -1)])
    hit = res[None, :] == jnp.asarray(resid)[:, None]
    count = resid.shape[0]
    edge = hit[:, None, :4] & (rank[None, None, :] == jnp.arange(2)[None, :, None])
    eye = jnp.eye(size, dtype=jnp.bool_)
    edge = edge[:, :, None, :, None] & eye[None, None, :, None, :]
    edge = jnp.concatenate(
        [edge.reshape(count, 2 * size, 4 * size), jnp.zeros((count, 2 * size, 4), jnp.bool_)], axis=2
    )
    corner = hit[:, 4:, None] & jnp.eye(4, dtype=jnp.bool_)[None]
    corner = jnp.concatenate([jnp.zeros((count, 4, 4 * size), jnp.bool_), corner], axis=2)
    route = jnp.concatenate([edge, corner], axis=1).astype(jnp.float32)
    return jnp.einsum(
        "twx,xc->twc", route, source, precision=lax.Precision.HIGHEST, preferred_element_type=jnp.float32
    )


def back_rims(received, theirs, back, like, offset):
    res, rank, sides, flips, live = theirs
    size = like.shape[1]
    n_src, width = received.shape[0], received.shape[1]
    hit = res == back[:, None]
    s = jnp.arange(4)[:, None, None, None, None]
    j = jnp.arange(size)[None, :, None, None, None]
    cols = jnp.arange(width) - offset
    q = (cols // size)[None, None, None, :, None]
    jj = (cols % size)[None, None, None, :, None]
    in_edge = ((cols >= 0) & (cols < 2 * size))[None, None, None, :, None]
    e_hit = hit[None, None, :, None, :4]
    e_side = sides[None, None, :, None, :4] == s
    e_rank = rank[None, None, :, None, :] == q
    e_cell = jnp.where(flips[None, None, :, None, :4] == 1, size - 1 - j, j) == jj
    edge = jnp.any(e_hit & e_side & e_rank & e_cell & in_edge, axis=4)
    at = corner_at(flips[:, 4:], size)
    c_slot = (cols - 2 * size)[None, None, None, :, None] == jnp.arange(4)[None, None, None, None, :]
    c_hit = hit[None, None, :, None, 4:] & (sides[None, None, :, None, 4:] == s)
    c_cell = j == at[None, None, :, None, :]
    corner = jnp.any(c_hit & c_cell & c_slot, axis=4)
    route = (edge | corner).reshape(4 * size, n_src * width).astype(jnp.float32)
    flat = jnp.dot(
        route, received.reshape(n_src * width, -1), precision=lax.Precision.HIGHEST,
        preferred_element_type=jnp.float32,
    )
    return to_rows(flat, like)


def add_rims(inner, total):
    inner = inner.at[:, 0].add(total[0]).at[:, -1].add(total[1])
    return inner.at[:, :, 0].add(total[2]).at[:, :, -1].add(total[3])


def xor_swap(value, axis, bit):
    size = lax.axis_size(axis)
    return lax.ppermute(value, axis, [(i, i ^ bit) for i in range(size)])


def halving_stages(axis):
    size = lax.axis_size(axis)
    stages = []
    bit = 1
    while bit < size:
        stages.append((axis, bit))
        bit *= 2
    return stages


def scatter_halves(buf, stages):
    for axis, bit in stages:
        half = buf.shape[0] // 2
        high = (lax.axis_index(axis) & bit) != 0
        low_part, high_part = buf[:half], buf[half:]
        send = jnp.where(high, low_part, high_part)
        keep = jnp.where(high, high_part, low_part)
        buf = keep + xor_swap(send, axis, bit)
    return buf


def gather_halves(buf, stages):
    for axis, bit in reversed(stages):
        high = (lax.axis_index(axis) & bit) != 0
        other = xor_swap(buf, axis, bit)
        buf = jnp.where(high, jnp.concatenate([other, buf]), jnp.concatenate([buf, other]))
    return buf


def all_reduce(flat, axes):
    outer, inner = axes
    for axis in axes:
        size = lax.axis_size(axis)
        if size & (size - 1):
            return lax.psum(flat, axes)
    outer_stages = halving_stages(outer)
    count = lax.axis_size(inner)
    if flat.shape[0] % ((1 << len(outer_stages)) * count):
        return lax.psum(flat, axes)
    buf = scatter_halves(flat, outer_stages)
    if count <= 16:
        got = lax.all_to_all(buf.reshape(count, -1), inner, 0, 0)
        part = jnp.sum(got, axis=0)
        full = lax.all_to_all(jnp.broadcast_to(part, (count,) + part.shape), inner, 0, 0)
        buf = full.reshape(-1)
    else:
        inner_stages = halving_stages(inner)
        buf = gather_halves(scatter_halves(buf, inner_stages), inner_stages)
    return gather_halves(buf, outer_stages)


def gelu_tanh(value):
    return jax.nn.gelu(value, approximate=True)


def shards(
    inputs,
    cotangent,
    weight_first,
    weight_second,
    slot_tile,
    neighbour_tile,
    neighbour_turns,
    corner_live,
):
    count = slot_tile.shape[0]
    devices = lax.axis_size("space")
    me = lax.axis_index("space")
    offs = residues(devices)
    slot_of_tile = (
        jnp.zeros((count,), jnp.int32).at[slot_tile].set(jnp.arange(count, dtype=jnp.int32))
    )
    tables = (slot_tile, slot_of_tile, neighbour_tile, neighbour_turns, corner_live)
    plans = make_plans(tables, devices)
    if devices <= 2 * REACH + 1:
        offs = None
        every = jnp.arange(devices, dtype=jnp.int32)
        resid = (every - me) % devices
        position = (every + me) % devices
        back = (me - every) % devices
        theirs = plans
    else:
        resid = np.array([0] + offs, np.int32)
        position = np.zeros((devices,), np.int32)
        position[resid] = np.arange(len(resid))
        back = jnp.asarray((-resid) % devices)
        theirs = tuple(p[(me + resid) % devices] for p in plans)
    mine = tuple(p[me] for p in plans)

    def trip(pull, push):
        if offs is None:
            arrived = swap_all(pull, push)
            return arrived, arrived, pull.shape[1]
        got_pull, got_push = round_trip(pull, push, offs)
        return got_pull, got_push, 0

    tile = inputs[0]
    cot_tile = cotangent[0]
    samples_all = tile.shape[0] * lax.axis_size("dp") * devices
    scale = 1.0 / math.sqrt(samples_all * tile.shape[1] * tile.shape[2])

    full_second = conv_full(cot_tile, weight_second)
    push_second = push_payloads(full_second, mine, resid)
    got_in, got_second, skip = trip(pull_payloads(tile, theirs, back), push_second)

    padded_in = pad_tile(tile, got_in, mine, position)
    hidden = conv_valid(padded_in, weight_first)
    active = gelu_tanh(hidden).astype(jnp.bfloat16)

    inner_second = full_second[:, 1:-1, 1:-1]
    grad_active = add_rims(inner_second, back_rims(got_second, theirs, back, inner_second, skip))
    _, pull_gelu = jax.vjp(gelu_tanh, hidden)
    grad_hidden = pull_gelu(grad_active)[0].astype(jnp.bfloat16)
    full_first = conv_full(grad_hidden, weight_first)
    push_first = push_payloads(full_first, mine, resid)
    pull_act = pull_payloads(active, theirs, back)
    pull_act, push_first, padded_in, grad_hidden = lax.optimization_barrier(
        (pull_act, push_first, padded_in, grad_hidden)
    )
    got_act, got_first, skip = trip(pull_act, push_first)
    local_first = weight_grad(padded_in, grad_hidden)
    got_act, got_first, local_first = lax.optimization_barrier((got_act, got_first, local_first))

    padded_act = pad_tile(active, got_act, mine, position)
    local_second = weight_grad(padded_act, cot_tile)
    inner_first = full_first[:, 1:-1, 1:-1]
    grad_tile = add_rims(inner_first, back_rims(got_first, theirs, back, inner_first, skip))
    grad_tile = grad_tile.astype(jnp.bfloat16)

    flat = jnp.concatenate([local_first.reshape(-1), local_second.reshape(-1)])
    summed = all_reduce(flat, ("dp", "space"))
    half = local_first.size
    summed_first = summed[:half].reshape(local_first.shape)
    summed_second = summed[half:].reshape(local_second.shape)
    return (grad_tile[None], summed_first * scale, summed_second * scale)


def solution(mesh):
    in_specs = (
        P("space", "dp", None, None, None),
        P("space", "dp", None, None, None),
        P(),
        P(),
        P(),
        P(),
        P(),
        P(),
    )
    out_specs = (P("space", "dp", None, None, None), P(), P())
    return jax.shard_map(shards, mesh=mesh, in_specs=in_specs, out_specs=out_specs, check_vma=False)
```

```python
import math

import jax
import jax.numpy as jnp
import numpy as np
from jax import lax
from jax.sharding import PartitionSpec as P

REACH = 7

NEED_SIDE = (1, 0, 3, 2, 1, 1, 0, 0)


def side_tables():
    one = ((3, 0), (2, 0), (0, 1), (1, 1))
    side = np.zeros((4, 4), np.int32)
    flip = np.zeros((4, 4), np.int32)
    side[0] = np.arange(4)
    for r in range(1, 4):
        for s in range(4):
            s1, f1 = one[s]
            side[r, s] = side[r - 1, s1]
            flip[r, s] = flip[r - 1, s1] ^ f1
    return side, flip


def edge_rims(tile):
    return jnp.stack([tile[:, 0], tile[:, -1], tile[:, :, 0], tile[:, :, -1]])


def residues(devices):
    found = []
    for offset in range(-REACH, REACH + 1):
        res = offset % devices
        if res != 0 and res not in found:
            found.append(res)
    return found


def shift(value, by):
    length = lax.axis_size("space")
    return lax.ppermute(value, "space", [(i, (i + by) % length) for i in range(length)])


def swap_all(pull, push):
    payload = jnp.concatenate([pull.astype(jnp.float32), push], axis=1)
    return lax.all_to_all(payload, "space", 0, 0)


def round_trip(pull, push, offs):
    devices = lax.axis_size("space")
    index = {o: i + 1 for i, o in enumerate(offs)}
    rows = pull.shape[1]
    got_pull = [pull[0]]
    got_push = [push[0]]
    for o in offs:
        back = index[(devices - o) % devices]
        payload = jnp.concatenate([pull[back].astype(jnp.float32), push[back]])
        arrived = lax.ppermute(payload, "space", [(i, (i - o) % devices) for i in range(devices)])
        got_pull.append(arrived[:rows].astype(pull.dtype))
        got_push.append(arrived[rows:])
    return jnp.stack(got_pull), jnp.stack(got_push)


def make_plans(tables, devices):
    slot_tile, slot_of_tile, neighbour_tile, neighbour_turns, corner_live = tables
    slots = jnp.arange(devices, dtype=jnp.int32)
    owners = slot_of_tile[neighbour_tile[slot_tile]]
    res = (owners - slots[:, None]) % devices
    turns = neighbour_turns[slot_tile]
    side_tab, flip_tab = side_tables()
    need = np.array(NEED_SIDE, np.int32)[None, :]
    sides = jnp.asarray(side_tab)[turns, need]
    flips = jnp.asarray(flip_tab)[turns, need]
    edge = res[:, :4]
    earlier = np.tril(np.ones((4, 4), bool), -1)
    rank = jnp.sum((edge[:, :, None] == edge[:, None, :]) & earlier, axis=2)
    return res, rank, sides, flips, corner_live[slot_tile]


def flip_index(flips, size):
    cells = jnp.arange(size, dtype=jnp.int32)[None, :]
    return jnp.where(flips[:, None] == 1, size - 1 - cells, cells)


def assemble(own, top, bottom, left, right, top_left, top_right, bottom_left, bottom_right):
    top_row = jnp.concatenate([top_left[:, None], top, top_right[:, None]], axis=1)
    bottom_row = jnp.concatenate([bottom_left[:, None], bottom, bottom_right[:, None]], axis=1)
    middle = jnp.concatenate([left[:, :, None], own, right[:, :, None]], axis=2)
    return jnp.concatenate([top_row[:, None], middle, bottom_row[:, None]], axis=1)


def corner_at(flips, size):
    ends = np.array([size - 1, 0, size - 1, 0], np.int32)
    return jnp.where(flips == 1, size - 1 - ends, ends)


def to_rows(flat, like):
    size = like.shape[1]
    return flat.reshape((-1, size) + like.shape[:1] + like.shape[3:]).transpose(0, 2, 1, 3)


def from_rows(rims):
    return rims.transpose(0, 2, 1, 3).reshape(rims.shape[0] * rims.shape[2], -1)


def pull_payloads(tile, theirs, back):
    res, rank, sides, flips, live = theirs
    size = tile.shape[1]
    hit = res == back[:, None]
    q = jnp.arange(2)[None, :, None, None]
    s = jnp.arange(4)[None, None, :, None]
    edge = jnp.sum(
        hit[:, None, None, :4] & (rank[:, None, None, :] == q) & (sides[:, None, None, :4] == s), axis=3
    )
    eye = jnp.eye(size, dtype=jnp.bool_)
    edge = (edge[:, :, None, :, None] > 0) & eye[None, None, :, None, :]
    at = corner_at(flips[:, 4:], size)
    corner = (
        hit[:, 4:, None, None]
        & (sides[:, 4:, None, None] == jnp.arange(4)[None, None, :, None])
        & (jnp.arange(size)[None, None, None, :] == at[:, :, None, None])
    )
    count = res.shape[0]
    pick = jnp.concatenate([edge.reshape(count, 2 * size, 4 * size), corner.reshape(count, 4, 4 * size)], axis=1)
    rims = from_rows(edge_rims(tile))
    out = jnp.einsum("twx,xc->twc", pick.astype(tile.dtype), rims, preferred_element_type=jnp.float32)
    return out.astype(tile.dtype)


def ring_parts(tile, received, mine, position):
    res, rank, sides, flips, live = mine
    size = tile.shape[1]
    n_src, width = received.shape[0], received.shape[1]
    src = jnp.asarray(position)[res]
    cells = flip_index(flips[:4], size)
    column = rank[:, None] * size + cells
    edge = (jnp.arange(n_src)[None, None, :, None] == src[:4, None, None, None]) & (
        jnp.arange(width)[None, None, None, :] == column[:, :, None, None]
    )
    corner = (jnp.arange(n_src)[None, :, None] == src[4:, None, None]) & (
        jnp.arange(width)[None, None, :] == (2 * size + jnp.arange(4))[:, None, None]
    )
    pick = jnp.concatenate([edge.reshape(4 * size, n_src * width), corner.reshape(4, n_src * width)])
    flat = jnp.dot(
        pick.astype(received.dtype), received.reshape(n_src * width, -1), precision=lax.Precision.HIGHEST,
        preferred_element_type=jnp.float32,
    )
    flat = flat.astype(tile.dtype)
    rows = to_rows(flat[: 4 * size], tile)
    corners = flat[4 * size :].reshape((4,) + tile.shape[:1] + tile.shape[3:])
    corners = corners * live.astype(tile.dtype)[:, None, None]
    return rows, corners


def pad_tile(tile, received, mine, position):
    rows, corners = ring_parts(tile, received, mine, position)
    return assemble(tile, rows[0], rows[1], rows[2], rows[3], corners[0], corners[1], corners[2], corners[3])


def conv_valid(padded, weight):
    return lax.conv_general_dilated(
        padded,
        weight,
        (1, 1),
        "VALID",
        dimension_numbers=("NHWC", "HWIO", "NHWC"),
        preferred_element_type=jnp.float32,
    )


def conv_full(cot, weight):
    flipped = jnp.flip(weight, (0, 1)).transpose(0, 1, 3, 2)
    return lax.conv_general_dilated(
        cot,
        flipped,
        (1, 1),
        ((2, 2), (2, 2)),
        dimension_numbers=("NHWC", "HWIO", "NHWC"),
        preferred_element_type=jnp.float32,
    )


def weight_grad(padded, cot):
    return lax.conv_general_dilated(
        padded,
        cot,
        (1, 1),
        "VALID",
        dimension_numbers=("CHWN", "IHWO", "HWNC"),
        preferred_element_type=jnp.float32,
    )


def zero_padded_weight_grad(tile, cot):
    return lax.conv_general_dilated(
        tile,
        cot,
        (1, 1),
        ((1, 1), (1, 1)),
        dimension_numbers=("CHWN", "IHWO", "HWNC"),
        preferred_element_type=jnp.float32,
    )


def ring_weight_grad(rows, corners, cot):
    size = cot.shape[1]
    zero = jnp.zeros_like(corners[0])[:, None]
    lines = jnp.stack([
        jnp.concatenate([corners[0][:, None], rows[0], corners[1][:, None]], axis=1),
        jnp.concatenate([corners[2][:, None], rows[1], corners[3][:, None]], axis=1),
        jnp.concatenate([zero, rows[2], zero], axis=1),
        jnp.concatenate([zero, rows[3], zero], axis=1),
    ])
    windows = jnp.stack([lines[:, :, t : t + size] for t in range(3)], axis=1)
    edges = jnp.stack([cot[:, 0], cot[:, -1], cot[:, :, 0], cot[:, :, -1]])
    taps = jnp.einsum("ktbjc,kbjd->ktcd", windows, edges, preferred_element_type=jnp.float32)
    grid = jnp.zeros((3, 3) + taps.shape[2:], jnp.float32)
    grid = grid.at[0, :].add(taps[0]).at[2, :].add(taps[1])
    return grid.at[:, 0].add(taps[2]).at[:, 2].add(taps[3])


def push_payloads(full, mine, resid):
    res, rank, sides, flips, live = mine
    size = full.shape[1] - 2
    rows = jnp.stack([full[:, 0, 1:-1], full[:, -1, 1:-1], full[:, 1:-1, 0], full[:, 1:-1, -1]])
    values = jnp.stack([full[:, 0, 0], full[:, 0, -1], full[:, -1, 0], full[:, -1, -1]])
    values = values * live.astype(jnp.float32)[:, None, None]
    source = jnp.concatenate([from_rows(rows), values.reshape(4, -1)])
    hit = res[None, :] == jnp.asarray(resid)[:, None]
    count = resid.shape[0]
    edge = hit[:, None, :4] & (rank[None, None, :] == jnp.arange(2)[None, :, None])
    eye = jnp.eye(size, dtype=jnp.bool_)
    edge = edge[:, :, None, :, None] & eye[None, None, :, None, :]
    edge = jnp.concatenate(
        [edge.reshape(count, 2 * size, 4 * size), jnp.zeros((count, 2 * size, 4), jnp.bool_)], axis=2
    )
    corner = hit[:, 4:, None] & jnp.eye(4, dtype=jnp.bool_)[None]
    corner = jnp.concatenate([jnp.zeros((count, 4, 4 * size), jnp.bool_), corner], axis=2)
    route = jnp.concatenate([edge, corner], axis=1).astype(jnp.float32)
    return jnp.einsum(
        "twx,xc->twc", route, source, precision=lax.Precision.HIGHEST, preferred_element_type=jnp.float32
    )


def back_rims(received, theirs, back, like, offset):
    res, rank, sides, flips, live = theirs
    size = like.shape[1]
    n_src, width = received.shape[0], received.shape[1]
    hit = res == back[:, None]
    s = jnp.arange(4)[:, None, None, None, None]
    j = jnp.arange(size)[None, :, None, None, None]
    cols = jnp.arange(width) - offset
    q = (cols // size)[None, None, None, :, None]
    jj = (cols % size)[None, None, None, :, None]
    in_edge = ((cols >= 0) & (cols < 2 * size))[None, None, None, :, None]
    e_hit = hit[None, None, :, None, :4]
    e_side = sides[None, None, :, None, :4] == s
    e_rank = rank[None, None, :, None, :] == q
    e_cell = jnp.where(flips[None, None, :, None, :4] == 1, size - 1 - j, j) == jj
    edge = jnp.any(e_hit & e_side & e_rank & e_cell & in_edge, axis=4)
    at = corner_at(flips[:, 4:], size)
    c_slot = (cols - 2 * size)[None, None, None, :, None] == jnp.arange(4)[None, None, None, None, :]
    c_hit = hit[None, None, :, None, 4:] & (sides[None, None, :, None, 4:] == s)
    c_cell = j == at[None, None, :, None, :]
    corner = jnp.any(c_hit & c_cell & c_slot, axis=4)
    route = (edge | corner).reshape(4 * size, n_src * width).astype(jnp.float32)
    flat = jnp.dot(
        route, received.reshape(n_src * width, -1), precision=lax.Precision.HIGHEST,
        preferred_element_type=jnp.float32,
    )
    return to_rows(flat, like)


def add_rims(inner, total):
    inner = inner.at[:, 0].add(total[0]).at[:, -1].add(total[1])
    return inner.at[:, :, 0].add(total[2]).at[:, :, -1].add(total[3])


def xor_swap(value, axis, bit):
    size = lax.axis_size(axis)
    return lax.ppermute(value, axis, [(i, i ^ bit) for i in range(size)])


def halving_stages(axis):
    size = lax.axis_size(axis)
    stages = []
    bit = 1
    while bit < size:
        stages.append((axis, bit))
        bit *= 2
    return stages


def scatter_halves(buf, stages):
    for axis, bit in stages:
        half = buf.shape[0] // 2
        high = (lax.axis_index(axis) & bit) != 0
        low_part, high_part = buf[:half], buf[half:]
        send = jnp.where(high, low_part, high_part)
        keep = jnp.where(high, high_part, low_part)
        buf = keep + xor_swap(send, axis, bit)
    return buf


def gather_halves(buf, stages):
    for axis, bit in reversed(stages):
        high = (lax.axis_index(axis) & bit) != 0
        other = xor_swap(buf, axis, bit)
        buf = jnp.where(high, jnp.concatenate([other, buf]), jnp.concatenate([buf, other]))
    return buf


def all_reduce(flat, axes):
    outer, inner = axes
    for axis in axes:
        size = lax.axis_size(axis)
        if size & (size - 1):
            return lax.psum(flat, axes)
    outer_stages = halving_stages(outer)
    count = lax.axis_size(inner)
    if flat.shape[0] % ((1 << len(outer_stages)) * count):
        return lax.psum(flat, axes)
    buf = scatter_halves(flat, outer_stages)
    if count <= 16:
        got = lax.all_to_all(buf.reshape(count, -1), inner, 0, 0)
        part = jnp.sum(got, axis=0)
        full = lax.all_to_all(jnp.broadcast_to(part, (count,) + part.shape), inner, 0, 0)
        buf = full.reshape(-1)
    else:
        inner_stages = halving_stages(inner)
        buf = gather_halves(scatter_halves(buf, inner_stages), inner_stages)
    return gather_halves(buf, outer_stages)


def gelu_tanh(value):
    return jax.nn.gelu(value, approximate=True)


def shards(
    inputs,
    cotangent,
    weight_first,
    weight_second,
    slot_tile,
    neighbour_tile,
    neighbour_turns,
    corner_live,
):
    count = slot_tile.shape[0]
    devices = lax.axis_size("space")
    me = lax.axis_index("space")
    offs = residues(devices)
    slot_of_tile = (
        jnp.zeros((count,), jnp.int32).at[slot_tile].set(jnp.arange(count, dtype=jnp.int32))
    )
    tables = (slot_tile, slot_of_tile, neighbour_tile, neighbour_turns, corner_live)
    plans = make_plans(tables, devices)
    if devices <= 2 * REACH + 1:
        offs = None
        every = jnp.arange(devices, dtype=jnp.int32)
        resid = (every - me) % devices
        position = (every + me) % devices
        back = (me - every) % devices
        theirs = plans
    else:
        resid = np.array([0] + offs, np.int32)
        position = np.zeros((devices,), np.int32)
        position[resid] = np.arange(len(resid))
        back = jnp.asarray((-resid) % devices)
        theirs = tuple(p[(me + resid) % devices] for p in plans)
    mine = tuple(p[me] for p in plans)

    def trip(pull, push):
        if offs is None:
            arrived = swap_all(pull, push)
            return arrived, arrived, pull.shape[1]
        got_pull, got_push = round_trip(pull, push, offs)
        return got_pull, got_push, 0

    tile = inputs[0]
    cot_tile = cotangent[0]
    samples_all = tile.shape[0] * lax.axis_size("dp") * devices
    scale = 1.0 / math.sqrt(samples_all * tile.shape[1] * tile.shape[2])

    full_second = conv_full(cot_tile, weight_second)
    push_second = push_payloads(full_second, mine, resid)
    got_in, got_second, skip = trip(pull_payloads(tile, theirs, back), push_second)

    padded_in = pad_tile(tile, got_in, mine, position)
    hidden = conv_valid(padded_in, weight_first)
    active = gelu_tanh(hidden).astype(jnp.bfloat16)

    inner_second = full_second[:, 1:-1, 1:-1]
    grad_active = add_rims(inner_second, back_rims(got_second, theirs, back, inner_second, skip))
    _, pull_gelu = jax.vjp(gelu_tanh, hidden)
    grad_hidden = pull_gelu(grad_active)[0].astype(jnp.bfloat16)
    full_first = conv_full(grad_hidden, weight_first)
    push_first = push_payloads(full_first, mine, resid)
    pull_act = pull_payloads(active, theirs, back)
    pull_act, push_first, padded_in, grad_hidden, active = lax.optimization_barrier(
        (pull_act, push_first, padded_in, grad_hidden, active)
    )
    got_act, got_first, skip = trip(pull_act, push_first)
    local_first = weight_grad(padded_in, grad_hidden)
    bulk_second = zero_padded_weight_grad(active, cot_tile)
    got_act, got_first, local_first, bulk_second = lax.optimization_barrier(
        (got_act, got_first, local_first, bulk_second)
    )

    rows_act, corners_act = ring_parts(active, got_act, mine, position)
    local_second = bulk_second + ring_weight_grad(rows_act, corners_act, cot_tile)
    inner_first = full_first[:, 1:-1, 1:-1]
    grad_tile = add_rims(inner_first, back_rims(got_first, theirs, back, inner_first, skip))
    grad_tile = grad_tile.astype(jnp.bfloat16)

    flat = jnp.concatenate([local_first.reshape(-1), local_second.reshape(-1)])
    summed = all_reduce(flat, ("dp", "space"))
    half = local_first.size
    summed_first = summed[:half].reshape(local_first.shape)
    summed_second = summed[half:].reshape(local_second.shape)
    return (grad_tile[None], summed_first * scale, summed_second * scale)


def solution(mesh):
    in_specs = (
        P("space", "dp", None, None, None),
        P("space", "dp", None, None, None),
        P(),
        P(),
        P(),
        P(),
        P(),
        P(),
    )
    out_specs = (P("space", "dp", None, None, None), P(), P())
    return jax.shard_map(shards, mesh=mesh, in_specs=in_specs, out_specs=out_specs, check_vma=False)
```

```python
import math

import jax
import jax.numpy as jnp
import numpy as np
from jax import lax
from jax.sharding import PartitionSpec as P

REACH = 7

NEED_SIDE = (1, 0, 3, 2, 1, 1, 0, 0)


def side_tables():
    one = ((3, 0), (2, 0), (0, 1), (1, 1))
    side = np.zeros((4, 4), np.int32)
    flip = np.zeros((4, 4), np.int32)
    side[0] = np.arange(4)
    for r in range(1, 4):
        for s in range(4):
            s1, f1 = one[s]
            side[r, s] = side[r - 1, s1]
            flip[r, s] = flip[r - 1, s1] ^ f1
    return side, flip


def edge_rims(tile):
    return jnp.stack([tile[:, 0], tile[:, -1], tile[:, :, 0], tile[:, :, -1]])


def residues(devices):
    found = []
    for offset in range(-REACH, REACH + 1):
        res = offset % devices
        if res != 0 and res not in found:
            found.append(res)
    return found


def shift(value, by):
    length = lax.axis_size("space")
    return lax.ppermute(value, "space", [(i, (i + by) % length) for i in range(length)])


def swap_all(pull, push):
    payload = jnp.concatenate([pull.astype(jnp.float32), push], axis=1)
    return lax.all_to_all(payload, "space", 0, 0)


def round_trip(pull, push, offs):
    devices = lax.axis_size("space")
    index = {o: i + 1 for i, o in enumerate(offs)}
    rows = pull.shape[1]
    got_pull = [pull[0]]
    got_push = [push[0]]
    for o in offs:
        back = index[(devices - o) % devices]
        payload = jnp.concatenate([pull[back].astype(jnp.float32), push[back]])
        arrived = lax.ppermute(payload, "space", [(i, (i - o) % devices) for i in range(devices)])
        got_pull.append(arrived[:rows].astype(pull.dtype))
        got_push.append(arrived[rows:])
    return jnp.stack(got_pull), jnp.stack(got_push)


def make_plans(tables, devices):
    slot_tile, slot_of_tile, neighbour_tile, neighbour_turns, corner_live = tables
    slots = jnp.arange(devices, dtype=jnp.int32)
    owners = slot_of_tile[neighbour_tile[slot_tile]]
    res = (owners - slots[:, None]) % devices
    turns = neighbour_turns[slot_tile]
    side_tab, flip_tab = side_tables()
    need = np.array(NEED_SIDE, np.int32)[None, :]
    sides = jnp.asarray(side_tab)[turns, need]
    flips = jnp.asarray(flip_tab)[turns, need]
    edge = res[:, :4]
    earlier = np.tril(np.ones((4, 4), bool), -1)
    rank = jnp.sum((edge[:, :, None] == edge[:, None, :]) & earlier, axis=2)
    return res, rank, sides, flips, corner_live[slot_tile]


def flip_index(flips, size):
    cells = jnp.arange(size, dtype=jnp.int32)[None, :]
    return jnp.where(flips[:, None] == 1, size - 1 - cells, cells)


def assemble(own, top, bottom, left, right, top_left, top_right, bottom_left, bottom_right):
    top_row = jnp.concatenate([top_left[:, None], top, top_right[:, None]], axis=1)
    bottom_row = jnp.concatenate([bottom_left[:, None], bottom, bottom_right[:, None]], axis=1)
    middle = jnp.concatenate([left[:, :, None], own, right[:, :, None]], axis=2)
    return jnp.concatenate([top_row[:, None], middle, bottom_row[:, None]], axis=1)


def corner_at(flips, size):
    ends = np.array([size - 1, 0, size - 1, 0], np.int32)
    return jnp.where(flips == 1, size - 1 - ends, ends)


def to_rows(flat, like):
    size = like.shape[1]
    return flat.reshape((-1, size) + like.shape[:1] + like.shape[3:]).transpose(0, 2, 1, 3)


def from_rows(rims):
    return rims.transpose(0, 2, 1, 3).reshape(rims.shape[0] * rims.shape[2], -1)


def pull_payloads(tile, theirs, back):
    res, rank, sides, flips, live = theirs
    size = tile.shape[1]
    hit = res == back[:, None]
    q = jnp.arange(2)[None, :, None, None]
    s = jnp.arange(4)[None, None, :, None]
    edge = jnp.sum(
        hit[:, None, None, :4] & (rank[:, None, None, :] == q) & (sides[:, None, None, :4] == s), axis=3
    )
    eye = jnp.eye(size, dtype=jnp.bool_)
    edge = (edge[:, :, None, :, None] > 0) & eye[None, None, :, None, :]
    at = corner_at(flips[:, 4:], size)
    corner = (
        hit[:, 4:, None, None]
        & (sides[:, 4:, None, None] == jnp.arange(4)[None, None, :, None])
        & (jnp.arange(size)[None, None, None, :] == at[:, :, None, None])
    )
    count = res.shape[0]
    pick = jnp.concatenate([edge.reshape(count, 2 * size, 4 * size), corner.reshape(count, 4, 4 * size)], axis=1)
    rims = from_rows(edge_rims(tile))
    out = jnp.einsum("twx,xc->twc", pick.astype(tile.dtype), rims, preferred_element_type=jnp.float32)
    return out.astype(tile.dtype)


def ring_parts(tile, received, mine, position):
    res, rank, sides, flips, live = mine
    size = tile.shape[1]
    n_src, width = received.shape[0], received.shape[1]
    src = jnp.asarray(position)[res]
    cells = flip_index(flips[:4], size)
    column = rank[:, None] * size + cells
    edge = (jnp.arange(n_src)[None, None, :, None] == src[:4, None, None, None]) & (
        jnp.arange(width)[None, None, None, :] == column[:, :, None, None]
    )
    corner = (jnp.arange(n_src)[None, :, None] == src[4:, None, None]) & (
        jnp.arange(width)[None, None, :] == (2 * size + jnp.arange(4))[:, None, None]
    )
    pick = jnp.concatenate([edge.reshape(4 * size, n_src * width), corner.reshape(4, n_src * width)])
    flat = jnp.dot(
        pick.astype(received.dtype), received.reshape(n_src * width, -1), precision=lax.Precision.HIGHEST,
        preferred_element_type=jnp.float32,
    )
    flat = flat.astype(tile.dtype)
    rows = to_rows(flat[: 4 * size], tile)
    corners = flat[4 * size :].reshape((4,) + tile.shape[:1] + tile.shape[3:])
    corners = corners * live.astype(tile.dtype)[:, None, None]
    return rows, corners


def pad_tile(tile, received, mine, position):
    rows, corners = ring_parts(tile, received, mine, position)
    return assemble(tile, rows[0], rows[1], rows[2], rows[3], corners[0], corners[1], corners[2], corners[3])


def conv_valid(padded, weight):
    return lax.conv_general_dilated(
        padded,
        weight,
        (1, 1),
        "VALID",
        dimension_numbers=("NHWC", "HWIO", "NHWC"),
        preferred_element_type=jnp.float32,
    )


def conv_full(cot, weight):
    flipped = jnp.flip(weight, (0, 1)).transpose(0, 1, 3, 2)
    return lax.conv_general_dilated(
        cot,
        flipped,
        (1, 1),
        ((2, 2), (2, 2)),
        dimension_numbers=("NHWC", "HWIO", "NHWC"),
        preferred_element_type=jnp.float32,
    )


def weight_grad(padded, cot):
    return lax.conv_general_dilated(
        padded,
        cot,
        (1, 1),
        "VALID",
        dimension_numbers=("CHWN", "IHWO", "HWNC"),
        preferred_element_type=jnp.float32,
    )


def zero_padded_weight_grad(tile, cot):
    return lax.conv_general_dilated(
        tile,
        cot,
        (1, 1),
        ((1, 1), (1, 1)),
        dimension_numbers=("CHWN", "IHWO", "HWNC"),
        preferred_element_type=jnp.float32,
    )


def ring_weight_grad(rows, corners, cot):
    size = cot.shape[1]
    zero = jnp.zeros_like(corners[0])[:, None]
    lines = jnp.stack([
        jnp.concatenate([corners[0][:, None], rows[0], corners[1][:, None]], axis=1),
        jnp.concatenate([corners[2][:, None], rows[1], corners[3][:, None]], axis=1),
        jnp.concatenate([zero, rows[2], zero], axis=1),
        jnp.concatenate([zero, rows[3], zero], axis=1),
    ])
    windows = jnp.stack([lines[:, :, t : t + size] for t in range(3)], axis=1)
    edges = jnp.stack([cot[:, 0], cot[:, -1], cot[:, :, 0], cot[:, :, -1]])
    taps = jnp.einsum("ktbjc,kbjd->ktcd", windows, edges, preferred_element_type=jnp.float32)
    grid = jnp.zeros((3, 3) + taps.shape[2:], jnp.float32)
    grid = grid.at[0, :].add(taps[0]).at[2, :].add(taps[1])
    return grid.at[:, 0].add(taps[2]).at[:, 2].add(taps[3])


def push_payloads(full, mine, resid):
    res, rank, sides, flips, live = mine
    size = full.shape[1] - 2
    rows = jnp.stack([full[:, 0, 1:-1], full[:, -1, 1:-1], full[:, 1:-1, 0], full[:, 1:-1, -1]])
    values = jnp.stack([full[:, 0, 0], full[:, 0, -1], full[:, -1, 0], full[:, -1, -1]])
    values = values * live.astype(jnp.float32)[:, None, None]
    source = jnp.concatenate([from_rows(rows), values.reshape(4, -1)])
    hit = res[None, :] == jnp.asarray(resid)[:, None]
    count = resid.shape[0]
    edge = hit[:, None, :4] & (rank[None, None, :] == jnp.arange(2)[None, :, None])
    eye = jnp.eye(size, dtype=jnp.bool_)
    edge = edge[:, :, None, :, None] & eye[None, None, :, None, :]
    edge = jnp.concatenate(
        [edge.reshape(count, 2 * size, 4 * size), jnp.zeros((count, 2 * size, 4), jnp.bool_)], axis=2
    )
    corner = hit[:, 4:, None] & jnp.eye(4, dtype=jnp.bool_)[None]
    corner = jnp.concatenate([jnp.zeros((count, 4, 4 * size), jnp.bool_), corner], axis=2)
    route = jnp.concatenate([edge, corner], axis=1).astype(jnp.float32)
    return jnp.einsum(
        "twx,xc->twc", route, source, precision=lax.Precision.HIGHEST, preferred_element_type=jnp.float32
    )


def back_rims(received, theirs, back, like, offset):
    res, rank, sides, flips, live = theirs
    size = like.shape[1]
    n_src, width = received.shape[0], received.shape[1]
    hit = res == back[:, None]
    s = jnp.arange(4)[:, None, None, None, None, None]
    j = jnp.arange(size)[None, :, None, None, None, None]
    q = jnp.arange(2)[None, None, None, :, None, None]
    jj = jnp.arange(size)[None, None, None, None, :, None]
    e_hit = hit[None, None, :, None, None, :4] & (sides[None, None, :, None, None, :4] == s)
    e_rank = rank[None, None, :, None, None, :] == q
    e_cell = jnp.where(flips[None, None, :, None, None, :4] == 1, size - 1 - j, j) == jj
    edge = jnp.any(e_hit & e_rank & e_cell, axis=5).reshape(4, size, n_src, 2 * size)
    at = corner_at(flips[:, 4:], size)
    c_hit = hit[None, None, :, 4:] & (sides[None, None, :, 4:] == jnp.arange(4)[:, None, None, None])
    corner = c_hit & (jnp.arange(size)[None, :, None, None] == at[None, None, :, :])
    block = jnp.concatenate([edge, corner], axis=3)
    tail = width - offset - block.shape[3]
    route = jnp.pad(block, ((0, 0), (0, 0), (0, 0), (offset, tail)))
    route = route.reshape(4 * size, n_src * width).astype(jnp.float32)
    flat = jnp.dot(
        route, received.reshape(n_src * width, -1), precision=lax.Precision.HIGHEST,
        preferred_element_type=jnp.float32,
    )
    return to_rows(flat, like)

def add_rims(inner, total):
    inner = inner.at[:, 0].add(total[0]).at[:, -1].add(total[1])
    return inner.at[:, :, 0].add(total[2]).at[:, :, -1].add(total[3])


def xor_swap(value, axis, bit):
    size = lax.axis_size(axis)
    return lax.ppermute(value, axis, [(i, i ^ bit) for i in range(size)])


def halving_stages(axis):
    size = lax.axis_size(axis)
    stages = []
    bit = 1
    while bit < size:
        stages.append((axis, bit))
        bit *= 2
    return stages


def scatter_halves(buf, stages):
    for axis, bit in stages:
        half = buf.shape[0] // 2
        high = (lax.axis_index(axis) & bit) != 0
        low_part, high_part = buf[:half], buf[half:]
        send = jnp.where(high, low_part, high_part)
        keep = jnp.where(high, high_part, low_part)
        buf = keep + xor_swap(send, axis, bit)
    return buf


def gather_halves(buf, stages):
    for axis, bit in reversed(stages):
        high = (lax.axis_index(axis) & bit) != 0
        other = xor_swap(buf, axis, bit)
        buf = jnp.where(high, jnp.concatenate([other, buf]), jnp.concatenate([buf, other]))
    return buf


def all_reduce(flat, axes):
    outer, inner = axes
    for axis in axes:
        size = lax.axis_size(axis)
        if size & (size - 1):
            return lax.psum(flat, axes)
    outer_stages = halving_stages(outer)
    count = lax.axis_size(inner)
    if flat.shape[0] % ((1 << len(outer_stages)) * count):
        return lax.psum(flat, axes)
    buf = scatter_halves(flat, outer_stages)
    if count <= 16:
        got = lax.all_to_all(buf.reshape(count, -1), inner, 0, 0)
        part = jnp.sum(got, axis=0)
        full = lax.all_to_all(jnp.broadcast_to(part, (count,) + part.shape), inner, 0, 0)
        buf = full.reshape(-1)
    else:
        inner_stages = halving_stages(inner)
        buf = gather_halves(scatter_halves(buf, inner_stages), inner_stages)
    return gather_halves(buf, outer_stages)


def gelu_tanh(value):
    return jax.nn.gelu(value, approximate=True)


def shards(
    inputs,
    cotangent,
    weight_first,
    weight_second,
    slot_tile,
    neighbour_tile,
    neighbour_turns,
    corner_live,
):
    count = slot_tile.shape[0]
    devices = lax.axis_size("space")
    me = lax.axis_index("space")
    offs = residues(devices)
    slot_of_tile = (
        jnp.zeros((count,), jnp.int32).at[slot_tile].set(jnp.arange(count, dtype=jnp.int32))
    )
    tables = (slot_tile, slot_of_tile, neighbour_tile, neighbour_turns, corner_live)
    plans = make_plans(tables, devices)
    if devices <= 2 * REACH + 1:
        offs = None
        every = jnp.arange(devices, dtype=jnp.int32)
        resid = (every - me) % devices
        position = (every + me) % devices
        back = (me - every) % devices
        theirs = plans
    else:
        resid = np.array([0] + offs, np.int32)
        position = np.zeros((devices,), np.int32)
        position[resid] = np.arange(len(resid))
        back = jnp.asarray((-resid) % devices)
        theirs = tuple(p[(me + resid) % devices] for p in plans)
    mine = tuple(p[me] for p in plans)

    def trip(pull, push):
        if offs is None:
            arrived = swap_all(pull, push)
            return arrived, arrived, pull.shape[1]
        got_pull, got_push = round_trip(pull, push, offs)
        return got_pull, got_push, 0

    tile = inputs[0]
    cot_tile = cotangent[0]
    samples_all = tile.shape[0] * lax.axis_size("dp") * devices
    scale = 1.0 / math.sqrt(samples_all * tile.shape[1] * tile.shape[2])

    full_second = conv_full(cot_tile, weight_second)
    push_second = push_payloads(full_second, mine, resid)
    got_in, got_second, skip = trip(pull_payloads(tile, theirs, back), push_second)

    padded_in = pad_tile(tile, got_in, mine, position)
    hidden = conv_valid(padded_in, weight_first)
    active = gelu_tanh(hidden).astype(jnp.bfloat16)

    inner_second = full_second[:, 1:-1, 1:-1]
    grad_active = add_rims(inner_second, back_rims(got_second, theirs, back, inner_second, skip))
    _, pull_gelu = jax.vjp(gelu_tanh, hidden)
    grad_hidden = pull_gelu(grad_active)[0].astype(jnp.bfloat16)
    full_first = conv_full(grad_hidden, weight_first)
    push_first = push_payloads(full_first, mine, resid)
    pull_act = pull_payloads(active, theirs, back)
    pull_act, push_first, padded_in, grad_hidden, active = lax.optimization_barrier(
        (pull_act, push_first, padded_in, grad_hidden, active)
    )
    got_act, got_first, skip = trip(pull_act, push_first)
    local_first = weight_grad(padded_in, grad_hidden)
    bulk_second = zero_padded_weight_grad(active, cot_tile)
    got_act, got_first, local_first, bulk_second = lax.optimization_barrier(
        (got_act, got_first, local_first, bulk_second)
    )

    rows_act, corners_act = ring_parts(active, got_act, mine, position)
    local_second = bulk_second + ring_weight_grad(rows_act, corners_act, cot_tile)
    inner_first = full_first[:, 1:-1, 1:-1]
    grad_tile = add_rims(inner_first, back_rims(got_first, theirs, back, inner_first, skip))
    grad_tile = grad_tile.astype(jnp.bfloat16)

    flat = jnp.concatenate([local_first.reshape(-1), local_second.reshape(-1)])
    summed = all_reduce(flat, ("dp", "space"))
    half = local_first.size
    summed_first = summed[:half].reshape(local_first.shape)
    summed_second = summed[half:].reshape(local_second.shape)
    return (grad_tile[None], summed_first * scale, summed_second * scale)


def solution(mesh):
    in_specs = (
        P("space", "dp", None, None, None),
        P("space", "dp", None, None, None),
        P(),
        P(),
        P(),
        P(),
        P(),
        P(),
    )
    out_specs = (P("space", "dp", None, None, None), P(), P())
    return jax.shard_map(shards, mesh=mesh, in_specs=in_specs, out_specs=out_specs, check_vma=False)
```

```python
import math

import jax
import jax.numpy as jnp
import numpy as np
from jax import lax
from jax.sharding import PartitionSpec as P

REACH = 7

NEED_SIDE = (1, 0, 3, 2, 1, 1, 0, 0)


def side_tables():
    one = ((3, 0), (2, 0), (0, 1), (1, 1))
    side = np.zeros((4, 4), np.int32)
    flip = np.zeros((4, 4), np.int32)
    side[0] = np.arange(4)
    for r in range(1, 4):
        for s in range(4):
            s1, f1 = one[s]
            side[r, s] = side[r - 1, s1]
            flip[r, s] = flip[r - 1, s1] ^ f1
    return side, flip


def edge_rims(tile):
    return jnp.stack([tile[:, 0], tile[:, -1], tile[:, :, 0], tile[:, :, -1]])


def residues(devices):
    found = []
    for offset in range(-REACH, REACH + 1):
        res = offset % devices
        if res != 0 and res not in found:
            found.append(res)
    return found


def shift(value, by):
    length = lax.axis_size("space")
    return lax.ppermute(value, "space", [(i, (i + by) % length) for i in range(length)])


def swap_all(pull, push):
    payload = jnp.concatenate([pull.astype(jnp.float32), push], axis=1)
    return lax.all_to_all(payload, "space", 0, 0)


def round_trip(pull, push, offs):
    devices = lax.axis_size("space")
    index = {o: i + 1 for i, o in enumerate(offs)}
    rows = pull.shape[1]
    got_pull = [pull[0]]
    got_push = [push[0]]
    for o in offs:
        back = index[(devices - o) % devices]
        payload = jnp.concatenate([pull[back].astype(jnp.float32), push[back]])
        arrived = lax.ppermute(payload, "space", [(i, (i - o) % devices) for i in range(devices)])
        got_pull.append(arrived[:rows].astype(pull.dtype))
        got_push.append(arrived[rows:])
    return jnp.stack(got_pull), jnp.stack(got_push)


def make_plans(tables, devices):
    slot_tile, slot_of_tile, neighbour_tile, neighbour_turns, corner_live = tables
    slots = jnp.arange(devices, dtype=jnp.int32)
    owners = slot_of_tile[neighbour_tile[slot_tile]]
    res = (owners - slots[:, None]) % devices
    turns = neighbour_turns[slot_tile]
    side_tab, flip_tab = side_tables()
    need = np.array(NEED_SIDE, np.int32)[None, :]
    sides = jnp.asarray(side_tab)[turns, need]
    flips = jnp.asarray(flip_tab)[turns, need]
    edge = res[:, :4]
    earlier = np.tril(np.ones((4, 4), bool), -1)
    rank = jnp.sum((edge[:, :, None] == edge[:, None, :]) & earlier, axis=2)
    return res, rank, sides, flips, corner_live[slot_tile]


def flip_index(flips, size):
    cells = jnp.arange(size, dtype=jnp.int32)[None, :]
    return jnp.where(flips[:, None] == 1, size - 1 - cells, cells)


def assemble(own, top, bottom, left, right, top_left, top_right, bottom_left, bottom_right):
    top_row = jnp.concatenate([top_left[:, None], top, top_right[:, None]], axis=1)
    bottom_row = jnp.concatenate([bottom_left[:, None], bottom, bottom_right[:, None]], axis=1)
    middle = jnp.concatenate([left[:, :, None], own, right[:, :, None]], axis=2)
    return jnp.concatenate([top_row[:, None], middle, bottom_row[:, None]], axis=1)


def corner_at(flips, size):
    ends = np.array([size - 1, 0, size - 1, 0], np.int32)
    return jnp.where(flips == 1, size - 1 - ends, ends)


def to_rows(flat, like):
    size = like.shape[1]
    return flat.reshape((-1, size) + like.shape[:1] + like.shape[3:]).transpose(0, 2, 1, 3)


def from_rows(rims):
    return rims.transpose(0, 2, 1, 3).reshape(rims.shape[0] * rims.shape[2], -1)


def pull_payloads(tile, theirs, back):
    res, rank, sides, flips, live = theirs
    size = tile.shape[1]
    hit = res == back[:, None]
    q = jnp.arange(2)[None, :, None, None]
    s = jnp.arange(4)[None, None, :, None]
    edge = jnp.sum(
        hit[:, None, None, :4] & (rank[:, None, None, :] == q) & (sides[:, None, None, :4] == s), axis=3
    )
    eye = jnp.eye(size, dtype=jnp.bool_)
    edge = (edge[:, :, None, :, None] > 0) & eye[None, None, :, None, :]
    at = corner_at(flips[:, 4:], size)
    corner = (
        hit[:, 4:, None, None]
        & (sides[:, 4:, None, None] == jnp.arange(4)[None, None, :, None])
        & (jnp.arange(size)[None, None, None, :] == at[:, :, None, None])
    )
    count = res.shape[0]
    pick = jnp.concatenate([edge.reshape(count, 2 * size, 4 * size), corner.reshape(count, 4, 4 * size)], axis=1)
    rims = from_rows(edge_rims(tile))
    out = jnp.einsum("twx,xc->twc", pick.astype(tile.dtype), rims, preferred_element_type=jnp.float32)
    return out.astype(tile.dtype)


def ring_parts(tile, received, mine, position):
    res, rank, sides, flips, live = mine
    size = tile.shape[1]
    n_src, width = received.shape[0], received.shape[1]
    src = jnp.asarray(position)[res]
    cells = flip_index(flips[:4], size)
    column = rank[:, None] * size + cells
    edge = (jnp.arange(n_src)[None, None, :, None] == src[:4, None, None, None]) & (
        jnp.arange(width)[None, None, None, :] == column[:, :, None, None]
    )
    corner = (jnp.arange(n_src)[None, :, None] == src[4:, None, None]) & (
        jnp.arange(width)[None, None, :] == (2 * size + jnp.arange(4))[:, None, None]
    )
    pick = jnp.concatenate([edge.reshape(4 * size, n_src * width), corner.reshape(4, n_src * width)])
    flat = jnp.dot(
        pick.astype(received.dtype), received.reshape(n_src * width, -1), precision=lax.Precision.HIGHEST,
        preferred_element_type=jnp.float32,
    )
    flat = flat.astype(tile.dtype)
    rows = to_rows(flat[: 4 * size], tile)
    corners = flat[4 * size :].reshape((4,) + tile.shape[:1] + tile.shape[3:])
    corners = corners * live.astype(tile.dtype)[:, None, None]
    return rows, corners


def pad_tile(tile, received, mine, position):
    rows, corners = ring_parts(tile, received, mine, position)
    return assemble(tile, rows[0], rows[1], rows[2], rows[3], corners[0], corners[1], corners[2], corners[3])


def conv_valid(padded, weight):
    return lax.conv_general_dilated(
        padded,
        weight,
        (1, 1),
        "VALID",
        dimension_numbers=("NHWC", "HWIO", "NHWC"),
        preferred_element_type=jnp.float32,
    )


def conv_full(cot, weight):
    flipped = jnp.flip(weight, (0, 1)).transpose(0, 1, 3, 2)
    return lax.conv_general_dilated(
        cot,
        flipped,
        (1, 1),
        ((2, 2), (2, 2)),
        dimension_numbers=("NHWC", "HWIO", "NHWC"),
        preferred_element_type=jnp.float32,
    )


def weight_grad(padded, cot):
    return lax.conv_general_dilated(
        padded,
        cot,
        (1, 1),
        "VALID",
        dimension_numbers=("CHWN", "IHWO", "HWNC"),
        preferred_element_type=jnp.float32,
    )


def zero_padded_weight_grad(tile, cot):
    return lax.conv_general_dilated(
        tile,
        cot,
        (1, 1),
        ((1, 1), (1, 1)),
        dimension_numbers=("CHWN", "IHWO", "HWNC"),
        preferred_element_type=jnp.float32,
    )


def ring_weight_grad(rows, corners, cot):
    size = cot.shape[1]
    zero = jnp.zeros_like(corners[0])[:, None]
    lines = jnp.stack([
        jnp.concatenate([corners[0][:, None], rows[0], corners[1][:, None]], axis=1),
        jnp.concatenate([corners[2][:, None], rows[1], corners[3][:, None]], axis=1),
        jnp.concatenate([zero, rows[2], zero], axis=1),
        jnp.concatenate([zero, rows[3], zero], axis=1),
    ])
    windows = jnp.stack([lines[:, :, t : t + size] for t in range(3)], axis=1)
    edges = jnp.stack([cot[:, 0], cot[:, -1], cot[:, :, 0], cot[:, :, -1]])
    taps = jnp.einsum("ktbjc,kbjd->ktcd", windows, edges, preferred_element_type=jnp.float32)
    grid = jnp.zeros((3, 3) + taps.shape[2:], jnp.float32)
    grid = grid.at[0, :].add(taps[0]).at[2, :].add(taps[1])
    return grid.at[:, 0].add(taps[2]).at[:, 2].add(taps[3])


def push_payloads(full, mine, resid):
    res, rank, sides, flips, live = mine
    size = full.shape[1] - 2
    rows = jnp.stack([full[:, 0, 1:-1], full[:, -1, 1:-1], full[:, 1:-1, 0], full[:, 1:-1, -1]])
    values = jnp.stack([full[:, 0, 0], full[:, 0, -1], full[:, -1, 0], full[:, -1, -1]])
    values = values * live.astype(jnp.float32)[:, None, None]
    source = jnp.concatenate([from_rows(rows), values.reshape(4, -1)])
    hit = res[None, :] == jnp.asarray(resid)[:, None]
    count = resid.shape[0]
    edge = hit[:, None, :4] & (rank[None, None, :] == jnp.arange(2)[None, :, None])
    eye = jnp.eye(size, dtype=jnp.bool_)
    edge = edge[:, :, None, :, None] & eye[None, None, :, None, :]
    edge = jnp.concatenate(
        [edge.reshape(count, 2 * size, 4 * size), jnp.zeros((count, 2 * size, 4), jnp.bool_)], axis=2
    )
    corner = hit[:, 4:, None] & jnp.eye(4, dtype=jnp.bool_)[None]
    corner = jnp.concatenate([jnp.zeros((count, 4, 4 * size), jnp.bool_), corner], axis=2)
    route = jnp.concatenate([edge, corner], axis=1).astype(jnp.float32)
    return jnp.einsum(
        "twx,xc->twc", route, source, precision=lax.Precision.HIGHEST, preferred_element_type=jnp.float32
    )


def back_rims(received, theirs, back, like, offset):
    res, rank, sides, flips, live = theirs
    size = like.shape[1]
    n_src, width = received.shape[0], received.shape[1]
    hit = res == back[:, None]
    s = jnp.arange(4)[:, None, None, None, None]
    j = jnp.arange(size)[None, :, None, None, None]
    cols = jnp.arange(width) - offset
    q = (cols // size)[None, None, None, :, None]
    jj = (cols % size)[None, None, None, :, None]
    in_edge = ((cols >= 0) & (cols < 2 * size))[None, None, None, :, None]
    e_hit = hit[None, None, :, None, :4]
    e_side = sides[None, None, :, None, :4] == s
    e_rank = rank[None, None, :, None, :] == q
    e_cell = jnp.where(flips[None, None, :, None, :4] == 1, size - 1 - j, j) == jj
    edge = jnp.any(e_hit & e_side & e_rank & e_cell & in_edge, axis=4)
    at = corner_at(flips[:, 4:], size)
    c_slot = (cols - 2 * size)[None, None, None, :, None] == jnp.arange(4)[None, None, None, None, :]
    c_hit = hit[None, None, :, None, 4:] & (sides[None, None, :, None, 4:] == s)
    c_cell = j == at[None, None, :, None, :]
    corner = jnp.any(c_hit & c_cell & c_slot, axis=4)
    route = (edge | corner).reshape(4 * size, n_src * width).astype(jnp.float32)
    flat = jnp.dot(
        route, received.reshape(n_src * width, -1), precision=lax.Precision.HIGHEST,
        preferred_element_type=jnp.float32,
    )
    return to_rows(flat, like)


def add_rims(inner, total):
    inner = inner.at[:, 0].add(total[0]).at[:, -1].add(total[1])
    return inner.at[:, :, 0].add(total[2]).at[:, :, -1].add(total[3])


def xor_swap(value, axis, bit):
    size = lax.axis_size(axis)
    return lax.ppermute(value, axis, [(i, i ^ bit) for i in range(size)])


def halving_stages(axis):
    size = lax.axis_size(axis)
    stages = []
    bit = 1
    while bit < size:
        stages.append((axis, bit))
        bit *= 2
    return stages


def scatter_halves(buf, stages):
    for axis, bit in stages:
        half = buf.shape[0] // 2
        high = (lax.axis_index(axis) & bit) != 0
        low_part, high_part = buf[:half], buf[half:]
        send = jnp.where(high, low_part, high_part)
        keep = jnp.where(high, high_part, low_part)
        buf = keep + xor_swap(send, axis, bit)
    return buf


def gather_halves(buf, stages):
    for axis, bit in reversed(stages):
        high = (lax.axis_index(axis) & bit) != 0
        other = xor_swap(buf, axis, bit)
        buf = jnp.where(high, jnp.concatenate([other, buf]), jnp.concatenate([buf, other]))
    return buf


def all_reduce(flat, axes):
    outer, inner = axes
    for axis in axes:
        size = lax.axis_size(axis)
        if size & (size - 1):
            return lax.psum(flat, axes)
    outer_stages = halving_stages(outer)
    count = lax.axis_size(inner)
    if flat.shape[0] % ((1 << len(outer_stages)) * count):
        return lax.psum(flat, axes)
    if count <= 16:
        near, far = outer_stages[:1], outer_stages[1:]
        buf = scatter_halves(flat, near)
        got = lax.all_to_all(buf.reshape(count, -1), inner, 0, 0)
        part = gather_halves(scatter_halves(jnp.sum(got, axis=0), far), far)
        full = lax.all_to_all(jnp.broadcast_to(part, (count,) + part.shape), inner, 0, 0)
        return gather_halves(full.reshape(-1), near)
    buf = scatter_halves(flat, outer_stages)
    inner_stages = halving_stages(inner)
    buf = gather_halves(scatter_halves(buf, inner_stages), inner_stages)
    return gather_halves(buf, outer_stages)


def gelu_tanh(value):
    return jax.nn.gelu(value, approximate=True)


def shards(
    inputs,
    cotangent,
    weight_first,
    weight_second,
    slot_tile,
    neighbour_tile,
    neighbour_turns,
    corner_live,
):
    count = slot_tile.shape[0]
    devices = lax.axis_size("space")
    me = lax.axis_index("space")
    offs = residues(devices)
    slot_of_tile = (
        jnp.zeros((count,), jnp.int32).at[slot_tile].set(jnp.arange(count, dtype=jnp.int32))
    )
    tables = (slot_tile, slot_of_tile, neighbour_tile, neighbour_turns, corner_live)
    plans = make_plans(tables, devices)
    if devices <= 2 * REACH + 1:
        offs = None
        every = jnp.arange(devices, dtype=jnp.int32)
        resid = (every - me) % devices
        position = (every + me) % devices
        back = (me - every) % devices
        theirs = plans
    else:
        resid = np.array([0] + offs, np.int32)
        position = np.zeros((devices,), np.int32)
        position[resid] = np.arange(len(resid))
        back = jnp.asarray((-resid) % devices)
        theirs = tuple(p[(me + resid) % devices] for p in plans)
    mine = tuple(p[me] for p in plans)

    def trip(pull, push):
        if offs is None:
            arrived = swap_all(pull, push)
            return arrived, arrived, pull.shape[1]
        got_pull, got_push = round_trip(pull, push, offs)
        return got_pull, got_push, 0

    tile = inputs[0]
    cot_tile = cotangent[0]
    samples_all = tile.shape[0] * lax.axis_size("dp") * devices
    scale = 1.0 / math.sqrt(samples_all * tile.shape[1] * tile.shape[2])

    full_second = conv_full(cot_tile, weight_second)
    push_second = push_payloads(full_second, mine, resid)
    got_in, got_second, skip = trip(pull_payloads(tile, theirs, back), push_second)

    padded_in = pad_tile(tile, got_in, mine, position)
    hidden = conv_valid(padded_in, weight_first)
    active = gelu_tanh(hidden).astype(jnp.bfloat16)

    inner_second = full_second[:, 1:-1, 1:-1]
    grad_active = add_rims(inner_second, back_rims(got_second, theirs, back, inner_second, skip))
    _, pull_gelu = jax.vjp(gelu_tanh, hidden)
    grad_hidden = pull_gelu(grad_active)[0].astype(jnp.bfloat16)
    full_first = conv_full(grad_hidden, weight_first)
    push_first = push_payloads(full_first, mine, resid)
    pull_act = pull_payloads(active, theirs, back)
    pull_act, push_first, padded_in, grad_hidden, active = lax.optimization_barrier(
        (pull_act, push_first, padded_in, grad_hidden, active)
    )
    got_act, got_first, skip = trip(pull_act, push_first)
    local_first = weight_grad(padded_in, grad_hidden)
    bulk_second = zero_padded_weight_grad(active, cot_tile)
    got_act, got_first, local_first, bulk_second = lax.optimization_barrier(
        (got_act, got_first, local_first, bulk_second)
    )

    rows_act, corners_act = ring_parts(active, got_act, mine, position)
    local_second = bulk_second + ring_weight_grad(rows_act, corners_act, cot_tile)
    inner_first = full_first[:, 1:-1, 1:-1]
    grad_tile = add_rims(inner_first, back_rims(got_first, theirs, back, inner_first, skip))
    grad_tile = grad_tile.astype(jnp.bfloat16)

    flat = jnp.concatenate([local_first.reshape(-1), local_second.reshape(-1)])
    summed = all_reduce(flat, ("dp", "space"))
    half = local_first.size
    summed_first = summed[:half].reshape(local_first.shape)
    summed_second = summed[half:].reshape(local_second.shape)
    return (grad_tile[None], summed_first * scale, summed_second * scale)


def solution(mesh):
    in_specs = (
        P("space", "dp", None, None, None),
        P("space", "dp", None, None, None),
        P(),
        P(),
        P(),
        P(),
        P(),
        P(),
    )
    out_specs = (P("space", "dp", None, None, None), P(), P())
    return jax.shard_map(shards, mesh=mesh, in_specs=in_specs, out_specs=out_specs, check_vma=False)
```

```python
import math

import jax
import jax.numpy as jnp
import numpy as np
from jax import lax
from jax.sharding import PartitionSpec as P

REACH = 7

NEED_SIDE = (1, 0, 3, 2, 1, 1, 0, 0)


def side_tables():
    one = ((3, 0), (2, 0), (0, 1), (1, 1))
    side = np.zeros((4, 4), np.int32)
    flip = np.zeros((4, 4), np.int32)
    side[0] = np.arange(4)
    for r in range(1, 4):
        for s in range(4):
            s1, f1 = one[s]
            side[r, s] = side[r - 1, s1]
            flip[r, s] = flip[r - 1, s1] ^ f1
    return side, flip


def edge_rims(tile):
    return jnp.stack([tile[:, 0], tile[:, -1], tile[:, :, 0], tile[:, :, -1]])


def residues(devices):
    found = []
    for offset in range(-REACH, REACH + 1):
        res = offset % devices
        if res != 0 and res not in found:
            found.append(res)
    return found


def shift(value, by):
    length = lax.axis_size("space")
    return lax.ppermute(value, "space", [(i, (i + by) % length) for i in range(length)])


def swap_all(pull, push):
    payload = jnp.concatenate([pull.astype(jnp.float32), push], axis=1)
    return lax.all_to_all(payload, "space", 0, 0)


def round_trip(pull, push, offs):
    devices = lax.axis_size("space")
    index = {o: i + 1 for i, o in enumerate(offs)}
    rows = pull.shape[1]
    got_pull = [pull[0]]
    got_push = [push[0]]
    for o in offs:
        back = index[(devices - o) % devices]
        payload = jnp.concatenate([pull[back].astype(jnp.float32), push[back]])
        arrived = lax.ppermute(payload, "space", [(i, (i - o) % devices) for i in range(devices)])
        got_pull.append(arrived[:rows].astype(pull.dtype))
        got_push.append(arrived[rows:])
    return jnp.stack(got_pull), jnp.stack(got_push)


def make_plans(tables, devices):
    slot_tile, slot_of_tile, neighbour_tile, neighbour_turns, corner_live = tables
    slots = jnp.arange(devices, dtype=jnp.int32)
    owners = slot_of_tile[neighbour_tile[slot_tile]]
    res = (owners - slots[:, None]) % devices
    turns = neighbour_turns[slot_tile]
    side_tab, flip_tab = side_tables()
    need = np.array(NEED_SIDE, np.int32)[None, :]
    sides = jnp.asarray(side_tab)[turns, need]
    flips = jnp.asarray(flip_tab)[turns, need]
    edge = res[:, :4]
    earlier = np.tril(np.ones((4, 4), bool), -1)
    rank = jnp.sum((edge[:, :, None] == edge[:, None, :]) & earlier, axis=2)
    return res, rank, sides, flips, corner_live[slot_tile]


def flip_index(flips, size):
    cells = jnp.arange(size, dtype=jnp.int32)[None, :]
    return jnp.where(flips[:, None] == 1, size - 1 - cells, cells)


def assemble(own, top, bottom, left, right, top_left, top_right, bottom_left, bottom_right):
    top_row = jnp.concatenate([top_left[:, None], top, top_right[:, None]], axis=1)
    bottom_row = jnp.concatenate([bottom_left[:, None], bottom, bottom_right[:, None]], axis=1)
    middle = jnp.concatenate([left[:, :, None], own, right[:, :, None]], axis=2)
    return jnp.concatenate([top_row[:, None], middle, bottom_row[:, None]], axis=1)


def corner_at(flips, size):
    ends = np.array([size - 1, 0, size - 1, 0], np.int32)
    return jnp.where(flips == 1, size - 1 - ends, ends)


def to_rows(flat, like):
    size = like.shape[1]
    return flat.reshape((-1, size) + like.shape[:1] + like.shape[3:]).transpose(0, 2, 1, 3)


def from_rows(rims):
    return rims.transpose(0, 2, 1, 3).reshape(rims.shape[0] * rims.shape[2], -1)


def pull_payloads(tile, theirs, back):
    res, rank, sides, flips, live = theirs
    size = tile.shape[1]
    hit = res == back[:, None]
    q = jnp.arange(2)[None, :, None, None]
    s = jnp.arange(4)[None, None, :, None]
    edge = jnp.sum(
        hit[:, None, None, :4] & (rank[:, None, None, :] == q) & (sides[:, None, None, :4] == s), axis=3
    )
    eye = jnp.eye(size, dtype=jnp.bool_)
    edge = (edge[:, :, None, :, None] > 0) & eye[None, None, :, None, :]
    at = corner_at(flips[:, 4:], size)
    corner = (
        hit[:, 4:, None, None]
        & (sides[:, 4:, None, None] == jnp.arange(4)[None, None, :, None])
        & (jnp.arange(size)[None, None, None, :] == at[:, :, None, None])
    )
    count = res.shape[0]
    pick = jnp.concatenate([edge.reshape(count, 2 * size, 4 * size), corner.reshape(count, 4, 4 * size)], axis=1)
    rims = from_rows(edge_rims(tile))
    out = jnp.einsum("twx,xc->twc", pick.astype(tile.dtype), rims, preferred_element_type=jnp.float32)
    return out.astype(tile.dtype)


def ring_parts(tile, received, mine, position):
    res, rank, sides, flips, live = mine
    size = tile.shape[1]
    n_src, width = received.shape[0], received.shape[1]
    src = jnp.asarray(position)[res]
    cells = flip_index(flips[:4], size)
    column = rank[:, None] * size + cells
    edge = (jnp.arange(n_src)[None, None, :, None] == src[:4, None, None, None]) & (
        jnp.arange(width)[None, None, None, :] == column[:, :, None, None]
    )
    corner = (jnp.arange(n_src)[None, :, None] == src[4:, None, None]) & (
        jnp.arange(width)[None, None, :] == (2 * size + jnp.arange(4))[:, None, None]
    )
    pick = jnp.concatenate([edge.reshape(4 * size, n_src * width), corner.reshape(4, n_src * width)])
    flat = jnp.dot(
        pick.astype(received.dtype), received.reshape(n_src * width, -1), precision=lax.Precision.HIGHEST,
        preferred_element_type=jnp.float32,
    )
    flat = flat.astype(tile.dtype)
    rows = to_rows(flat[: 4 * size], tile)
    corners = flat[4 * size :].reshape((4,) + tile.shape[:1] + tile.shape[3:])
    corners = corners * live.astype(tile.dtype)[:, None, None]
    return rows, corners


def pad_tile(tile, received, mine, position):
    rows, corners = ring_parts(tile, received, mine, position)
    return assemble(tile, rows[0], rows[1], rows[2], rows[3], corners[0], corners[1], corners[2], corners[3])


def conv_valid(padded, weight):
    return lax.conv_general_dilated(
        padded,
        weight,
        (1, 1),
        "VALID",
        dimension_numbers=("NHWC", "HWIO", "NHWC"),
        preferred_element_type=jnp.float32,
    )


def conv_full(cot, weight):
    flipped = jnp.flip(weight, (0, 1)).transpose(0, 1, 3, 2)
    return lax.conv_general_dilated(
        cot,
        flipped,
        (1, 1),
        ((2, 2), (2, 2)),
        dimension_numbers=("NHWC", "HWIO", "NHWC"),
        preferred_element_type=jnp.float32,
    )


def weight_grad(padded, cot):
    return lax.conv_general_dilated(
        padded,
        cot,
        (1, 1),
        "VALID",
        dimension_numbers=("CHWN", "IHWO", "HWNC"),
        preferred_element_type=jnp.float32,
    )


def zero_padded_weight_grad(tile, cot):
    return lax.conv_general_dilated(
        tile,
        cot,
        (1, 1),
        ((1, 1), (1, 1)),
        dimension_numbers=("CHWN", "IHWO", "HWNC"),
        preferred_element_type=jnp.float32,
    )


def ring_weight_grad(rows, corners, cot):
    size = cot.shape[1]
    zero = jnp.zeros_like(corners[0])[:, None]
    lines = jnp.stack([
        jnp.concatenate([corners[0][:, None], rows[0], corners[1][:, None]], axis=1),
        jnp.concatenate([corners[2][:, None], rows[1], corners[3][:, None]], axis=1),
        jnp.concatenate([zero, rows[2], zero], axis=1),
        jnp.concatenate([zero, rows[3], zero], axis=1),
    ])
    windows = jnp.stack([lines[:, :, t : t + size] for t in range(3)], axis=1)
    edges = jnp.stack([cot[:, 0], cot[:, -1], cot[:, :, 0], cot[:, :, -1]])
    taps = jnp.einsum("ktbjc,kbjd->ktcd", windows, edges, preferred_element_type=jnp.float32)
    grid = jnp.zeros((3, 3) + taps.shape[2:], jnp.float32)
    grid = grid.at[0, :].add(taps[0]).at[2, :].add(taps[1])
    return grid.at[:, 0].add(taps[2]).at[:, 2].add(taps[3])


def push_payloads(full, mine, resid):
    res, rank, sides, flips, live = mine
    size = full.shape[1] - 2
    rows = jnp.stack([full[:, 0, 1:-1], full[:, -1, 1:-1], full[:, 1:-1, 0], full[:, 1:-1, -1]])
    values = jnp.stack([full[:, 0, 0], full[:, 0, -1], full[:, -1, 0], full[:, -1, -1]])
    values = values * live.astype(jnp.float32)[:, None, None]
    source = jnp.concatenate([from_rows(rows), values.reshape(4, -1)])
    hit = res[None, :] == jnp.asarray(resid)[:, None]
    count = resid.shape[0]
    edge = hit[:, None, :4] & (rank[None, None, :] == jnp.arange(2)[None, :, None])
    eye = jnp.eye(size, dtype=jnp.bool_)
    edge = edge[:, :, None, :, None] & eye[None, None, :, None, :]
    edge = jnp.concatenate(
        [edge.reshape(count, 2 * size, 4 * size), jnp.zeros((count, 2 * size, 4), jnp.bool_)], axis=2
    )
    corner = hit[:, 4:, None] & jnp.eye(4, dtype=jnp.bool_)[None]
    corner = jnp.concatenate([jnp.zeros((count, 4, 4 * size), jnp.bool_), corner], axis=2)
    route = jnp.concatenate([edge, corner], axis=1).astype(jnp.float32)
    return jnp.einsum(
        "twx,xc->twc", route, source, precision=lax.Precision.HIGHEST, preferred_element_type=jnp.float32
    )


def back_rims(received, theirs, back, like, offset):
    res, rank, sides, flips, live = theirs
    size = like.shape[1]
    n_src, width = received.shape[0], received.shape[1]
    hit = res == back[:, None]
    s = jnp.arange(4)[:, None, None, None, None]
    j = jnp.arange(size)[None, :, None, None, None]
    cols = jnp.arange(width) - offset
    q = (cols // size)[None, None, None, :, None]
    jj = (cols % size)[None, None, None, :, None]
    in_edge = ((cols >= 0) & (cols < 2 * size))[None, None, None, :, None]
    e_hit = hit[None, None, :, None, :4]
    e_side = sides[None, None, :, None, :4] == s
    e_rank = rank[None, None, :, None, :] == q
    e_cell = jnp.where(flips[None, None, :, None, :4] == 1, size - 1 - j, j) == jj
    edge = jnp.any(e_hit & e_side & e_rank & e_cell & in_edge, axis=4)
    at = corner_at(flips[:, 4:], size)
    c_slot = (cols - 2 * size)[None, None, None, :, None] == jnp.arange(4)[None, None, None, None, :]
    c_hit = hit[None, None, :, None, 4:] & (sides[None, None, :, None, 4:] == s)
    c_cell = j == at[None, None, :, None, :]
    corner = jnp.any(c_hit & c_cell & c_slot, axis=4)
    route = (edge | corner).reshape(4 * size, n_src * width).astype(jnp.float32)
    flat = jnp.dot(
        route, received.reshape(n_src * width, -1), precision=lax.Precision.HIGHEST,
        preferred_element_type=jnp.float32,
    )
    return to_rows(flat, like)


def add_rims(inner, total):
    inner = inner.at[:, 0].add(total[0]).at[:, -1].add(total[1])
    return inner.at[:, :, 0].add(total[2]).at[:, :, -1].add(total[3])


def xor_swap(value, axis, bit):
    size = lax.axis_size(axis)
    return lax.ppermute(value, axis, [(i, i ^ bit) for i in range(size)])


def halving_stages(axis):
    size = lax.axis_size(axis)
    stages = []
    bit = 1
    while bit < size:
        stages.append((axis, bit))
        bit *= 2
    return stages


def scatter_halves(buf, stages):
    for axis, bit in stages:
        half = buf.shape[0] // 2
        high = (lax.axis_index(axis) & bit) != 0
        low_part, high_part = buf[:half], buf[half:]
        send = jnp.where(high, low_part, high_part)
        keep = jnp.where(high, high_part, low_part)
        buf = keep + xor_swap(send, axis, bit)
    return buf


def gather_halves(buf, stages):
    for axis, bit in reversed(stages):
        high = (lax.axis_index(axis) & bit) != 0
        other = xor_swap(buf, axis, bit)
        buf = jnp.where(high, jnp.concatenate([other, buf]), jnp.concatenate([buf, other]))
    return buf


def all_reduce(flat, axes):
    outer, inner = axes
    for axis in axes:
        size = lax.axis_size(axis)
        if size & (size - 1):
            return lax.psum(flat, axes)
    outer_stages = halving_stages(outer)
    count = lax.axis_size(inner)
    if flat.shape[0] % ((1 << len(outer_stages)) * count):
        return lax.psum(flat, axes)
    buf = scatter_halves(flat, outer_stages)
    if count <= 16:
        got = lax.all_to_all(buf.reshape(count, -1), inner, 0, 0)
        part = jnp.sum(got, axis=0)
        full = lax.all_to_all(jnp.broadcast_to(part, (count,) + part.shape), inner, 0, 0)
        buf = full.reshape(-1)
    else:
        inner_stages = halving_stages(inner)
        buf = gather_halves(scatter_halves(buf, inner_stages), inner_stages)
    return gather_halves(buf, outer_stages)


def gelu_tanh(value):
    return jax.nn.gelu(value, approximate=True)


def shards(
    inputs,
    cotangent,
    weight_first,
    weight_second,
    slot_tile,
    neighbour_tile,
    neighbour_turns,
    corner_live,
):
    count = slot_tile.shape[0]
    devices = lax.axis_size("space")
    me = lax.axis_index("space")
    offs = residues(devices)
    slot_of_tile = (
        jnp.zeros((count,), jnp.int32).at[slot_tile].set(jnp.arange(count, dtype=jnp.int32))
    )
    tables = (slot_tile, slot_of_tile, neighbour_tile, neighbour_turns, corner_live)
    plans = make_plans(tables, devices)
    if devices <= 2 * REACH + 1:
        offs = None
        every = jnp.arange(devices, dtype=jnp.int32)
        resid = (every - me) % devices
        position = (every + me) % devices
        back = (me - every) % devices
        theirs = plans
    else:
        resid = np.array([0] + offs, np.int32)
        position = np.zeros((devices,), np.int32)
        position[resid] = np.arange(len(resid))
        back = jnp.asarray((-resid) % devices)
        theirs = tuple(p[(me + resid) % devices] for p in plans)
    mine = tuple(p[me] for p in plans)

    def trip(pull, push):
        if offs is None:
            arrived = swap_all(pull, push)
            return arrived, arrived, pull.shape[1]
        got_pull, got_push = round_trip(pull, push, offs)
        return got_pull, got_push, 0

    tile = inputs[0]
    cot_tile = cotangent[0]
    samples_all = tile.shape[0] * lax.axis_size("dp") * devices
    scale = 1.0 / math.sqrt(samples_all * tile.shape[1] * tile.shape[2])

    full_second = conv_full(cot_tile, weight_second)
    push_second = push_payloads(full_second, mine, resid)
    got_in, got_second, skip = trip(pull_payloads(tile, theirs, back), push_second)

    padded_in = pad_tile(tile, got_in, mine, position)
    hidden = conv_valid(padded_in, weight_first)
    active = gelu_tanh(hidden).astype(jnp.bfloat16)

    inner_second = full_second[:, 1:-1, 1:-1]
    grad_active = add_rims(inner_second, back_rims(got_second, theirs, back, inner_second, skip))
    _, pull_gelu = jax.vjp(gelu_tanh, hidden)
    grad_hidden = pull_gelu(grad_active)[0].astype(jnp.bfloat16)
    full_first = conv_full(grad_hidden, weight_first)
    push_first = push_payloads(full_first, mine, resid)
    pull_act = pull_payloads(active, theirs, back)
    pull_act, push_first, padded_in, grad_hidden, active = lax.optimization_barrier(
        (pull_act, push_first, padded_in, grad_hidden, active)
    )
    got_act, got_first, skip = trip(pull_act, push_first)
    local_first = weight_grad(padded_in, grad_hidden)
    bulk_second = zero_padded_weight_grad(active, cot_tile)
    got_act, got_first, local_first, bulk_second = lax.optimization_barrier(
        (got_act, got_first, local_first, bulk_second)
    )

    rows_act, corners_act = ring_parts(active, got_act, mine, position)
    local_second = bulk_second + ring_weight_grad(rows_act, corners_act, cot_tile)
    inner_first = full_first[:, 1:-1, 1:-1]
    grad_tile = add_rims(inner_first, back_rims(got_first, theirs, back, inner_first, skip))
    grad_tile = grad_tile.astype(jnp.bfloat16)

    flat = jnp.concatenate([local_first.reshape(-1), local_second.reshape(-1)]) * scale
    summed = all_reduce(flat, ("dp", "space"))
    half = local_first.size
    summed_first = summed[:half].reshape(local_first.shape)
    summed_second = summed[half:].reshape(local_second.shape)
    return (grad_tile[None], summed_first, summed_second)


def solution(mesh):
    in_specs = (
        P("space", "dp", None, None, None),
        P("space", "dp", None, None, None),
        P(),
        P(),
        P(),
        P(),
        P(),
        P(),
    )
    out_specs = (P("space", "dp", None, None, None), P(), P())
    return jax.shard_map(shards, mesh=mesh, in_specs=in_specs, out_specs=out_specs, check_vma=False)
```

```python
import math

import jax
import jax.numpy as jnp
import numpy as np
from jax import lax
from jax.sharding import PartitionSpec as P

REACH = 7

NEED_SIDE = (1, 0, 3, 2, 1, 1, 0, 0)


def side_tables():
    one = ((3, 0), (2, 0), (0, 1), (1, 1))
    side = np.zeros((4, 4), np.int32)
    flip = np.zeros((4, 4), np.int32)
    side[0] = np.arange(4)
    for r in range(1, 4):
        for s in range(4):
            s1, f1 = one[s]
            side[r, s] = side[r - 1, s1]
            flip[r, s] = flip[r - 1, s1] ^ f1
    return side, flip


def edge_rims(tile):
    return jnp.stack([tile[:, 0], tile[:, -1], tile[:, :, 0], tile[:, :, -1]])


def residues(devices):
    found = []
    for offset in range(-REACH, REACH + 1):
        res = offset % devices
        if res != 0 and res not in found:
            found.append(res)
    return found


def shift(value, by):
    length = lax.axis_size("space")
    return lax.ppermute(value, "space", [(i, (i + by) % length) for i in range(length)])


def swap_all(pull, push):
    payload = jnp.concatenate([pull.astype(jnp.float32), push], axis=1)
    return lax.all_to_all(payload, "space", 0, 0)


def round_trip(pull, push, offs):
    devices = lax.axis_size("space")
    index = {o: i + 1 for i, o in enumerate(offs)}
    rows = pull.shape[1]
    got_pull = [pull[0]]
    got_push = [push[0]]
    for o in offs:
        back = index[(devices - o) % devices]
        payload = jnp.concatenate([pull[back].astype(jnp.float32), push[back]])
        arrived = lax.ppermute(payload, "space", [(i, (i - o) % devices) for i in range(devices)])
        got_pull.append(arrived[:rows].astype(pull.dtype))
        got_push.append(arrived[rows:])
    return jnp.stack(got_pull), jnp.stack(got_push)


def make_plans(tables, devices):
    slot_tile, slot_of_tile, neighbour_tile, neighbour_turns, corner_live = tables
    slots = jnp.arange(devices, dtype=jnp.int32)
    owners = slot_of_tile[neighbour_tile[slot_tile]]
    res = (owners - slots[:, None]) % devices
    turns = neighbour_turns[slot_tile]
    side_tab, flip_tab = side_tables()
    need = np.array(NEED_SIDE, np.int32)[None, :]
    sides = jnp.asarray(side_tab)[turns, need]
    flips = jnp.asarray(flip_tab)[turns, need]
    edge = res[:, :4]
    earlier = np.tril(np.ones((4, 4), bool), -1)
    rank = jnp.sum((edge[:, :, None] == edge[:, None, :]) & earlier, axis=2)
    return res, rank, sides, flips, corner_live[slot_tile]


def flip_index(flips, size):
    cells = jnp.arange(size, dtype=jnp.int32)[None, :]
    return jnp.where(flips[:, None] == 1, size - 1 - cells, cells)


def assemble(own, top, bottom, left, right, top_left, top_right, bottom_left, bottom_right):
    top_row = jnp.concatenate([top_left[:, None], top, top_right[:, None]], axis=1)
    bottom_row = jnp.concatenate([bottom_left[:, None], bottom, bottom_right[:, None]], axis=1)
    middle = jnp.concatenate([left[:, :, None], own, right[:, :, None]], axis=2)
    return jnp.concatenate([top_row[:, None], middle, bottom_row[:, None]], axis=1)


def corner_at(flips, size):
    ends = np.array([size - 1, 0, size - 1, 0], np.int32)
    return jnp.where(flips == 1, size - 1 - ends, ends)


def to_rows(flat, like):
    size = like.shape[1]
    return flat.reshape((-1, size) + like.shape[:1] + like.shape[3:]).transpose(0, 2, 1, 3)


def from_rows(rims):
    return rims.transpose(0, 2, 1, 3).reshape(rims.shape[0] * rims.shape[2], -1)


def pull_payloads(tile, theirs, back):
    res, rank, sides, flips, live = theirs
    size = tile.shape[1]
    hit = res == back[:, None]
    q = jnp.arange(2)[None, :, None, None]
    s = jnp.arange(4)[None, None, :, None]
    edge = jnp.sum(
        hit[:, None, None, :4] & (rank[:, None, None, :] == q) & (sides[:, None, None, :4] == s), axis=3
    )
    eye = jnp.eye(size, dtype=jnp.bool_)
    edge = (edge[:, :, None, :, None] > 0) & eye[None, None, :, None, :]
    at = corner_at(flips[:, 4:], size)
    corner = (
        hit[:, 4:, None, None]
        & (sides[:, 4:, None, None] == jnp.arange(4)[None, None, :, None])
        & (jnp.arange(size)[None, None, None, :] == at[:, :, None, None])
    )
    count = res.shape[0]
    pick = jnp.concatenate([edge.reshape(count, 2 * size, 4 * size), corner.reshape(count, 4, 4 * size)], axis=1)
    rims = from_rows(edge_rims(tile))
    out = jnp.einsum("twx,xc->twc", pick.astype(tile.dtype), rims, preferred_element_type=jnp.float32)
    return out.astype(tile.dtype)


def ring_parts(tile, received, mine, position):
    res, rank, sides, flips, live = mine
    size = tile.shape[1]
    n_src, width = received.shape[0], received.shape[1]
    src = jnp.asarray(position)[res]
    cells = flip_index(flips[:4], size)
    column = rank[:, None] * size + cells
    edge = (jnp.arange(n_src)[None, None, :, None] == src[:4, None, None, None]) & (
        jnp.arange(width)[None, None, None, :] == column[:, :, None, None]
    )
    corner = (jnp.arange(n_src)[None, :, None] == src[4:, None, None]) & (
        jnp.arange(width)[None, None, :] == (2 * size + jnp.arange(4))[:, None, None]
    )
    pick = jnp.concatenate([edge.reshape(4 * size, n_src * width), corner.reshape(4, n_src * width)])
    flat = jnp.dot(
        pick.astype(received.dtype), received.reshape(n_src * width, -1), precision=lax.Precision.DEFAULT,
        preferred_element_type=jnp.float32,
    )
    flat = flat.astype(tile.dtype)
    rows = to_rows(flat[: 4 * size], tile)
    corners = flat[4 * size :].reshape((4,) + tile.shape[:1] + tile.shape[3:])
    corners = corners * live.astype(tile.dtype)[:, None, None]
    return rows, corners


def pad_tile(tile, received, mine, position):
    rows, corners = ring_parts(tile, received, mine, position)
    return assemble(tile, rows[0], rows[1], rows[2], rows[3], corners[0], corners[1], corners[2], corners[3])


def conv_valid(padded, weight):
    return lax.conv_general_dilated(
        padded,
        weight,
        (1, 1),
        "VALID",
        dimension_numbers=("NHWC", "HWIO", "NHWC"),
        preferred_element_type=jnp.float32,
    )


def conv_full(cot, weight):
    flipped = jnp.flip(weight, (0, 1)).transpose(0, 1, 3, 2)
    return lax.conv_general_dilated(
        cot,
        flipped,
        (1, 1),
        ((2, 2), (2, 2)),
        dimension_numbers=("NHWC", "HWIO", "NHWC"),
        preferred_element_type=jnp.float32,
    )


def weight_grad(padded, cot):
    return lax.conv_general_dilated(
        padded,
        cot,
        (1, 1),
        "VALID",
        dimension_numbers=("CHWN", "IHWO", "HWNC"),
        preferred_element_type=jnp.float32,
    )


def zero_padded_weight_grad(tile, cot):
    return lax.conv_general_dilated(
        tile,
        cot,
        (1, 1),
        ((1, 1), (1, 1)),
        dimension_numbers=("CHWN", "IHWO", "HWNC"),
        preferred_element_type=jnp.float32,
    )


def ring_weight_grad(rows, corners, cot):
    size = cot.shape[1]
    zero = jnp.zeros_like(corners[0])[:, None]
    lines = jnp.stack([
        jnp.concatenate([corners[0][:, None], rows[0], corners[1][:, None]], axis=1),
        jnp.concatenate([corners[2][:, None], rows[1], corners[3][:, None]], axis=1),
        jnp.concatenate([zero, rows[2], zero], axis=1),
        jnp.concatenate([zero, rows[3], zero], axis=1),
    ])
    windows = jnp.stack([lines[:, :, t : t + size] for t in range(3)], axis=1)
    edges = jnp.stack([cot[:, 0], cot[:, -1], cot[:, :, 0], cot[:, :, -1]])
    taps = jnp.einsum("ktbjc,kbjd->ktcd", windows, edges, preferred_element_type=jnp.float32)
    grid = jnp.zeros((3, 3) + taps.shape[2:], jnp.float32)
    grid = grid.at[0, :].add(taps[0]).at[2, :].add(taps[1])
    return grid.at[:, 0].add(taps[2]).at[:, 2].add(taps[3])


def push_payloads(full, mine, resid):
    res, rank, sides, flips, live = mine
    size = full.shape[1] - 2
    rows = jnp.stack([full[:, 0, 1:-1], full[:, -1, 1:-1], full[:, 1:-1, 0], full[:, 1:-1, -1]])
    values = jnp.stack([full[:, 0, 0], full[:, 0, -1], full[:, -1, 0], full[:, -1, -1]])
    values = values * live.astype(jnp.float32)[:, None, None]
    source = jnp.concatenate([from_rows(rows), values.reshape(4, -1)])
    hit = res[None, :] == jnp.asarray(resid)[:, None]
    count = resid.shape[0]
    edge = hit[:, None, :4] & (rank[None, None, :] == jnp.arange(2)[None, :, None])
    eye = jnp.eye(size, dtype=jnp.bool_)
    edge = edge[:, :, None, :, None] & eye[None, None, :, None, :]
    edge = jnp.concatenate(
        [edge.reshape(count, 2 * size, 4 * size), jnp.zeros((count, 2 * size, 4), jnp.bool_)], axis=2
    )
    corner = hit[:, 4:, None] & jnp.eye(4, dtype=jnp.bool_)[None]
    corner = jnp.concatenate([jnp.zeros((count, 4, 4 * size), jnp.bool_), corner], axis=2)
    route = jnp.concatenate([edge, corner], axis=1).astype(jnp.float32)
    return jnp.einsum(
        "twx,xc->twc", route, source, precision=lax.Precision.HIGHEST, preferred_element_type=jnp.float32
    )


def back_rims(received, theirs, back, like, offset):
    res, rank, sides, flips, live = theirs
    size = like.shape[1]
    n_src, width = received.shape[0], received.shape[1]
    hit = res == back[:, None]
    s = jnp.arange(4)[:, None, None, None, None]
    j = jnp.arange(size)[None, :, None, None, None]
    cols = jnp.arange(width) - offset
    q = (cols // size)[None, None, None, :, None]
    jj = (cols % size)[None, None, None, :, None]
    in_edge = ((cols >= 0) & (cols < 2 * size))[None, None, None, :, None]
    e_hit = hit[None, None, :, None, :4]
    e_side = sides[None, None, :, None, :4] == s
    e_rank = rank[None, None, :, None, :] == q
    e_cell = jnp.where(flips[None, None, :, None, :4] == 1, size - 1 - j, j) == jj
    edge = jnp.any(e_hit & e_side & e_rank & e_cell & in_edge, axis=4)
    at = corner_at(flips[:, 4:], size)
    c_slot = (cols - 2 * size)[None, None, None, :, None] == jnp.arange(4)[None, None, None, None, :]
    c_hit = hit[None, None, :, None, 4:] & (sides[None, None, :, None, 4:] == s)
    c_cell = j == at[None, None, :, None, :]
    corner = jnp.any(c_hit & c_cell & c_slot, axis=4)
    route = (edge | corner).reshape(4 * size, n_src * width).astype(jnp.float32)
    flat = jnp.dot(
        route, received.reshape(n_src * width, -1), precision=lax.Precision.HIGHEST,
        preferred_element_type=jnp.float32,
    )
    return to_rows(flat, like)


def add_rims(inner, total):
    inner = inner.at[:, 0].add(total[0]).at[:, -1].add(total[1])
    return inner.at[:, :, 0].add(total[2]).at[:, :, -1].add(total[3])


def xor_swap(value, axis, bit):
    size = lax.axis_size(axis)
    return lax.ppermute(value, axis, [(i, i ^ bit) for i in range(size)])


def halving_stages(axis):
    size = lax.axis_size(axis)
    stages = []
    bit = 1
    while bit < size:
        stages.append((axis, bit))
        bit *= 2
    return stages


def scatter_halves(buf, stages):
    for axis, bit in stages:
        half = buf.shape[0] // 2
        high = (lax.axis_index(axis) & bit) != 0
        low_part, high_part = buf[:half], buf[half:]
        send = jnp.where(high, low_part, high_part)
        keep = jnp.where(high, high_part, low_part)
        buf = keep + xor_swap(send, axis, bit)
    return buf


def gather_halves(buf, stages):
    for axis, bit in reversed(stages):
        high = (lax.axis_index(axis) & bit) != 0
        other = xor_swap(buf, axis, bit)
        buf = jnp.where(high, jnp.concatenate([other, buf]), jnp.concatenate([buf, other]))
    return buf


def all_reduce(flat, axes):
    outer, inner = axes
    for axis in axes:
        size = lax.axis_size(axis)
        if size & (size - 1):
            return lax.psum(flat, axes)
    outer_stages = halving_stages(outer)
    count = lax.axis_size(inner)
    if flat.shape[0] % ((1 << len(outer_stages)) * count):
        return lax.psum(flat, axes)
    buf = scatter_halves(flat, outer_stages)
    if count <= 16:
        got = lax.all_to_all(buf.reshape(count, -1), inner, 0, 0)
        part = jnp.sum(got, axis=0)
        full = lax.all_to_all(jnp.broadcast_to(part, (count,) + part.shape), inner, 0, 0)
        buf = full.reshape(-1)
    else:
        inner_stages = halving_stages(inner)
        buf = gather_halves(scatter_halves(buf, inner_stages), inner_stages)
    return gather_halves(buf, outer_stages)


def gelu_tanh(value):
    return jax.nn.gelu(value, approximate=True)


def shards(
    inputs,
    cotangent,
    weight_first,
    weight_second,
    slot_tile,
    neighbour_tile,
    neighbour_turns,
    corner_live,
):
    count = slot_tile.shape[0]
    devices = lax.axis_size("space")
    me = lax.axis_index("space")
    offs = residues(devices)
    slot_of_tile = (
        jnp.zeros((count,), jnp.int32).at[slot_tile].set(jnp.arange(count, dtype=jnp.int32))
    )
    tables = (slot_tile, slot_of_tile, neighbour_tile, neighbour_turns, corner_live)
    plans = make_plans(tables, devices)
    if devices <= 2 * REACH + 1:
        offs = None
        every = jnp.arange(devices, dtype=jnp.int32)
        resid = (every - me) % devices
        position = (every + me) % devices
        back = (me - every) % devices
        theirs = plans
    else:
        resid = np.array([0] + offs, np.int32)
        position = np.zeros((devices,), np.int32)
        position[resid] = np.arange(len(resid))
        back = jnp.asarray((-resid) % devices)
        theirs = tuple(p[(me + resid) % devices] for p in plans)
    mine = tuple(p[me] for p in plans)

    def trip(pull, push):
        if offs is None:
            arrived = swap_all(pull, push)
            return arrived, arrived, pull.shape[1]
        got_pull, got_push = round_trip(pull, push, offs)
        return got_pull, got_push, 0

    tile = inputs[0]
    cot_tile = cotangent[0]
    samples_all = tile.shape[0] * lax.axis_size("dp") * devices
    scale = 1.0 / math.sqrt(samples_all * tile.shape[1] * tile.shape[2])

    full_second = conv_full(cot_tile, weight_second)
    push_second = push_payloads(full_second, mine, resid)
    got_in, got_second, skip = trip(pull_payloads(tile, theirs, back), push_second)

    padded_in = pad_tile(tile, got_in, mine, position)
    hidden = conv_valid(padded_in, weight_first)
    active = gelu_tanh(hidden).astype(jnp.bfloat16)

    inner_second = full_second[:, 1:-1, 1:-1]
    grad_active = add_rims(inner_second, back_rims(got_second, theirs, back, inner_second, skip))
    _, pull_gelu = jax.vjp(gelu_tanh, hidden)
    grad_hidden = pull_gelu(grad_active)[0].astype(jnp.bfloat16)
    full_first = conv_full(grad_hidden, weight_first)
    push_first = push_payloads(full_first, mine, resid)
    pull_act = pull_payloads(active, theirs, back)
    pull_act, push_first, padded_in, grad_hidden, active = lax.optimization_barrier(
        (pull_act, push_first, padded_in, grad_hidden, active)
    )
    got_act, got_first, skip = trip(pull_act, push_first)
    local_first = weight_grad(padded_in, grad_hidden)
    bulk_second = zero_padded_weight_grad(active, cot_tile)
    got_act, got_first, local_first, bulk_second = lax.optimization_barrier(
        (got_act, got_first, local_first, bulk_second)
    )

    rows_act, corners_act = ring_parts(active, got_act, mine, position)
    local_second = bulk_second + ring_weight_grad(rows_act, corners_act, cot_tile)
    inner_first = full_first[:, 1:-1, 1:-1]
    grad_tile = add_rims(inner_first, back_rims(got_first, theirs, back, inner_first, skip))
    grad_tile = grad_tile.astype(jnp.bfloat16)

    flat = jnp.concatenate([local_first.reshape(-1), local_second.reshape(-1)]) * scale
    summed = all_reduce(flat, ("dp", "space"))
    half = local_first.size
    summed_first = summed[:half].reshape(local_first.shape)
    summed_second = summed[half:].reshape(local_second.shape)
    return (grad_tile[None], summed_first, summed_second)


def solution(mesh):
    in_specs = (
        P("space", "dp", None, None, None),
        P("space", "dp", None, None, None),
        P(),
        P(),
        P(),
        P(),
        P(),
        P(),
    )
    out_specs = (P("space", "dp", None, None, None), P(), P())
    return jax.shard_map(shards, mesh=mesh, in_specs=in_specs, out_specs=out_specs, check_vma=False)
```

```python
import math

import jax
import jax.numpy as jnp
import numpy as np
from jax import lax
from jax.sharding import PartitionSpec as P

REACH = 7

NEED_SIDE = (1, 0, 3, 2, 1, 1, 0, 0)


def side_tables():
    one = ((3, 0), (2, 0), (0, 1), (1, 1))
    side = np.zeros((4, 4), np.int32)
    flip = np.zeros((4, 4), np.int32)
    side[0] = np.arange(4)
    for r in range(1, 4):
        for s in range(4):
            s1, f1 = one[s]
            side[r, s] = side[r - 1, s1]
            flip[r, s] = flip[r - 1, s1] ^ f1
    return side, flip


def edge_rims(tile):
    return jnp.stack([tile[:, 0], tile[:, -1], tile[:, :, 0], tile[:, :, -1]])


def residues(devices):
    found = []
    for offset in range(-REACH, REACH + 1):
        res = offset % devices
        if res != 0 and res not in found:
            found.append(res)
    return found


def shift(value, by):
    length = lax.axis_size("space")
    return lax.ppermute(value, "space", [(i, (i + by) % length) for i in range(length)])


def swap_all(pull, push):
    payload = jnp.concatenate([pull.astype(jnp.float32), push], axis=1)
    return lax.all_to_all(payload, "space", 0, 0)


def round_trip(pull, push, offs):
    devices = lax.axis_size("space")
    index = {o: i + 1 for i, o in enumerate(offs)}
    rows = pull.shape[1]
    got_pull = [pull[0]]
    got_push = [push[0]]
    for o in offs:
        back = index[(devices - o) % devices]
        payload = jnp.concatenate([pull[back].astype(jnp.float32), push[back]])
        arrived = lax.ppermute(payload, "space", [(i, (i - o) % devices) for i in range(devices)])
        got_pull.append(arrived[:rows].astype(pull.dtype))
        got_push.append(arrived[rows:])
    return jnp.stack(got_pull), jnp.stack(got_push)


def make_plans(tables, devices):
    slot_tile, slot_of_tile, neighbour_tile, neighbour_turns, corner_live = tables
    slots = jnp.arange(devices, dtype=jnp.int32)
    owners = slot_of_tile[neighbour_tile[slot_tile]]
    res = (owners - slots[:, None]) % devices
    turns = neighbour_turns[slot_tile]
    side_tab, flip_tab = side_tables()
    need = np.array(NEED_SIDE, np.int32)[None, :]
    sides = jnp.asarray(side_tab)[turns, need]
    flips = jnp.asarray(flip_tab)[turns, need]
    edge = res[:, :4]
    earlier = np.tril(np.ones((4, 4), bool), -1)
    rank = jnp.sum((edge[:, :, None] == edge[:, None, :]) & earlier, axis=2)
    return res, rank, sides, flips, corner_live[slot_tile]


def flip_index(flips, size):
    cells = jnp.arange(size, dtype=jnp.int32)[None, :]
    return jnp.where(flips[:, None] == 1, size - 1 - cells, cells)


def assemble(own, top, bottom, left, right, top_left, top_right, bottom_left, bottom_right):
    top_row = jnp.concatenate([top_left[:, None], top, top_right[:, None]], axis=1)
    bottom_row = jnp.concatenate([bottom_left[:, None], bottom, bottom_right[:, None]], axis=1)
    middle = jnp.concatenate([left[:, :, None], own, right[:, :, None]], axis=2)
    return jnp.concatenate([top_row[:, None], middle, bottom_row[:, None]], axis=1)


def corner_at(flips, size):
    ends = np.array([size - 1, 0, size - 1, 0], np.int32)
    return jnp.where(flips == 1, size - 1 - ends, ends)


def to_rows(flat, like):
    size = like.shape[1]
    return flat.reshape((-1, size) + like.shape[:1] + like.shape[3:]).transpose(0, 2, 1, 3)


def from_rows(rims):
    return rims.transpose(0, 2, 1, 3).reshape(rims.shape[0] * rims.shape[2], -1)


def pull_payloads(tile, theirs, back):
    res, rank, sides, flips, live = theirs
    size = tile.shape[1]
    hit = res == back[:, None]
    q = jnp.arange(2)[None, :, None, None]
    s = jnp.arange(4)[None, None, :, None]
    edge = jnp.sum(
        hit[:, None, None, :4] & (rank[:, None, None, :] == q) & (sides[:, None, None, :4] == s), axis=3
    )
    eye = jnp.eye(size, dtype=jnp.bool_)
    edge = (edge[:, :, None, :, None] > 0) & eye[None, None, :, None, :]
    at = corner_at(flips[:, 4:], size)
    corner = (
        hit[:, 4:, None, None]
        & (sides[:, 4:, None, None] == jnp.arange(4)[None, None, :, None])
        & (jnp.arange(size)[None, None, None, :] == at[:, :, None, None])
    )
    count = res.shape[0]
    pick = jnp.concatenate([edge.reshape(count, 2 * size, 4 * size), corner.reshape(count, 4, 4 * size)], axis=1)
    rims = from_rows(edge_rims(tile))
    out = jnp.einsum("twx,xc->twc", pick.astype(tile.dtype), rims, preferred_element_type=jnp.float32)
    return out.astype(tile.dtype)


def ring_parts(tile, received, mine, position):
    res, rank, sides, flips, live = mine
    size = tile.shape[1]
    n_src, width = received.shape[0], received.shape[1]
    src = jnp.asarray(position)[res]
    cells = flip_index(flips[:4], size)
    column = rank[:, None] * size + cells
    edge = (jnp.arange(n_src)[None, None, :, None] == src[:4, None, None, None]) & (
        jnp.arange(width)[None, None, None, :] == column[:, :, None, None]
    )
    corner = (jnp.arange(n_src)[None, :, None] == src[4:, None, None]) & (
        jnp.arange(width)[None, None, :] == (2 * size + jnp.arange(4))[:, None, None]
    )
    pick = jnp.concatenate([edge.reshape(4 * size, n_src * width), corner.reshape(4, n_src * width)])
    flat = jnp.dot(
        pick.astype(received.dtype), received.reshape(n_src * width, -1), precision=lax.Precision.DEFAULT,
        preferred_element_type=jnp.float32,
    )
    flat = flat.astype(tile.dtype)
    rows = to_rows(flat[: 4 * size], tile)
    corners = flat[4 * size :].reshape((4,) + tile.shape[:1] + tile.shape[3:])
    corners = corners * live.astype(tile.dtype)[:, None, None]
    return rows, corners


def pad_tile(tile, received, mine, position):
    rows, corners = ring_parts(tile, received, mine, position)
    return assemble(tile, rows[0], rows[1], rows[2], rows[3], corners[0], corners[1], corners[2], corners[3])


def conv_valid(padded, weight):
    return lax.conv_general_dilated(
        padded,
        weight,
        (1, 1),
        "VALID",
        dimension_numbers=("NHWC", "HWIO", "NHWC"),
        preferred_element_type=jnp.float32,
    )


def conv_full(cot, weight):
    flipped = jnp.flip(weight, (0, 1)).transpose(0, 1, 3, 2)
    return lax.conv_general_dilated(
        cot,
        flipped,
        (1, 1),
        ((2, 2), (2, 2)),
        dimension_numbers=("NHWC", "HWIO", "NHWC"),
        preferred_element_type=jnp.float32,
    )


def weight_grad(padded, cot):
    return lax.conv_general_dilated(
        padded,
        cot,
        (1, 1),
        "VALID",
        dimension_numbers=("CHWN", "IHWO", "HWNC"),
        preferred_element_type=jnp.float32,
    )


def zero_padded_weight_grad(tile, cot):
    return lax.conv_general_dilated(
        tile,
        cot,
        (1, 1),
        ((1, 1), (1, 1)),
        dimension_numbers=("CHWN", "IHWO", "HWNC"),
        preferred_element_type=jnp.float32,
    )


def ring_weight_grad(rows, corners, cot):
    size = cot.shape[1]
    zero = jnp.zeros_like(corners[0])[:, None]
    lines = jnp.stack([
        jnp.concatenate([corners[0][:, None], rows[0], corners[1][:, None]], axis=1),
        jnp.concatenate([corners[2][:, None], rows[1], corners[3][:, None]], axis=1),
        jnp.concatenate([zero, rows[2], zero], axis=1),
        jnp.concatenate([zero, rows[3], zero], axis=1),
    ])
    windows = jnp.stack([lines[:, :, t : t + size] for t in range(3)], axis=1)
    edges = jnp.stack([cot[:, 0], cot[:, -1], cot[:, :, 0], cot[:, :, -1]])
    taps = jnp.einsum("ktbjc,kbjd->ktcd", windows, edges, preferred_element_type=jnp.float32)
    grid = jnp.zeros((3, 3) + taps.shape[2:], jnp.float32)
    grid = grid.at[0, :].add(taps[0]).at[2, :].add(taps[1])
    return grid.at[:, 0].add(taps[2]).at[:, 2].add(taps[3])


def push_payloads(full, mine, resid):
    res, rank, sides, flips, live = mine
    size = full.shape[1] - 2
    rows = jnp.stack([full[:, 0, 1:-1], full[:, -1, 1:-1], full[:, 1:-1, 0], full[:, 1:-1, -1]])
    values = jnp.stack([full[:, 0, 0], full[:, 0, -1], full[:, -1, 0], full[:, -1, -1]])
    values = values * live.astype(jnp.float32)[:, None, None]
    source = jnp.concatenate([from_rows(rows), values.reshape(4, -1)])
    hit = res[None, :] == jnp.asarray(resid)[:, None]
    count = resid.shape[0]
    edge = hit[:, None, :4] & (rank[None, None, :] == jnp.arange(2)[None, :, None])
    eye = jnp.eye(size, dtype=jnp.bool_)
    edge = edge[:, :, None, :, None] & eye[None, None, :, None, :]
    edge = jnp.concatenate(
        [edge.reshape(count, 2 * size, 4 * size), jnp.zeros((count, 2 * size, 4), jnp.bool_)], axis=2
    )
    corner = hit[:, 4:, None] & jnp.eye(4, dtype=jnp.bool_)[None]
    corner = jnp.concatenate([jnp.zeros((count, 4, 4 * size), jnp.bool_), corner], axis=2)
    route = jnp.concatenate([edge, corner], axis=1).astype(jnp.float32)
    return jnp.einsum(
        "twx,xc->twc", route, source, precision=lax.Precision.HIGHEST, preferred_element_type=jnp.float32
    )


def back_rims(received, theirs, back, like, offset):
    res, rank, sides, flips, live = theirs
    size = like.shape[1]
    n_src, width = received.shape[0], received.shape[1]
    hit = res == back[:, None]
    s = jnp.arange(4)[:, None, None, None, None]
    j = jnp.arange(size)[None, :, None, None, None]
    cols = jnp.arange(width) - offset
    q = (cols // size)[None, None, None, :, None]
    jj = (cols % size)[None, None, None, :, None]
    in_edge = ((cols >= 0) & (cols < 2 * size))[None, None, None, :, None]
    e_hit = hit[None, None, :, None, :4]
    e_side = sides[None, None, :, None, :4] == s
    e_rank = rank[None, None, :, None, :] == q
    e_cell = jnp.where(flips[None, None, :, None, :4] == 1, size - 1 - j, j) == jj
    edge = jnp.any(e_hit & e_side & e_rank & e_cell & in_edge, axis=4)
    at = corner_at(flips[:, 4:], size)
    c_slot = (cols - 2 * size)[None, None, None, :, None] == jnp.arange(4)[None, None, None, None, :]
    c_hit = hit[None, None, :, None, 4:] & (sides[None, None, :, None, 4:] == s)
    c_cell = j == at[None, None, :, None, :]
    corner = jnp.any(c_hit & c_cell & c_slot, axis=4)
    route = (edge | corner).reshape(4 * size, n_src * width).astype(jnp.float32)
    flat = jnp.dot(
        route, received.reshape(n_src * width, -1), precision=lax.Precision.HIGHEST,
        preferred_element_type=jnp.float32,
    )
    return to_rows(flat, like)


def add_rims(inner, total):
    inner = inner.at[:, 0].add(total[0]).at[:, -1].add(total[1])
    return inner.at[:, :, 0].add(total[2]).at[:, :, -1].add(total[3])


def xor_swap(value, axis, bit):
    size = lax.axis_size(axis)
    return lax.ppermute(value, axis, [(i, i ^ bit) for i in range(size)])


def halving_stages(axis):
    size = lax.axis_size(axis)
    stages = []
    bit = 1
    while bit < size:
        stages.append((axis, bit))
        bit *= 2
    return stages


def scatter_halves(buf, stages):
    for axis, bit in stages:
        half = buf.shape[0] // 2
        high = (lax.axis_index(axis) & bit) != 0
        low_part, high_part = buf[:half], buf[half:]
        send = jnp.where(high, low_part, high_part)
        keep = jnp.where(high, high_part, low_part)
        buf = keep + xor_swap(send, axis, bit)
    return buf


def gather_halves(buf, stages):
    for axis, bit in reversed(stages):
        high = (lax.axis_index(axis) & bit) != 0
        other = xor_swap(buf, axis, bit)
        buf = jnp.where(high, jnp.concatenate([other, buf]), jnp.concatenate([buf, other]))
    return buf


def all_reduce(flat, axes):
    outer, inner = axes
    for axis in axes:
        size = lax.axis_size(axis)
        if size & (size - 1):
            total = lax.psum(flat, axes)
            return total[: flat.shape[0] // 2], total[flat.shape[0] // 2 :]
    outer_stages = halving_stages(outer)
    count = lax.axis_size(inner)
    if flat.shape[0] % ((1 << len(outer_stages)) * count):
        total = lax.psum(flat, axes)
        return total[: flat.shape[0] // 2], total[flat.shape[0] // 2 :]
    buf = scatter_halves(flat, outer_stages)
    if count <= 16:
        got = lax.all_to_all(buf.reshape(count, -1), inner, 0, 0)
        part = jnp.sum(got, axis=0)
        full = lax.all_to_all(jnp.broadcast_to(part, (count,) + part.shape), inner, 0, 0)
        buf = full.reshape(-1)
    else:
        inner_stages = halving_stages(inner)
        buf = gather_halves(scatter_halves(buf, inner_stages), inner_stages)
    if not outer_stages:
        return buf[: flat.shape[0] // 2], buf[flat.shape[0] // 2 :]
    buf = gather_halves(buf, outer_stages[1:])
    axis, bit = outer_stages[0]
    high = (lax.axis_index(axis) & bit) != 0
    other = xor_swap(buf, axis, bit)
    return jnp.where(high, other, buf), jnp.where(high, buf, other)


def gelu_tanh(value):
    return jax.nn.gelu(value, approximate=True)


def shards(
    inputs,
    cotangent,
    weight_first,
    weight_second,
    slot_tile,
    neighbour_tile,
    neighbour_turns,
    corner_live,
):
    count = slot_tile.shape[0]
    devices = lax.axis_size("space")
    me = lax.axis_index("space")
    offs = residues(devices)
    slot_of_tile = (
        jnp.zeros((count,), jnp.int32).at[slot_tile].set(jnp.arange(count, dtype=jnp.int32))
    )
    tables = (slot_tile, slot_of_tile, neighbour_tile, neighbour_turns, corner_live)
    plans = make_plans(tables, devices)
    if devices <= 2 * REACH + 1:
        offs = None
        every = jnp.arange(devices, dtype=jnp.int32)
        resid = (every - me) % devices
        position = (every + me) % devices
        back = (me - every) % devices
        theirs = plans
    else:
        resid = np.array([0] + offs, np.int32)
        position = np.zeros((devices,), np.int32)
        position[resid] = np.arange(len(resid))
        back = jnp.asarray((-resid) % devices)
        theirs = tuple(p[(me + resid) % devices] for p in plans)
    mine = tuple(p[me] for p in plans)

    def trip(pull, push):
        if offs is None:
            arrived = swap_all(pull, push)
            return arrived, arrived, pull.shape[1]
        got_pull, got_push = round_trip(pull, push, offs)
        return got_pull, got_push, 0

    tile = inputs[0]
    cot_tile = cotangent[0]
    samples_all = tile.shape[0] * lax.axis_size("dp") * devices
    scale = 1.0 / math.sqrt(samples_all * tile.shape[1] * tile.shape[2])

    full_second = conv_full(cot_tile, weight_second)
    push_second = push_payloads(full_second, mine, resid)
    got_in, got_second, skip = trip(pull_payloads(tile, theirs, back), push_second)

    padded_in = pad_tile(tile, got_in, mine, position)
    hidden = conv_valid(padded_in, weight_first)
    active = gelu_tanh(hidden).astype(jnp.bfloat16)

    inner_second = full_second[:, 1:-1, 1:-1]
    grad_active = add_rims(inner_second, back_rims(got_second, theirs, back, inner_second, skip))
    _, pull_gelu = jax.vjp(gelu_tanh, hidden)
    grad_hidden = pull_gelu(grad_active)[0].astype(jnp.bfloat16)
    full_first = conv_full(grad_hidden, weight_first)
    push_first = push_payloads(full_first, mine, resid)
    pull_act = pull_payloads(active, theirs, back)
    pull_act, push_first, padded_in, grad_hidden, active = lax.optimization_barrier(
        (pull_act, push_first, padded_in, grad_hidden, active)
    )
    got_act, got_first, skip = trip(pull_act, push_first)
    local_first = weight_grad(padded_in, grad_hidden)
    bulk_second = zero_padded_weight_grad(active, cot_tile)
    got_act, got_first, local_first, bulk_second = lax.optimization_barrier(
        (got_act, got_first, local_first, bulk_second)
    )

    rows_act, corners_act = ring_parts(active, got_act, mine, position)
    local_second = bulk_second + ring_weight_grad(rows_act, corners_act, cot_tile)
    inner_first = full_first[:, 1:-1, 1:-1]
    grad_tile = add_rims(inner_first, back_rims(got_first, theirs, back, inner_first, skip))
    grad_tile = grad_tile.astype(jnp.bfloat16)

    flat = jnp.concatenate([local_first.reshape(-1), local_second.reshape(-1)]) * scale
    low, high = all_reduce(flat, ("dp", "space"))
    summed_first = low.reshape(local_first.shape)
    summed_second = high.reshape(local_second.shape)
    return (grad_tile[None], summed_first, summed_second)


def solution(mesh):
    in_specs = (
        P("space", "dp", None, None, None),
        P("space", "dp", None, None, None),
        P(),
        P(),
        P(),
        P(),
        P(),
        P(),
    )
    out_specs = (P("space", "dp", None, None, None), P(), P())
    return jax.shard_map(shards, mesh=mesh, in_specs=in_specs, out_specs=out_specs, check_vma=False)
```

```python
import math

import jax
import jax.numpy as jnp
import numpy as np
from jax import lax
from jax.sharding import PartitionSpec as P

REACH = 7

NEED_SIDE = (1, 0, 3, 2, 1, 1, 0, 0)


def side_tables():
    one = ((3, 0), (2, 0), (0, 1), (1, 1))
    side = np.zeros((4, 4), np.int32)
    flip = np.zeros((4, 4), np.int32)
    side[0] = np.arange(4)
    for r in range(1, 4):
        for s in range(4):
            s1, f1 = one[s]
            side[r, s] = side[r - 1, s1]
            flip[r, s] = flip[r - 1, s1] ^ f1
    return side, flip


def edge_rims(tile):
    return jnp.stack([tile[:, 0], tile[:, -1], tile[:, :, 0], tile[:, :, -1]])


def residues(devices):
    found = []
    for offset in range(-REACH, REACH + 1):
        res = offset % devices
        if res != 0 and res not in found:
            found.append(res)
    return found


def shift(value, by):
    length = lax.axis_size("space")
    return lax.ppermute(value, "space", [(i, (i + by) % length) for i in range(length)])


def swap_all(pull, push):
    payload = jnp.concatenate([pull.astype(jnp.float32), push], axis=1)
    return lax.all_to_all(payload, "space", 0, 0)


def round_trip(pull, push, offs):
    devices = lax.axis_size("space")
    index = {o: i + 1 for i, o in enumerate(offs)}
    rows = pull.shape[1]
    got_pull = [pull[0].astype(jnp.bfloat16)]
    got_push = [push[0]]
    for o in offs:
        back = index[(devices - o) % devices]
        payload = jnp.concatenate([pull[back].astype(jnp.float32), push[back]])
        arrived = lax.ppermute(payload, "space", [(i, (i - o) % devices) for i in range(devices)])
        got_pull.append(arrived[:rows].astype(jnp.bfloat16))
        got_push.append(arrived[rows:])
    return jnp.stack(got_pull), jnp.stack(got_push)


def make_plans(tables, devices):
    slot_tile, slot_of_tile, neighbour_tile, neighbour_turns, corner_live = tables
    slots = jnp.arange(devices, dtype=jnp.int32)
    owners = slot_of_tile[neighbour_tile[slot_tile]]
    res = (owners - slots[:, None]) % devices
    turns = neighbour_turns[slot_tile]
    side_tab, flip_tab = side_tables()
    need = np.array(NEED_SIDE, np.int32)[None, :]
    sides = jnp.asarray(side_tab)[turns, need]
    flips = jnp.asarray(flip_tab)[turns, need]
    edge = res[:, :4]
    earlier = np.tril(np.ones((4, 4), bool), -1)
    rank = jnp.sum((edge[:, :, None] == edge[:, None, :]) & earlier, axis=2)
    return res, rank, sides, flips, corner_live[slot_tile]


def flip_index(flips, size):
    cells = jnp.arange(size, dtype=jnp.int32)[None, :]
    return jnp.where(flips[:, None] == 1, size - 1 - cells, cells)


def assemble(own, top, bottom, left, right, top_left, top_right, bottom_left, bottom_right):
    top_row = jnp.concatenate([top_left[:, None], top, top_right[:, None]], axis=1)
    bottom_row = jnp.concatenate([bottom_left[:, None], bottom, bottom_right[:, None]], axis=1)
    middle = jnp.concatenate([left[:, :, None], own, right[:, :, None]], axis=2)
    return jnp.concatenate([top_row[:, None], middle, bottom_row[:, None]], axis=1)


def corner_at(flips, size):
    ends = np.array([size - 1, 0, size - 1, 0], np.int32)
    return jnp.where(flips == 1, size - 1 - ends, ends)


def to_rows(flat, like):
    size = like.shape[1]
    return flat.reshape((-1, size) + like.shape[:1] + like.shape[3:]).transpose(0, 2, 1, 3)


def from_rows(rims):
    return rims.transpose(0, 2, 1, 3).reshape(rims.shape[0] * rims.shape[2], -1)


def pull_payloads(tile, theirs, back):
    res, rank, sides, flips, live = theirs
    size = tile.shape[1]
    hit = res == back[:, None]
    q = jnp.arange(2)[None, :, None, None]
    s = jnp.arange(4)[None, None, :, None]
    edge = jnp.sum(
        hit[:, None, None, :4] & (rank[:, None, None, :] == q) & (sides[:, None, None, :4] == s), axis=3
    )
    eye = jnp.eye(size, dtype=jnp.bool_)
    edge = (edge[:, :, None, :, None] > 0) & eye[None, None, :, None, :]
    at = corner_at(flips[:, 4:], size)
    corner = (
        hit[:, 4:, None, None]
        & (sides[:, 4:, None, None] == jnp.arange(4)[None, None, :, None])
        & (jnp.arange(size)[None, None, None, :] == at[:, :, None, None])
    )
    count = res.shape[0]
    pick = jnp.concatenate([edge.reshape(count, 2 * size, 4 * size), corner.reshape(count, 4, 4 * size)], axis=1)
    rims = from_rows(edge_rims(tile))
    return jnp.einsum("twx,xc->twc", pick.astype(tile.dtype), rims, preferred_element_type=jnp.float32)


def ring_parts(tile, received, mine, position):
    res, rank, sides, flips, live = mine
    size = tile.shape[1]
    n_src, width = received.shape[0], received.shape[1]
    src = jnp.asarray(position)[res]
    cells = flip_index(flips[:4], size)
    column = rank[:, None] * size + cells
    edge = (jnp.arange(n_src)[None, None, :, None] == src[:4, None, None, None]) & (
        jnp.arange(width)[None, None, None, :] == column[:, :, None, None]
    )
    corner = (jnp.arange(n_src)[None, :, None] == src[4:, None, None]) & (
        jnp.arange(width)[None, None, :] == (2 * size + jnp.arange(4))[:, None, None]
    )
    pick = jnp.concatenate([edge.reshape(4 * size, n_src * width), corner.reshape(4, n_src * width)])
    flat = jnp.dot(
        pick.astype(received.dtype), received.reshape(n_src * width, -1), precision=lax.Precision.DEFAULT,
        preferred_element_type=jnp.float32,
    )
    flat = flat.astype(tile.dtype)
    rows = to_rows(flat[: 4 * size], tile)
    corners = flat[4 * size :].reshape((4,) + tile.shape[:1] + tile.shape[3:])
    corners = corners * live.astype(tile.dtype)[:, None, None]
    return rows, corners


def pad_tile(tile, received, mine, position):
    rows, corners = ring_parts(tile, received, mine, position)
    return assemble(tile, rows[0], rows[1], rows[2], rows[3], corners[0], corners[1], corners[2], corners[3])


def conv_valid(padded, weight):
    return lax.conv_general_dilated(
        padded,
        weight,
        (1, 1),
        "VALID",
        dimension_numbers=("NHWC", "HWIO", "NHWC"),
        preferred_element_type=jnp.float32,
    )


def conv_full(cot, weight):
    flipped = jnp.flip(weight, (0, 1)).transpose(0, 1, 3, 2)
    return lax.conv_general_dilated(
        cot,
        flipped,
        (1, 1),
        ((2, 2), (2, 2)),
        dimension_numbers=("NHWC", "HWIO", "NHWC"),
        preferred_element_type=jnp.float32,
    )


def weight_grad(padded, cot):
    return lax.conv_general_dilated(
        padded,
        cot,
        (1, 1),
        "VALID",
        dimension_numbers=("CHWN", "IHWO", "HWNC"),
        preferred_element_type=jnp.float32,
    )


def zero_padded_weight_grad(tile, cot):
    return lax.conv_general_dilated(
        tile,
        cot,
        (1, 1),
        ((1, 1), (1, 1)),
        dimension_numbers=("CHWN", "IHWO", "HWNC"),
        preferred_element_type=jnp.float32,
    )


def ring_weight_grad(rows, corners, cot):
    size = cot.shape[1]
    zero = jnp.zeros_like(corners[0])[:, None]
    lines = jnp.stack([
        jnp.concatenate([corners[0][:, None], rows[0], corners[1][:, None]], axis=1),
        jnp.concatenate([corners[2][:, None], rows[1], corners[3][:, None]], axis=1),
        jnp.concatenate([zero, rows[2], zero], axis=1),
        jnp.concatenate([zero, rows[3], zero], axis=1),
    ])
    windows = jnp.stack([lines[:, :, t : t + size] for t in range(3)], axis=1)
    edges = jnp.stack([cot[:, 0], cot[:, -1], cot[:, :, 0], cot[:, :, -1]])
    taps = jnp.einsum("ktbjc,kbjd->ktcd", windows, edges, preferred_element_type=jnp.float32)
    grid = jnp.zeros((3, 3) + taps.shape[2:], jnp.float32)
    grid = grid.at[0, :].add(taps[0]).at[2, :].add(taps[1])
    return grid.at[:, 0].add(taps[2]).at[:, 2].add(taps[3])


def push_payloads(full, mine, resid):
    res, rank, sides, flips, live = mine
    size = full.shape[1] - 2
    rows = jnp.stack([full[:, 0, 1:-1], full[:, -1, 1:-1], full[:, 1:-1, 0], full[:, 1:-1, -1]])
    values = jnp.stack([full[:, 0, 0], full[:, 0, -1], full[:, -1, 0], full[:, -1, -1]])
    values = values * live.astype(jnp.float32)[:, None, None]
    source = jnp.concatenate([from_rows(rows), values.reshape(4, -1)])
    hit = res[None, :] == jnp.asarray(resid)[:, None]
    count = resid.shape[0]
    edge = hit[:, None, :4] & (rank[None, None, :] == jnp.arange(2)[None, :, None])
    eye = jnp.eye(size, dtype=jnp.bool_)
    edge = edge[:, :, None, :, None] & eye[None, None, :, None, :]
    edge = jnp.concatenate(
        [edge.reshape(count, 2 * size, 4 * size), jnp.zeros((count, 2 * size, 4), jnp.bool_)], axis=2
    )
    corner = hit[:, 4:, None] & jnp.eye(4, dtype=jnp.bool_)[None]
    corner = jnp.concatenate([jnp.zeros((count, 4, 4 * size), jnp.bool_), corner], axis=2)
    route = jnp.concatenate([edge, corner], axis=1).astype(jnp.float32)
    return jnp.einsum(
        "twx,xc->twc", route, source, precision=lax.Precision.HIGHEST, preferred_element_type=jnp.float32
    )


def back_rims(received, theirs, back, like, offset):
    res, rank, sides, flips, live = theirs
    size = like.shape[1]
    n_src, width = received.shape[0], received.shape[1]
    hit = res == back[:, None]
    s = jnp.arange(4)[:, None, None, None, None]
    j = jnp.arange(size)[None, :, None, None, None]
    cols = jnp.arange(width) - offset
    q = (cols // size)[None, None, None, :, None]
    jj = (cols % size)[None, None, None, :, None]
    in_edge = ((cols >= 0) & (cols < 2 * size))[None, None, None, :, None]
    e_hit = hit[None, None, :, None, :4]
    e_side = sides[None, None, :, None, :4] == s
    e_rank = rank[None, None, :, None, :] == q
    e_cell = jnp.where(flips[None, None, :, None, :4] == 1, size - 1 - j, j) == jj
    edge = jnp.any(e_hit & e_side & e_rank & e_cell & in_edge, axis=4)
    at = corner_at(flips[:, 4:], size)
    c_slot = (cols - 2 * size)[None, None, None, :, None] == jnp.arange(4)[None, None, None, None, :]
    c_hit = hit[None, None, :, None, 4:] & (sides[None, None, :, None, 4:] == s)
    c_cell = j == at[None, None, :, None, :]
    corner = jnp.any(c_hit & c_cell & c_slot, axis=4)
    route = (edge | corner).reshape(4 * size, n_src * width).astype(jnp.float32)
    flat = jnp.dot(
        route, received.reshape(n_src * width, -1), precision=lax.Precision.HIGHEST,
        preferred_element_type=jnp.float32,
    )
    return to_rows(flat, like)


def add_rims(inner, total):
    inner = inner.at[:, 0].add(total[0]).at[:, -1].add(total[1])
    return inner.at[:, :, 0].add(total[2]).at[:, :, -1].add(total[3])


def xor_swap(value, axis, bit):
    size = lax.axis_size(axis)
    return lax.ppermute(value, axis, [(i, i ^ bit) for i in range(size)])


def halving_stages(axis):
    size = lax.axis_size(axis)
    stages = []
    bit = 1
    while bit < size:
        stages.append((axis, bit))
        bit *= 2
    return stages


def scatter_halves(buf, stages):
    for axis, bit in stages:
        half = buf.shape[0] // 2
        high = (lax.axis_index(axis) & bit) != 0
        low_part, high_part = buf[:half], buf[half:]
        send = jnp.where(high, low_part, high_part)
        keep = jnp.where(high, high_part, low_part)
        buf = keep + xor_swap(send, axis, bit)
    return buf


def gather_halves(buf, stages):
    for axis, bit in reversed(stages):
        high = (lax.axis_index(axis) & bit) != 0
        other = xor_swap(buf, axis, bit)
        buf = jnp.where(high, jnp.concatenate([other, buf]), jnp.concatenate([buf, other]))
    return buf


def all_reduce(flat, axes):
    outer, inner = axes
    for axis in axes:
        size = lax.axis_size(axis)
        if size & (size - 1):
            total = lax.psum(flat, axes)
            return total[: flat.shape[0] // 2], total[flat.shape[0] // 2 :]
    outer_stages = halving_stages(outer)
    count = lax.axis_size(inner)
    if flat.shape[0] % ((1 << len(outer_stages)) * count):
        total = lax.psum(flat, axes)
        return total[: flat.shape[0] // 2], total[flat.shape[0] // 2 :]
    buf = scatter_halves(flat, outer_stages)
    if count <= 16:
        got = lax.all_to_all(buf.reshape(count, -1), inner, 0, 0)
        part = jnp.sum(got, axis=0)
        full = lax.all_to_all(jnp.broadcast_to(part, (count,) + part.shape), inner, 0, 0)
        buf = full.reshape(-1)
    else:
        inner_stages = halving_stages(inner)
        buf = gather_halves(scatter_halves(buf, inner_stages), inner_stages)
    if not outer_stages:
        return buf[: flat.shape[0] // 2], buf[flat.shape[0] // 2 :]
    buf = gather_halves(buf, outer_stages[1:])
    axis, bit = outer_stages[0]
    high = (lax.axis_index(axis) & bit) != 0
    other = xor_swap(buf, axis, bit)
    return jnp.where(high, other, buf), jnp.where(high, buf, other)


def gelu_tanh(value):
    return jax.nn.gelu(value, approximate=True)


def shards(
    inputs,
    cotangent,
    weight_first,
    weight_second,
    slot_tile,
    neighbour_tile,
    neighbour_turns,
    corner_live,
):
    count = slot_tile.shape[0]
    devices = lax.axis_size("space")
    me = lax.axis_index("space")
    offs = residues(devices)
    slot_of_tile = (
        jnp.zeros((count,), jnp.int32).at[slot_tile].set(jnp.arange(count, dtype=jnp.int32))
    )
    tables = (slot_tile, slot_of_tile, neighbour_tile, neighbour_turns, corner_live)
    plans = make_plans(tables, devices)
    if devices <= 2 * REACH + 1:
        offs = None
        every = jnp.arange(devices, dtype=jnp.int32)
        resid = (every - me) % devices
        position = (every + me) % devices
        back = (me - every) % devices
        theirs = plans
    else:
        resid = np.array([0] + offs, np.int32)
        position = np.zeros((devices,), np.int32)
        position[resid] = np.arange(len(resid))
        back = jnp.asarray((-resid) % devices)
        theirs = tuple(p[(me + resid) % devices] for p in plans)
    mine = tuple(p[me] for p in plans)

    def trip(pull, push):
        if offs is None:
            arrived = swap_all(pull, push)
            return arrived, arrived, pull.shape[1]
        got_pull, got_push = round_trip(pull, push, offs)
        return got_pull, got_push, 0

    tile = inputs[0]
    cot_tile = cotangent[0]
    samples_all = tile.shape[0] * lax.axis_size("dp") * devices
    scale = 1.0 / math.sqrt(samples_all * tile.shape[1] * tile.shape[2])

    full_second = conv_full(cot_tile, weight_second)
    push_second = push_payloads(full_second, mine, resid)
    got_in, got_second, skip = trip(pull_payloads(tile, theirs, back), push_second)

    padded_in = pad_tile(tile, got_in, mine, position)
    hidden = conv_valid(padded_in, weight_first)
    active = gelu_tanh(hidden).astype(jnp.bfloat16)

    inner_second = full_second[:, 1:-1, 1:-1]
    grad_active = add_rims(inner_second, back_rims(got_second, theirs, back, inner_second, skip))
    _, pull_gelu = jax.vjp(gelu_tanh, hidden)
    grad_hidden = pull_gelu(grad_active)[0].astype(jnp.bfloat16)
    full_first = conv_full(grad_hidden, weight_first)
    push_first = push_payloads(full_first, mine, resid)
    pull_act = pull_payloads(active, theirs, back)
    pull_act, push_first, padded_in, grad_hidden, active = lax.optimization_barrier(
        (pull_act, push_first, padded_in, grad_hidden, active)
    )
    got_act, got_first, skip = trip(pull_act, push_first)
    local_first = weight_grad(padded_in, grad_hidden)
    bulk_second = zero_padded_weight_grad(active, cot_tile)
    got_act, got_first, local_first, bulk_second = lax.optimization_barrier(
        (got_act, got_first, local_first, bulk_second)
    )

    rows_act, corners_act = ring_parts(active, got_act, mine, position)
    local_second = bulk_second + ring_weight_grad(rows_act, corners_act, cot_tile)
    inner_first = full_first[:, 1:-1, 1:-1]
    grad_tile = add_rims(inner_first, back_rims(got_first, theirs, back, inner_first, skip))
    grad_tile = grad_tile.astype(jnp.bfloat16)

    flat = jnp.concatenate([local_first.reshape(-1), local_second.reshape(-1)]) * scale
    low, high = all_reduce(flat, ("dp", "space"))
    summed_first = low.reshape(local_first.shape)
    summed_second = high.reshape(local_second.shape)
    return (grad_tile[None], summed_first, summed_second)


def solution(mesh):
    in_specs = (
        P("space", "dp", None, None, None),
        P("space", "dp", None, None, None),
        P(),
        P(),
        P(),
        P(),
        P(),
        P(),
    )
    out_specs = (P("space", "dp", None, None, None), P(), P())
    return jax.shard_map(shards, mesh=mesh, in_specs=in_specs, out_specs=out_specs, check_vma=False)
```
